128 devices in a mesh: box: 32 (over z, x_hi, y), dir: 4 (over x_lo, core).
Axes of the slice: x: 4 (x_hi: 2, x_lo: 2; x = x_hi * 2 + x_lo), y: 4, z: 4, core: 2. Of those that a mesh axis runs over, the one named last changes fastest.
Arguments:
- pattern: float32 [512, 8, 16384], P('dir', None, 'box'), may hold values from -6 to 6
- child_coef: float32 [2, 4, 512], P(None, None, 'dir'), may hold values from -3 to 3
- child_mask: int32 [4, 16384], P(None, 'box'), may hold values 0 or 1
- interp_index: int32 [16, 2048], replicated, may hold values from 0 to 511, as said below
- interp_weight: float32 [16, 2048], replicated, may hold values from -1.25 to 1.25
- phase_angle: float32 [8, 2048], replicated, may hold values from -3.140625 to 3.140625
- parent_coef: float32 [2, 32, 2048], replicated, may hold values from -3 to 3
- parent_mask: int32 [32, 2048], replicated, may hold values 0 or 1
Outputs:
- local_field: float32 [512, 8, 16384], P('dir', None, 'box')
The draws below stay inside these ranges and needn't reach their ends.
Inputs may be any that keep to these rules, and one draw needn't show every extreme that they name: `interp_index`: child directions form a grid of 16 polar by 32 azimuthal angles, numbered as (azimuth % 4) * 128 + polar * 8 + azimuth // 4; each parent direction reads the 16 child directions of a 4 by 4 block of neighbouring angles, the azimuth wrapping round.
All inputs are finite; a program needn't handle non-finite values. No bound on the sum of `child_mask` on one device may be relied on, other than what follows from the above.
Results may differ from the reference program's by a relative error of at most 0.000053.
Values sent between devices are 32-bit elements; how exact they have to be, the bound alone decides.
No kernel may reach another device: no remote copies, remote signals or barrier semaphores. Data moves between devices by JAX's collectives and lax.ppermute only.
A program may use at most 192 MiB of HBM per device.

```python
import jax
import jax.numpy as jnp
from jax import lax

CHILD_DIRS = 512
PARENT_DIRS = 2048
CHILD_THETA = 16
RHS = 4
GROUP = 8
POINTS = 16
CHILD_REACH = 2
PARENT_REACH = 16
BOX_DEV = 512
BOXES = 16384
PAR_DEV = 64
PARENTS = 2048
N_BOX = 32


def draw_interp_index(key, part):
    child_theta = CHILD_THETA
    child_phi = 2 * CHILD_THETA
    parent_phi = 2 * child_phi
    parent = jnp.arange(PARENT_DIRS, dtype=jnp.int32)
    theta_parent = parent // parent_phi
    phi_parent = parent % parent_phi
    key_theta, key_phi = jax.random.split(jax.random.fold_in(key, 7))
    jitter_theta = jax.random.randint(key_theta, (PARENT_DIRS,), -1, 2, dtype=jnp.int32)
    jitter_phi = jax.random.randint(key_phi, (PARENT_DIRS,), -1, 2, dtype=jnp.int32)
    theta_start = jnp.clip(theta_parent // 2 - 1 + jitter_theta, 0, child_theta - 4)
    phi_start = phi_parent // 2 - 1 + jitter_phi + child_phi
    point = jnp.arange(POINTS, dtype=jnp.int32)
    theta_child = theta_start[None, :] + (point // 4)[:, None]
    phi_child = (phi_start[None, :] + (point % 4)[:, None]) % child_phi
    index = phi_child % 4 * (CHILD_DIRS // 4) + theta_child * (child_phi // 4) + phi_child // 4
    return index.astype(jnp.int32)


def touch_ends(entries, rng, low, top_value):
    spot = [jax.random.randint(jax.random.fold_in(rng, axis), (), 0, length) for axis, length in enumerate(entries.shape)]
    longest = entries.shape.index(max(entries.shape))
    neighbour = spot[:longest] + [(spot[longest] + 1) % entries.shape[longest]] + spot[longest + 1:]
    return entries.at[tuple(spot)].set(low).at[tuple(neighbour)].set(top_value)


def block_levels(stream_key, extent, cuts, smallest, high):
    level, own = 1.0, jax.random.fold_in(stream_key, 6)
    for dim, blocks in cuts:
        heights = jnp.exp(jax.random.uniform(jax.random.fold_in(own, dim), (blocks,), jnp.float32, smallest / len(cuts), high / len(cuts)))
        level = level * jnp.repeat(heights, extent[dim] // blocks).reshape([-1 if axis == dim else 1 for axis in range(len(extent))])
    return level


def centred(rng, dims, scale, limit, cuts=(), kind=jnp.bfloat16):
    drawn = scale * jax.random.normal(rng, dims, jnp.float32)
    if cuts:
        drawn = drawn * block_levels(rng, dims, cuts, -0.22, 0.18)
    return jnp.clip(drawn, -limit, limit).astype(kind)


def setup_inputs(seed: int = 0) -> dict:
    seeds = jax.random.split(jax.random.key(seed), 9)
    pattern = centred(seeds[0], (CHILD_DIRS, 2 * RHS, BOXES), 1.0, 6.0, ((0, 4), (2, 32)), jnp.float32)
    child_coef = centred(seeds[1], (2, 2 * CHILD_REACH, CHILD_DIRS), 0.5, 3.0, ((2, 4),), jnp.float32)
    child_mask = touch_ends((jax.random.randint(seeds[2], (2 * CHILD_REACH, BOXES), 0, 4) < 3).astype(jnp.int32), jax.random.fold_in(seeds[2], 1), 0, 1)
    interp_index = draw_interp_index(jax.random.fold_in(seeds[8], 71), 0)
    interp_weight = centred(seeds[4], (POINTS, PARENT_DIRS), 0.09, 1.25, (), jnp.float32)
    phase_angle = jnp.clip(jax.random.uniform(seeds[5], (GROUP, PARENT_DIRS), jnp.float32, -3.140625, 3.140625), -3.140625, 3.140625)
    parent_coef = centred(seeds[6], (2, 2 * PARENT_REACH, PARENT_DIRS), 0.2, 3.0, (), jnp.float32)
    parent_mask = touch_ends((jax.random.randint(seeds[7], (2 * PARENT_REACH, PARENTS), 0, 4) < 3).astype(jnp.int32), jax.random.fold_in(seeds[7], 1), 0, 1)
    return {"pattern": pattern, "child_coef": child_coef, "child_mask": child_mask, "interp_index": interp_index, "interp_weight": interp_weight, "phase_angle": phase_angle, "parent_coef": parent_coef, "parent_mask": parent_mask}


def interp_matrix(index, weight, first_row, row_count):
    rows = first_row + lax.iota(jnp.int32, row_count)
    matrix = jnp.zeros((row_count, index.shape[1]), jnp.float32)
    for point in range(index.shape[0]):
        matrix = matrix + jnp.where(rows[:, None] == index[point][None, :], weight[point][None, :], jnp.float32(0.0))
    return matrix


def translate_padded(padded, coef_real, coef_imag, mask, reach):
    count = padded.shape[2] - 2 * reach
    half = padded.shape[1] // 2
    offsets = list(range(-reach, 0)) + list(range(1, reach + 1))
    summed = jnp.zeros((padded.shape[0], padded.shape[1], count), jnp.float32)
    for position, offset in enumerate(offsets):
        source = padded[:, :, reach + offset:reach + offset + count]
        real_part = source[:, :half]
        imag_part = source[:, half:]
        scale_real = coef_real[position][:, None, None]
        scale_imag = coef_imag[position][:, None, None]
        weight = mask[position].astype(jnp.float32)[None, None, :]
        turned = jnp.concatenate([scale_real * real_part - scale_imag * imag_part, scale_real * imag_part + scale_imag * real_part], axis=1)
        summed = summed + weight * turned
    return summed


def aggregate(raw, cosine, sine_table):
    direction_count, component_count, box_count = raw.shape
    half = component_count // 2
    group = cosine.shape[1]
    cos_box = jnp.tile(cosine, (1, box_count // group))[:, None, :]
    sin_box = jnp.tile(sine_table, (1, box_count // group))[:, None, :]
    real_part = raw[:, :half]
    imag_part = raw[:, half:]
    turned = jnp.concatenate([cos_box * real_part - sin_box * imag_part, cos_box * imag_part + sin_box * real_part], axis=1)
    return turned.reshape(direction_count, component_count, box_count // group, group).sum(axis=3)


def disaggregate(local, cosine, sine_table):
    group = cosine.shape[1]
    expanded = jnp.repeat(local, group, axis=2)
    box_count = expanded.shape[2]
    half = expanded.shape[1] // 2
    cos_box = jnp.tile(cosine, (1, box_count // group))[:, None, :]
    sin_box = jnp.tile(sine_table, (1, box_count // group))[:, None, :]
    real_part = expanded[:, :half]
    imag_part = expanded[:, half:]
    return jnp.concatenate([cos_box * real_part + sin_box * imag_part, cos_box * imag_part - sin_box * real_part], axis=1)


def reference(pattern, child_coef, child_mask, interp_index, interp_weight, phase_angle, parent_coef, parent_mask):
    highest = lax.Precision.HIGHEST
    matrix = interp_matrix(interp_index, interp_weight, 0, CHILD_DIRS)
    cosine = jnp.cos(phase_angle).T
    sine_table = jnp.sin(phase_angle).T
    blocks = jnp.arange(N_BOX, dtype=jnp.int32)

    def upward(block):
        piece = lax.dynamic_slice_in_dim(pattern, block * BOX_DEV, BOX_DEV, 2)
        raw = jnp.einsum("qp,qcb->pcb", matrix, piece, precision=highest)
        return aggregate(raw, cosine, sine_table)

    parent_blocks = lax.map(upward, blocks)
    parent_field = jnp.transpose(parent_blocks, (1, 2, 0, 3)).reshape(PARENT_DIRS, 2 * RHS, PARENTS)
    parent_padded = jnp.pad(parent_field, ((0, 0), (0, 0), (PARENT_REACH, PARENT_REACH)))
    parent_local = translate_padded(parent_padded, parent_coef[0], parent_coef[1], parent_mask, PARENT_REACH)
    child_padded = jnp.pad(pattern, ((0, 0), (0, 0), (CHILD_REACH, CHILD_REACH)))
    child_local = translate_padded(child_padded, child_coef[0], child_coef[1], child_mask, CHILD_REACH)

    def downward(block):
        local_piece = lax.dynamic_slice_in_dim(parent_local, block * PAR_DEV, PAR_DEV, 2)
        spread = disaggregate(local_piece, cosine, sine_table)
        return jnp.einsum("qp,pcb->qcb", matrix, spread, precision=highest)

    far_blocks = lax.map(downward, blocks)
    far_part = jnp.transpose(far_blocks, (1, 2, 0, 3)).reshape(CHILD_DIRS, 2 * RHS, BOXES)
    return child_local + far_part
```

```python
import functools

import jax
import jax.numpy as jnp
from jax import lax
from jax.experimental import pallas as pl
from jax.experimental.pallas import tpu as pltpu
from jax.sharding import PartitionSpec as P

HIGHEST = lax.Precision.HIGHEST


def with_halo(block, sides, width):
    for axis, dim in sides:
        count = lax.axis_size(axis)
        forward = [(i, i + 1) for i in range(count - 1)]
        backward = [(target, source) for source, target in forward]
        low = lax.ppermute(
            lax.slice_in_dim(block, block.shape[dim] - width, None, axis=dim), axis, forward
        )
        high = lax.ppermute(lax.slice_in_dim(block, 0, width, axis=dim), axis, backward)
        block = jnp.concatenate([low, block, high], axis=dim)
    return block


def interp_matrix(index, weight, first_row, row_count):
    rows = first_row + lax.iota(jnp.int32, row_count)
    matrix = jnp.zeros((row_count, index.shape[1]), jnp.float32)
    for point in range(index.shape[0]):
        matrix = matrix + jnp.where(
            rows[:, None] == index[point][None, :], weight[point][None, :], jnp.float32(0.0)
        )
    return matrix


def translate_padded(padded, coef_real, coef_imag, mask, reach):
    count = padded.shape[2] - 2 * reach
    half = padded.shape[1] // 2
    offsets = list(range(-reach, 0)) + list(range(1, reach + 1))
    summed = jnp.zeros((padded.shape[0], padded.shape[1], count), jnp.float32)
    for position, offset in enumerate(offsets):
        source = padded[:, :, reach + offset : reach + offset + count]
        real_part = source[:, :half]
        imag_part = source[:, half:]
        scale_real = coef_real[position][:, None, None]
        scale_imag = coef_imag[position][:, None, None]
        weight = mask[position].astype(jnp.float32)[None, None, :]
        turned = jnp.concatenate(
            [
                scale_real * real_part - scale_imag * imag_part,
                scale_real * imag_part + scale_imag * real_part,
            ],
            axis=1,
        )
        summed = summed + weight * turned
    return summed


def upward_kernel(xt_ref, m_ref, cos_ref, sin_ref, out_ref):
    groups = xt_ref.shape[0]
    comps, slots, width = out_ref.shape[1:]
    half = comps // 2
    m = m_ref[...]
    acc_re = jnp.zeros((half, slots, width), jnp.float32)
    acc_im = jnp.zeros((half, slots, width), jnp.float32)
    for g in range(groups):
        r = jnp.dot(xt_ref[g], m, precision=HIGHEST, preferred_element_type=jnp.float32)
        r = r.reshape(comps, slots, width)
        c = cos_ref[pl.ds(g, 1), :].reshape(1, 1, width)
        s = sin_ref[pl.ds(g, 1), :].reshape(1, 1, width)
        re = r[:half]
        im = r[half:]
        acc_re = acc_re + (c * re - s * im)
        acc_im = acc_im + (c * im + s * re)
    out_ref[0, :half] = acc_re
    out_ref[0, half:] = acc_im


def upward(xt, m, cos, sin, parts):
    groups, rows, q = xt.shape
    total = m.shape[1]
    width = total // parts
    comps = 8
    slots = rows // comps
    return pl.pallas_call(
        upward_kernel,
        grid=(parts,),
        in_specs=[
            pl.BlockSpec((groups, rows, q), lambda j: (0, 0, 0)),
            pl.BlockSpec((q, width), lambda j: (0, j)),
            pl.BlockSpec((groups, width), lambda j: (0, j)),
            pl.BlockSpec((groups, width), lambda j: (0, j)),
        ],
        out_specs=pl.BlockSpec((1, comps, slots, width), lambda j: (j, 0, 0, 0)),
        out_shape=jax.ShapeDtypeStruct((parts, comps, slots, width), jnp.float32),
    )(xt, m, cos, sin)


def downward_kernel(pl_ref, m_ref, cos_ref, sin_ref, out_ref):
    g = pl.program_id(0)
    parts, comps, slots, width = pl_ref.shape
    half = comps // 2
    q = m_ref.shape[0]
    acc = jnp.zeros((q, comps * slots), jnp.float32)
    for d in range(parts):
        x = pl_ref[d]
        c = cos_ref[pl.ds(g, 1), pl.ds(d * width, width)].reshape(1, 1, width)
        s = sin_ref[pl.ds(g, 1), pl.ds(d * width, width)].reshape(1, 1, width)
        re = x[:half]
        im = x[half:]
        spread = jnp.concatenate([c * re + s * im, c * im - s * re], axis=0)
        spread = spread.reshape(comps * slots, width)
        acc = acc + lax.dot_general(
            m_ref[:, pl.ds(d * width, width)],
            spread,
            (((1,), (1,)), ((), ())),
            precision=HIGHEST,
            preferred_element_type=jnp.float32,
        )
    out_ref[0] = acc


def downward(parent_local, m, cos, sin):
    parts, comps, slots, width = parent_local.shape
    groups = cos.shape[0]
    q = m.shape[0]
    return pl.pallas_call(
        downward_kernel,
        grid=(groups,),
        in_specs=[
            pl.BlockSpec((parts, comps, slots, width), lambda g: (0, 0, 0, 0)),
            pl.BlockSpec((q, parts * width), lambda g: (0, 0)),
            pl.BlockSpec((groups, parts * width), lambda g: (0, 0)),
            pl.BlockSpec((groups, parts * width), lambda g: (0, 0)),
        ],
        out_specs=pl.BlockSpec((1, q, comps * slots), lambda g: (g, 0, 0)),
        out_shape=jax.ShapeDtypeStruct((groups, q, comps * slots), jnp.float32),
    )(parent_local, m, cos, sin)


def parent_translate(padded, coef_real, coef_imag, mask, reach):
    comps = padded.shape[0]
    half = comps // 2
    count = padded.shape[1] - 2 * reach
    offsets = list(range(-reach, 0)) + list(range(1, reach + 1))
    re_sum = jnp.zeros((half, count, padded.shape[2]), jnp.float32)
    im_sum = jnp.zeros((half, count, padded.shape[2]), jnp.float32)
    for position, offset in enumerate(offsets):
        source = padded[:, reach + offset : reach + offset + count]
        re = source[:half]
        im = source[half:]
        cr = coef_real[position][None, None, :]
        ci = coef_imag[position][None, None, :]
        weight = mask[position].astype(jnp.float32)[None, :, None]
        re_sum = re_sum + weight * (cr * re - ci * im)
        im_sum = im_sum + weight * (cr * im + ci * re)
    return jnp.concatenate([re_sum, im_sum], axis=0)


def body(
    pattern,
    child_coef,
    child_mask,
    interp_index,
    interp_weight,
    phase_angle,
    parent_coef,
    parent_mask,
):
    child_dev, comps, box_dev = pattern.shape
    dir_size = lax.axis_size("dir")
    parent_dirs = interp_index.shape[1]
    parent_dev = parent_dirs // dir_size
    groups = phase_angle.shape[0]
    slots = box_dev // groups
    dir_rank = lax.axis_index("dir")
    box_rank = lax.axis_index("box")
    child_first = dir_rank * child_dev
    parent_first = dir_rank * parent_dev
    cosine = jnp.cos(phase_angle)
    sine = jnp.sin(phase_angle)
    rows = interp_matrix(interp_index, interp_weight, child_first, child_dev)

    child_reach = child_coef.shape[1] // 2
    child_padded = with_halo(pattern, (("box", 2),), child_reach)
    child_local = translate_padded(
        child_padded, child_coef[0], child_coef[1], child_mask, child_reach
    )

    xt = pattern.reshape(child_dev, comps, slots, groups).transpose(3, 1, 2, 0)
    xt = xt.reshape(groups, comps * slots, child_dev)
    field = upward(xt, rows, cosine, sine, dir_size)
    field = lax.psum_scatter(field, "dir", scatter_dimension=0, tiled=True)[0]

    parent_reach = parent_coef.shape[1] // 2
    padded = with_halo(field, (("box", 1),), parent_reach)
    own_real = lax.dynamic_slice_in_dim(parent_coef[0], parent_first, parent_dev, 1)
    own_imag = lax.dynamic_slice_in_dim(parent_coef[1], parent_first, parent_dev, 1)
    own_mask = lax.dynamic_slice_in_dim(parent_mask, box_rank * slots, slots, 1)
    local = parent_translate(padded, own_real, own_imag, own_mask, parent_reach)
    local_all = lax.all_gather(local, "dir", axis=0, tiled=False)

    far = downward(local_all, rows, cosine, sine)
    far = far.reshape(groups, child_dev, comps, slots).transpose(1, 2, 3, 0)
    far = far.reshape(child_dev, comps, box_dev)
    return child_local + far


def solution(mesh):
    placed = (P("dir", None, "box"), P(None, None, "dir"), P(None, "box"), P(), P(), P(), P(), P())
    return jax.shard_map(
        body, mesh=mesh, in_specs=placed, out_specs=P("dir", None, "box"), check_vma=False
    )
```

```python
import jax
import jax.numpy as jnp
from jax import lax
from jax.experimental import pallas as pl
from jax.experimental.pallas import tpu as pltpu
from jax.sharding import PartitionSpec as P

HIGHEST = lax.Precision.HIGHEST
CHUNKS = 2


def with_halo(block, sides, width):
    for axis, dim in sides:
        count = lax.axis_size(axis)
        forward = [(i, i + 1) for i in range(count - 1)]
        backward = [(target, source) for source, target in forward]
        low = lax.ppermute(
            lax.slice_in_dim(block, block.shape[dim] - width, None, axis=dim), axis, forward
        )
        high = lax.ppermute(lax.slice_in_dim(block, 0, width, axis=dim), axis, backward)
        block = jnp.concatenate([low, block, high], axis=dim)
    return block


def interp_matrix(index, weight, first_row, row_count):
    rows = first_row + lax.iota(jnp.int32, row_count)
    matrix = jnp.zeros((row_count, index.shape[1]), jnp.float32)
    for point in range(index.shape[0]):
        matrix = matrix + jnp.where(
            rows[:, None] == index[point][None, :], weight[point][None, :], jnp.float32(0.0)
        )
    return matrix


def translate_padded(padded, coef_real, coef_imag, mask, reach):
    count = padded.shape[2] - 2 * reach
    half = padded.shape[1] // 2
    offsets = list(range(-reach, 0)) + list(range(1, reach + 1))
    summed = jnp.zeros((padded.shape[0], padded.shape[1], count), jnp.float32)
    for position, offset in enumerate(offsets):
        source = padded[:, :, reach + offset : reach + offset + count]
        real_part = source[:, :half]
        imag_part = source[:, half:]
        scale_real = coef_real[position][:, None, None]
        scale_imag = coef_imag[position][:, None, None]
        weight = mask[position].astype(jnp.float32)[None, None, :]
        turned = jnp.concatenate(
            [
                scale_real * real_part - scale_imag * imag_part,
                scale_real * imag_part + scale_imag * real_part,
            ],
            axis=1,
        )
        summed = summed + weight * turned
    return summed


def upward_kernel(xt_ref, m_ref, cos_ref, sin_ref, out_ref):
    groups = xt_ref.shape[0]
    comps, slots, width = out_ref.shape[1:]
    half = comps // 2
    m = m_ref[...]
    acc_re = jnp.zeros((half, slots, width), jnp.float32)
    acc_im = jnp.zeros((half, slots, width), jnp.float32)
    for g in range(groups):
        r = jnp.dot(xt_ref[g], m, precision=HIGHEST, preferred_element_type=jnp.float32)
        r = r.reshape(comps, slots, width)
        c = cos_ref[pl.ds(g, 1), :].reshape(1, 1, width)
        s = sin_ref[pl.ds(g, 1), :].reshape(1, 1, width)
        re = r[:half]
        im = r[half:]
        acc_re = acc_re + (c * re - s * im)
        acc_im = acc_im + (c * im + s * re)
    out_ref[0, :half] = acc_re
    out_ref[0, half:] = acc_im


def upward(xt, m, cos, sin, parts, comps):
    groups, rows, q = xt.shape
    total = m.shape[1]
    width = total // parts
    slots = rows // comps
    return pl.pallas_call(
        upward_kernel,
        grid=(parts,),
        in_specs=[
            pl.BlockSpec((groups, rows, q), lambda j: (0, 0, 0)),
            pl.BlockSpec((q, width), lambda j: (0, j)),
            pl.BlockSpec((groups, width), lambda j: (0, j)),
            pl.BlockSpec((groups, width), lambda j: (0, j)),
        ],
        out_specs=pl.BlockSpec((1, comps, slots, width), lambda j: (j, 0, 0, 0)),
        out_shape=jax.ShapeDtypeStruct((parts, comps, slots, width), jnp.float32),
    )(xt, m, cos, sin)


def downward_kernel(pl_ref, m_ref, cos_ref, sin_ref, out_ref):
    g = pl.program_id(0)
    parts, comps, slots, width = pl_ref.shape
    half = comps // 2
    q = m_ref.shape[0]
    acc = jnp.zeros((q, comps * slots), jnp.float32)
    for d in range(parts):
        x = pl_ref[d]
        c = cos_ref[pl.ds(g, 1), pl.ds(d * width, width)].reshape(1, 1, width)
        s = sin_ref[pl.ds(g, 1), pl.ds(d * width, width)].reshape(1, 1, width)
        re = x[:half]
        im = x[half:]
        spread = jnp.concatenate([c * re + s * im, c * im - s * re], axis=0)
        spread = spread.reshape(comps * slots, width)
        acc = acc + lax.dot_general(
            m_ref[:, pl.ds(d * width, width)],
            spread,
            (((1,), (1,)), ((), ())),
            precision=HIGHEST,
            preferred_element_type=jnp.float32,
        )
    out_ref[0] = acc


def downward(parent_local, m, cos, sin):
    parts, comps, slots, width = parent_local.shape
    groups = cos.shape[0]
    q = m.shape[0]
    return pl.pallas_call(
        downward_kernel,
        grid=(groups,),
        in_specs=[
            pl.BlockSpec((parts, comps, slots, width), lambda g: (0, 0, 0, 0)),
            pl.BlockSpec((q, parts * width), lambda g: (0, 0)),
            pl.BlockSpec((groups, parts * width), lambda g: (0, 0)),
            pl.BlockSpec((groups, parts * width), lambda g: (0, 0)),
        ],
        out_specs=pl.BlockSpec((1, q, comps * slots), lambda g: (g, 0, 0)),
        out_shape=jax.ShapeDtypeStruct((groups, q, comps * slots), jnp.float32),
    )(parent_local, m, cos, sin)


def parent_translate(padded, coef_real, coef_imag, mask, reach):
    comps = padded.shape[0]
    half = comps // 2
    count = padded.shape[1] - 2 * reach
    offsets = list(range(-reach, 0)) + list(range(1, reach + 1))
    re_sum = jnp.zeros((half, count, padded.shape[2]), jnp.float32)
    im_sum = jnp.zeros((half, count, padded.shape[2]), jnp.float32)
    for position, offset in enumerate(offsets):
        source = padded[:, reach + offset : reach + offset + count]
        re = source[:half]
        im = source[half:]
        cr = coef_real[position][None, None, :]
        ci = coef_imag[position][None, None, :]
        weight = mask[position].astype(jnp.float32)[None, :, None]
        re_sum = re_sum + weight * (cr * re - ci * im)
        im_sum = im_sum + weight * (cr * im + ci * re)
    return jnp.concatenate([re_sum, im_sum], axis=0)


def body(
    pattern,
    child_coef,
    child_mask,
    interp_index,
    interp_weight,
    phase_angle,
    parent_coef,
    parent_mask,
):
    child_dev, comps, box_dev = pattern.shape
    dir_size = lax.axis_size("dir")
    parent_dirs = interp_index.shape[1]
    parent_dev = parent_dirs // dir_size
    groups = phase_angle.shape[0]
    slots = box_dev // groups
    dir_rank = lax.axis_index("dir")
    box_rank = lax.axis_index("box")
    child_first = dir_rank * child_dev
    parent_first = dir_rank * parent_dev
    cosine = jnp.cos(phase_angle)
    sine = jnp.sin(phase_angle)
    rows = interp_matrix(interp_index, interp_weight, child_first, child_dev)

    child_reach = child_coef.shape[1] // 2
    child_padded = with_halo(pattern, (("box", 2),), child_reach)
    child_local = translate_padded(
        child_padded, child_coef[0], child_coef[1], child_mask, child_reach
    )

    parent_reach = parent_coef.shape[1] // 2
    own_real = lax.dynamic_slice_in_dim(parent_coef[0], parent_first, parent_dev, 1)
    own_imag = lax.dynamic_slice_in_dim(parent_coef[1], parent_first, parent_dev, 1)
    own_mask = lax.dynamic_slice_in_dim(parent_mask, box_rank * slots, slots, 1)
    rhs = comps // 2
    step = rhs // CHUNKS
    fars = []
    for chunk in range(CHUNKS):
        part = pattern.reshape(child_dev, 2, rhs, box_dev)[:, :, chunk * step : (chunk + 1) * step]
        xt = part.reshape(child_dev, 2 * step, slots, groups).transpose(3, 1, 2, 0)
        xt = xt.reshape(groups, 2 * step * slots, child_dev)
        field = upward(xt, rows, cosine, sine, dir_size, 2 * step)
        field = lax.psum_scatter(field, "dir", scatter_dimension=0, tiled=True)[0]
        padded = with_halo(field, (("box", 1),), parent_reach)
        local = parent_translate(padded, own_real, own_imag, own_mask, parent_reach)
        local_all = lax.all_gather(local, "dir", axis=0, tiled=False)
        far = downward(local_all, rows, cosine, sine)
        fars.append(far.reshape(groups, child_dev, 2, step, slots))
    far = jnp.concatenate(fars, axis=3).transpose(1, 2, 3, 4, 0)
    far = far.reshape(child_dev, comps, box_dev)
    return child_local + far


def solution(mesh):
    placed = (P("dir", None, "box"), P(None, None, "dir"), P(None, "box"), P(), P(), P(), P(), P())
    return jax.shard_map(
        body, mesh=mesh, in_specs=placed, out_specs=P("dir", None, "box"), check_vma=False
    )
```

```python
import jax
import jax.numpy as jnp
from jax import lax
from jax.experimental import pallas as pl
from jax.experimental.pallas import tpu as pltpu
from jax.sharding import PartitionSpec as P

HIGHEST = lax.Precision.HIGHEST
CHUNKS = 2


def with_halo(block, sides, width):
    for axis, dim in sides:
        count = lax.axis_size(axis)
        forward = [(i, i + 1) for i in range(count - 1)]
        backward = [(target, source) for source, target in forward]
        low = lax.ppermute(
            lax.slice_in_dim(block, block.shape[dim] - width, None, axis=dim), axis, forward
        )
        high = lax.ppermute(lax.slice_in_dim(block, 0, width, axis=dim), axis, backward)
        block = jnp.concatenate([low, block, high], axis=dim)
    return block


def dir_reduce_scatter(field):
    rank = lax.axis_index("dir")
    core = rank % 2
    row = rank // 2
    pairs = field.reshape((2, 2) + field.shape[1:])
    keep = lax.dynamic_index_in_dim(pairs, core, 1, keepdims=False)
    send = lax.dynamic_index_in_dim(pairs, 1 - core, 1, keepdims=False)
    acc = keep + lax.ppermute(send, "dir", [(0, 1), (1, 0), (2, 3), (3, 2)])
    keep = lax.dynamic_index_in_dim(acc, row, 0, keepdims=False)
    send = lax.dynamic_index_in_dim(acc, 1 - row, 0, keepdims=False)
    return keep + lax.ppermute(send, "dir", [(0, 2), (2, 0), (1, 3), (3, 1)])


def dir_all_gather(local):
    rank = lax.axis_index("dir")
    core = rank % 2
    row = rank // 2
    other = lax.ppermute(local, "dir", [(0, 2), (2, 0), (1, 3), (3, 1)])
    first = row == 0
    pair = jnp.stack([jnp.where(first, local, other), jnp.where(first, other, local)], axis=0)
    mate = lax.ppermute(pair, "dir", [(0, 1), (1, 0), (2, 3), (3, 2)])
    low = core == 0
    quad = jnp.stack([jnp.where(low, pair, mate), jnp.where(low, mate, pair)], axis=1)
    return quad.reshape((4,) + local.shape)


def interp_matrix(index, weight, first_row, row_count):
    rows = first_row + lax.iota(jnp.int32, row_count)
    matrix = jnp.zeros((row_count, index.shape[1]), jnp.float32)
    for point in range(index.shape[0]):
        matrix = matrix + jnp.where(
            rows[:, None] == index[point][None, :], weight[point][None, :], jnp.float32(0.0)
        )
    return matrix


def translate_padded(padded, coef_real, coef_imag, mask, reach):
    count = padded.shape[2] - 2 * reach
    half = padded.shape[1] // 2
    offsets = list(range(-reach, 0)) + list(range(1, reach + 1))
    summed = jnp.zeros((padded.shape[0], padded.shape[1], count), jnp.float32)
    for position, offset in enumerate(offsets):
        source = padded[:, :, reach + offset : reach + offset + count]
        real_part = source[:, :half]
        imag_part = source[:, half:]
        scale_real = coef_real[position][:, None, None]
        scale_imag = coef_imag[position][:, None, None]
        weight = mask[position].astype(jnp.float32)[None, None, :]
        turned = jnp.concatenate(
            [
                scale_real * real_part - scale_imag * imag_part,
                scale_real * imag_part + scale_imag * real_part,
            ],
            axis=1,
        )
        summed = summed + weight * turned
    return summed


def upward_kernel(xt_ref, m_ref, cos_ref, sin_ref, out_ref):
    groups = xt_ref.shape[0]
    comps, slots, width = out_ref.shape[1:]
    half = comps // 2
    m = m_ref[...]
    acc_re = jnp.zeros((half, slots, width), jnp.float32)
    acc_im = jnp.zeros((half, slots, width), jnp.float32)
    for g in range(groups):
        r = jnp.dot(xt_ref[g], m, precision=HIGHEST, preferred_element_type=jnp.float32)
        r = r.reshape(comps, slots, width)
        c = cos_ref[pl.ds(g, 1), :].reshape(1, 1, width)
        s = sin_ref[pl.ds(g, 1), :].reshape(1, 1, width)
        re = r[:half]
        im = r[half:]
        acc_re = acc_re + (c * re - s * im)
        acc_im = acc_im + (c * im + s * re)
    out_ref[0, :half] = acc_re
    out_ref[0, half:] = acc_im


def upward(xt, m, cos, sin, parts, comps):
    groups, rows, q = xt.shape
    total = m.shape[1]
    width = total // parts
    slots = rows // comps
    return pl.pallas_call(
        upward_kernel,
        grid=(parts,),
        in_specs=[
            pl.BlockSpec((groups, rows, q), lambda j: (0, 0, 0)),
            pl.BlockSpec((q, width), lambda j: (0, j)),
            pl.BlockSpec((groups, width), lambda j: (0, j)),
            pl.BlockSpec((groups, width), lambda j: (0, j)),
        ],
        out_specs=pl.BlockSpec((1, comps, slots, width), lambda j: (j, 0, 0, 0)),
        out_shape=jax.ShapeDtypeStruct((parts, comps, slots, width), jnp.float32),
    )(xt, m, cos, sin)


def downward_kernel(pl_ref, m_ref, cos_ref, sin_ref, out_ref):
    g = pl.program_id(0)
    parts, comps, slots, width = pl_ref.shape
    half = comps // 2
    q = m_ref.shape[0]
    acc = jnp.zeros((q, comps * slots), jnp.float32)
    for d in range(parts):
        x = pl_ref[d]
        c = cos_ref[pl.ds(g, 1), pl.ds(d * width, width)].reshape(1, 1, width)
        s = sin_ref[pl.ds(g, 1), pl.ds(d * width, width)].reshape(1, 1, width)
        re = x[:half]
        im = x[half:]
        spread = jnp.concatenate([c * re + s * im, c * im - s * re], axis=0)
        spread = spread.reshape(comps * slots, width)
        acc = acc + lax.dot_general(
            m_ref[:, pl.ds(d * width, width)],
            spread,
            (((1,), (1,)), ((), ())),
            precision=HIGHEST,
            preferred_element_type=jnp.float32,
        )
    out_ref[0] = acc


def downward(parent_local, m, cos, sin):
    parts, comps, slots, width = parent_local.shape
    groups = cos.shape[0]
    q = m.shape[0]
    return pl.pallas_call(
        downward_kernel,
        grid=(groups,),
        in_specs=[
            pl.BlockSpec((parts, comps, slots, width), lambda g: (0, 0, 0, 0)),
            pl.BlockSpec((q, parts * width), lambda g: (0, 0)),
            pl.BlockSpec((groups, parts * width), lambda g: (0, 0)),
            pl.BlockSpec((groups, parts * width), lambda g: (0, 0)),
        ],
        out_specs=pl.BlockSpec((1, q, comps * slots), lambda g: (g, 0, 0)),
        out_shape=jax.ShapeDtypeStruct((groups, q, comps * slots), jnp.float32),
    )(parent_local, m, cos, sin)


def parent_translate(padded, coef_real, coef_imag, mask, reach):
    comps = padded.shape[0]
    half = comps // 2
    count = padded.shape[1] - 2 * reach
    offsets = list(range(-reach, 0)) + list(range(1, reach + 1))
    re_sum = jnp.zeros((half, count, padded.shape[2]), jnp.float32)
    im_sum = jnp.zeros((half, count, padded.shape[2]), jnp.float32)
    for position, offset in enumerate(offsets):
        source = padded[:, reach + offset : reach + offset + count]
        re = source[:half]
        im = source[half:]
        cr = coef_real[position][None, None, :]
        ci = coef_imag[position][None, None, :]
        weight = mask[position].astype(jnp.float32)[None, :, None]
        re_sum = re_sum + weight * (cr * re - ci * im)
        im_sum = im_sum + weight * (cr * im + ci * re)
    return jnp.concatenate([re_sum, im_sum], axis=0)


def body(
    pattern,
    child_coef,
    child_mask,
    interp_index,
    interp_weight,
    phase_angle,
    parent_coef,
    parent_mask,
):
    child_dev, comps, box_dev = pattern.shape
    dir_size = lax.axis_size("dir")
    parent_dirs = interp_index.shape[1]
    parent_dev = parent_dirs // dir_size
    groups = phase_angle.shape[0]
    slots = box_dev // groups
    dir_rank = lax.axis_index("dir")
    box_rank = lax.axis_index("box")
    child_first = dir_rank * child_dev
    parent_first = dir_rank * parent_dev
    cosine = jnp.cos(phase_angle)
    sine = jnp.sin(phase_angle)
    rows = interp_matrix(interp_index, interp_weight, child_first, child_dev)

    child_reach = child_coef.shape[1] // 2
    child_padded = with_halo(pattern, (("box", 2),), child_reach)
    child_local = translate_padded(
        child_padded, child_coef[0], child_coef[1], child_mask, child_reach
    )

    parent_reach = parent_coef.shape[1] // 2
    own_real = lax.dynamic_slice_in_dim(parent_coef[0], parent_first, parent_dev, 1)
    own_imag = lax.dynamic_slice_in_dim(parent_coef[1], parent_first, parent_dev, 1)
    own_mask = lax.dynamic_slice_in_dim(parent_mask, box_rank * slots, slots, 1)
    rhs = comps // 2
    step = rhs // CHUNKS
    fars = []
    for chunk in range(CHUNKS):
        part = pattern.reshape(child_dev, 2, rhs, box_dev)[:, :, chunk * step : (chunk + 1) * step]
        xt = part.reshape(child_dev, 2 * step, slots, groups).transpose(3, 1, 2, 0)
        xt = xt.reshape(groups, 2 * step * slots, child_dev)
        field = upward(xt, rows, cosine, sine, dir_size, 2 * step)
        field = dir_reduce_scatter(field)
        padded = with_halo(field, (("box", 1),), parent_reach)
        local = parent_translate(padded, own_real, own_imag, own_mask, parent_reach)
        local_all = dir_all_gather(local)
        far = downward(local_all, rows, cosine, sine)
        fars.append(far.reshape(groups, child_dev, 2, step, slots))
    far = jnp.concatenate(fars, axis=3).transpose(1, 2, 3, 4, 0)
    far = far.reshape(child_dev, comps, box_dev)
    return child_local + far


def solution(mesh):
    placed = (P("dir", None, "box"), P(None, None, "dir"), P(None, "box"), P(), P(), P(), P(), P())
    return jax.shard_map(
        body, mesh=mesh, in_specs=placed, out_specs=P("dir", None, "box"), check_vma=False
    )
```

```python
import jax
import jax.numpy as jnp
from jax import lax
from jax.experimental import pallas as pl
from jax.experimental.pallas import tpu as pltpu
from jax.sharding import PartitionSpec as P

HIGHEST = lax.Precision.HIGH
CHUNKS = 2


def with_halo(block, sides, width):
    for axis, dim in sides:
        count = lax.axis_size(axis)
        forward = [(i, i + 1) for i in range(count - 1)]
        backward = [(target, source) for source, target in forward]
        low = lax.ppermute(
            lax.slice_in_dim(block, block.shape[dim] - width, None, axis=dim), axis, forward
        )
        high = lax.ppermute(lax.slice_in_dim(block, 0, width, axis=dim), axis, backward)
        block = jnp.concatenate([low, block, high], axis=dim)
    return block


def dir_reduce_scatter(field):
    rank = lax.axis_index("dir")
    core = rank % 2
    row = rank // 2
    pairs = field.reshape((2, 2) + field.shape[1:])
    keep = lax.dynamic_index_in_dim(pairs, core, 1, keepdims=False)
    send = lax.dynamic_index_in_dim(pairs, 1 - core, 1, keepdims=False)
    acc = keep + lax.ppermute(send, "dir", [(0, 1), (1, 0), (2, 3), (3, 2)])
    keep = lax.dynamic_index_in_dim(acc, row, 0, keepdims=False)
    send = lax.dynamic_index_in_dim(acc, 1 - row, 0, keepdims=False)
    return keep + lax.ppermute(send, "dir", [(0, 2), (2, 0), (1, 3), (3, 1)])


def dir_all_gather(local):
    rank = lax.axis_index("dir")
    core = rank % 2
    row = rank // 2
    other = lax.ppermute(local, "dir", [(0, 2), (2, 0), (1, 3), (3, 1)])
    first = row == 0
    pair = jnp.stack([jnp.where(first, local, other), jnp.where(first, other, local)], axis=0)
    mate = lax.ppermute(pair, "dir", [(0, 1), (1, 0), (2, 3), (3, 2)])
    low = core == 0
    quad = jnp.stack([jnp.where(low, pair, mate), jnp.where(low, mate, pair)], axis=1)
    return quad.reshape((4,) + local.shape)


def interp_matrix(index, weight, first_row, row_count):
    rows = first_row + lax.iota(jnp.int32, row_count)
    matrix = jnp.zeros((row_count, index.shape[1]), jnp.float32)
    for point in range(index.shape[0]):
        matrix = matrix + jnp.where(
            rows[:, None] == index[point][None, :], weight[point][None, :], jnp.float32(0.0)
        )
    return matrix


def translate_padded(padded, coef_real, coef_imag, mask, reach):
    count = padded.shape[2] - 2 * reach
    half = padded.shape[1] // 2
    offsets = list(range(-reach, 0)) + list(range(1, reach + 1))
    summed = jnp.zeros((padded.shape[0], padded.shape[1], count), jnp.float32)
    for position, offset in enumerate(offsets):
        source = padded[:, :, reach + offset : reach + offset + count]
        real_part = source[:, :half]
        imag_part = source[:, half:]
        scale_real = coef_real[position][:, None, None]
        scale_imag = coef_imag[position][:, None, None]
        weight = mask[position].astype(jnp.float32)[None, None, :]
        turned = jnp.concatenate(
            [
                scale_real * real_part - scale_imag * imag_part,
                scale_real * imag_part + scale_imag * real_part,
            ],
            axis=1,
        )
        summed = summed + weight * turned
    return summed


def upward_kernel(xt_ref, m_ref, cos_ref, sin_ref, out_ref):
    groups = xt_ref.shape[0]
    comps, slots, width = out_ref.shape[1:]
    half = comps // 2
    m = m_ref[...]
    acc_re = jnp.zeros((half, slots, width), jnp.float32)
    acc_im = jnp.zeros((half, slots, width), jnp.float32)
    for g in range(groups):
        r = jnp.dot(xt_ref[g], m, precision=HIGHEST, preferred_element_type=jnp.float32)
        r = r.reshape(comps, slots, width)
        c = cos_ref[pl.ds(g, 1), :].reshape(1, 1, width)
        s = sin_ref[pl.ds(g, 1), :].reshape(1, 1, width)
        re = r[:half]
        im = r[half:]
        acc_re = acc_re + (c * re - s * im)
        acc_im = acc_im + (c * im + s * re)
    out_ref[0, :half] = acc_re
    out_ref[0, half:] = acc_im


def upward(xt, m, cos, sin, parts, comps):
    groups, rows, q = xt.shape
    total = m.shape[1]
    width = total // parts
    slots = rows // comps
    return pl.pallas_call(
        upward_kernel,
        grid=(parts,),
        in_specs=[
            pl.BlockSpec((groups, rows, q), lambda j: (0, 0, 0)),
            pl.BlockSpec((q, width), lambda j: (0, j)),
            pl.BlockSpec((groups, width), lambda j: (0, j)),
            pl.BlockSpec((groups, width), lambda j: (0, j)),
        ],
        out_specs=pl.BlockSpec((1, comps, slots, width), lambda j: (j, 0, 0, 0)),
        out_shape=jax.ShapeDtypeStruct((parts, comps, slots, width), jnp.float32),
    )(xt, m, cos, sin)


def downward_kernel(pl_ref, m_ref, cos_ref, sin_ref, out_ref):
    g = pl.program_id(0)
    parts, comps, slots, width = pl_ref.shape
    half = comps // 2
    q = m_ref.shape[0]
    acc = jnp.zeros((q, comps * slots), jnp.float32)
    for d in range(parts):
        x = pl_ref[d]
        c = cos_ref[pl.ds(g, 1), pl.ds(d * width, width)].reshape(1, 1, width)
        s = sin_ref[pl.ds(g, 1), pl.ds(d * width, width)].reshape(1, 1, width)
        re = x[:half]
        im = x[half:]
        spread = jnp.concatenate([c * re + s * im, c * im - s * re], axis=0)
        spread = spread.reshape(comps * slots, width)
        acc = acc + lax.dot_general(
            m_ref[:, pl.ds(d * width, width)],
            spread,
            (((1,), (1,)), ((), ())),
            precision=HIGHEST,
            preferred_element_type=jnp.float32,
        )
    out_ref[0] = acc


def downward(parent_local, m, cos, sin):
    parts, comps, slots, width = parent_local.shape
    groups = cos.shape[0]
    q = m.shape[0]
    return pl.pallas_call(
        downward_kernel,
        grid=(groups,),
        in_specs=[
            pl.BlockSpec((parts, comps, slots, width), lambda g: (0, 0, 0, 0)),
            pl.BlockSpec((q, parts * width), lambda g: (0, 0)),
            pl.BlockSpec((groups, parts * width), lambda g: (0, 0)),
            pl.BlockSpec((groups, parts * width), lambda g: (0, 0)),
        ],
        out_specs=pl.BlockSpec((1, q, comps * slots), lambda g: (g, 0, 0)),
        out_shape=jax.ShapeDtypeStruct((groups, q, comps * slots), jnp.float32),
    )(parent_local, m, cos, sin)


def parent_translate(padded, coef_real, coef_imag, mask, reach):
    comps = padded.shape[0]
    half = comps // 2
    count = padded.shape[1] - 2 * reach
    offsets = list(range(-reach, 0)) + list(range(1, reach + 1))
    re_sum = jnp.zeros((half, count, padded.shape[2]), jnp.float32)
    im_sum = jnp.zeros((half, count, padded.shape[2]), jnp.float32)
    for position, offset in enumerate(offsets):
        source = padded[:, reach + offset : reach + offset + count]
        re = source[:half]
        im = source[half:]
        cr = coef_real[position][None, None, :]
        ci = coef_imag[position][None, None, :]
        weight = mask[position].astype(jnp.float32)[None, :, None]
        re_sum = re_sum + weight * (cr * re - ci * im)
        im_sum = im_sum + weight * (cr * im + ci * re)
    return jnp.concatenate([re_sum, im_sum], axis=0)


def body(
    pattern,
    child_coef,
    child_mask,
    interp_index,
    interp_weight,
    phase_angle,
    parent_coef,
    parent_mask,
):
    child_dev, comps, box_dev = pattern.shape
    dir_size = lax.axis_size("dir")
    parent_dirs = interp_index.shape[1]
    parent_dev = parent_dirs // dir_size
    groups = phase_angle.shape[0]
    slots = box_dev // groups
    dir_rank = lax.axis_index("dir")
    box_rank = lax.axis_index("box")
    child_first = dir_rank * child_dev
    parent_first = dir_rank * parent_dev
    cosine = jnp.cos(phase_angle)
    sine = jnp.sin(phase_angle)
    rows = interp_matrix(interp_index, interp_weight, child_first, child_dev)

    child_reach = child_coef.shape[1] // 2
    child_padded = with_halo(pattern, (("box", 2),), child_reach)
    child_local = translate_padded(
        child_padded, child_coef[0], child_coef[1], child_mask, child_reach
    )

    parent_reach = parent_coef.shape[1] // 2
    own_real = lax.dynamic_slice_in_dim(parent_coef[0], parent_first, parent_dev, 1)
    own_imag = lax.dynamic_slice_in_dim(parent_coef[1], parent_first, parent_dev, 1)
    own_mask = lax.dynamic_slice_in_dim(parent_mask, box_rank * slots, slots, 1)
    rhs = comps // 2
    step = rhs // CHUNKS
    fars = []
    for chunk in range(CHUNKS):
        part = pattern.reshape(child_dev, 2, rhs, box_dev)[:, :, chunk * step : (chunk + 1) * step]
        xt = part.reshape(child_dev, 2 * step, slots, groups).transpose(3, 1, 2, 0)
        xt = xt.reshape(groups, 2 * step * slots, child_dev)
        field = upward(xt, rows, cosine, sine, dir_size, 2 * step)
        field = dir_reduce_scatter(field)
        padded = with_halo(field, (("box", 1),), parent_reach)
        local = parent_translate(padded, own_real, own_imag, own_mask, parent_reach)
        local_all = dir_all_gather(local)
        far = downward(local_all, rows, cosine, sine)
        fars.append(far.reshape(groups, child_dev, 2, step, slots))
    far = jnp.concatenate(fars, axis=3).transpose(1, 2, 3, 4, 0)
    far = far.reshape(child_dev, comps, box_dev)
    return child_local + far


def solution(mesh):
    placed = (P("dir", None, "box"), P(None, None, "dir"), P(None, "box"), P(), P(), P(), P(), P())
    return jax.shard_map(
        body, mesh=mesh, in_specs=placed, out_specs=P("dir", None, "box"), check_vma=False
    )
```

```python
import jax
import jax.numpy as jnp
from jax import lax
from jax.experimental import pallas as pl
from jax.experimental.pallas import tpu as pltpu
from jax.sharding import PartitionSpec as P

HIGHEST = lax.Precision.HIGH
CHUNKS = 4


def with_halo(block, sides, width):
    for axis, dim in sides:
        count = lax.axis_size(axis)
        forward = [(i, i + 1) for i in range(count - 1)]
        backward = [(target, source) for source, target in forward]
        low = lax.ppermute(
            lax.slice_in_dim(block, block.shape[dim] - width, None, axis=dim), axis, forward
        )
        high = lax.ppermute(lax.slice_in_dim(block, 0, width, axis=dim), axis, backward)
        block = jnp.concatenate([low, block, high], axis=dim)
    return block


def dir_reduce_scatter(field):
    rank = lax.axis_index("dir")
    core = rank % 2
    row = rank // 2
    pairs = field.reshape((2, 2) + field.shape[1:])
    keep = lax.dynamic_index_in_dim(pairs, core, 1, keepdims=False)
    send = lax.dynamic_index_in_dim(pairs, 1 - core, 1, keepdims=False)
    acc = keep + lax.ppermute(send, "dir", [(0, 1), (1, 0), (2, 3), (3, 2)])
    keep = lax.dynamic_index_in_dim(acc, row, 0, keepdims=False)
    send = lax.dynamic_index_in_dim(acc, 1 - row, 0, keepdims=False)
    return keep + lax.ppermute(send, "dir", [(0, 2), (2, 0), (1, 3), (3, 1)])


def dir_all_gather(local):
    rank = lax.axis_index("dir")
    core = rank % 2
    row = rank // 2
    other = lax.ppermute(local, "dir", [(0, 2), (2, 0), (1, 3), (3, 1)])
    first = row == 0
    pair = jnp.stack([jnp.where(first, local, other), jnp.where(first, other, local)], axis=0)
    mate = lax.ppermute(pair, "dir", [(0, 1), (1, 0), (2, 3), (3, 2)])
    low = core == 0
    quad = jnp.stack([jnp.where(low, pair, mate), jnp.where(low, mate, pair)], axis=1)
    return quad.reshape((4,) + local.shape)


def interp_matrix(index, weight, first_row, row_count):
    rows = first_row + lax.iota(jnp.int32, row_count)
    matrix = jnp.zeros((row_count, index.shape[1]), jnp.float32)
    for point in range(index.shape[0]):
        matrix = matrix + jnp.where(
            rows[:, None] == index[point][None, :], weight[point][None, :], jnp.float32(0.0)
        )
    return matrix


def translate_padded(padded, coef_real, coef_imag, mask, reach):
    count = padded.shape[2] - 2 * reach
    half = padded.shape[1] // 2
    offsets = list(range(-reach, 0)) + list(range(1, reach + 1))
    summed = jnp.zeros((padded.shape[0], padded.shape[1], count), jnp.float32)
    for position, offset in enumerate(offsets):
        source = padded[:, :, reach + offset : reach + offset + count]
        real_part = source[:, :half]
        imag_part = source[:, half:]
        scale_real = coef_real[position][:, None, None]
        scale_imag = coef_imag[position][:, None, None]
        weight = mask[position].astype(jnp.float32)[None, None, :]
        turned = jnp.concatenate(
            [
                scale_real * real_part - scale_imag * imag_part,
                scale_real * imag_part + scale_imag * real_part,
            ],
            axis=1,
        )
        summed = summed + weight * turned
    return summed


def upward_kernel(xt_ref, m_ref, cos_ref, sin_ref, out_ref):
    groups = xt_ref.shape[0]
    comps, slots, width = out_ref.shape[1:]
    half = comps // 2
    m = m_ref[...]
    acc_re = jnp.zeros((half, slots, width), jnp.float32)
    acc_im = jnp.zeros((half, slots, width), jnp.float32)
    for g in range(groups):
        r = jnp.dot(xt_ref[g], m, precision=HIGHEST, preferred_element_type=jnp.float32)
        r = r.reshape(comps, slots, width)
        c = cos_ref[pl.ds(g, 1), :].reshape(1, 1, width)
        s = sin_ref[pl.ds(g, 1), :].reshape(1, 1, width)
        re = r[:half]
        im = r[half:]
        acc_re = acc_re + (c * re - s * im)
        acc_im = acc_im + (c * im + s * re)
    out_ref[0, :half] = acc_re
    out_ref[0, half:] = acc_im


def upward(xt, m, cos, sin, parts, comps):
    groups, rows, q = xt.shape
    total = m.shape[1]
    width = total // parts
    slots = rows // comps
    return pl.pallas_call(
        upward_kernel,
        grid=(parts,),
        in_specs=[
            pl.BlockSpec((groups, rows, q), lambda j: (0, 0, 0)),
            pl.BlockSpec((q, width), lambda j: (0, j)),
            pl.BlockSpec((groups, width), lambda j: (0, j)),
            pl.BlockSpec((groups, width), lambda j: (0, j)),
        ],
        out_specs=pl.BlockSpec((1, comps, slots, width), lambda j: (j, 0, 0, 0)),
        out_shape=jax.ShapeDtypeStruct((parts, comps, slots, width), jnp.float32),
    )(xt, m, cos, sin)


def downward_kernel(pl_ref, m_ref, cos_ref, sin_ref, out_ref):
    g = pl.program_id(0)
    parts, comps, slots, width = pl_ref.shape
    half = comps // 2
    q = m_ref.shape[0]
    acc = jnp.zeros((q, comps * slots), jnp.float32)
    for d in range(parts):
        x = pl_ref[d]
        c = cos_ref[pl.ds(g, 1), pl.ds(d * width, width)].reshape(1, 1, width)
        s = sin_ref[pl.ds(g, 1), pl.ds(d * width, width)].reshape(1, 1, width)
        re = x[:half]
        im = x[half:]
        spread = jnp.concatenate([c * re + s * im, c * im - s * re], axis=0)
        spread = spread.reshape(comps * slots, width)
        acc = acc + lax.dot_general(
            m_ref[:, pl.ds(d * width, width)],
            spread,
            (((1,), (1,)), ((), ())),
            precision=HIGHEST,
            preferred_element_type=jnp.float32,
        )
    out_ref[0] = acc


def downward(parent_local, m, cos, sin):
    parts, comps, slots, width = parent_local.shape
    groups = cos.shape[0]
    q = m.shape[0]
    return pl.pallas_call(
        downward_kernel,
        grid=(groups,),
        in_specs=[
            pl.BlockSpec((parts, comps, slots, width), lambda g: (0, 0, 0, 0)),
            pl.BlockSpec((q, parts * width), lambda g: (0, 0)),
            pl.BlockSpec((groups, parts * width), lambda g: (0, 0)),
            pl.BlockSpec((groups, parts * width), lambda g: (0, 0)),
        ],
        out_specs=pl.BlockSpec((1, q, comps * slots), lambda g: (g, 0, 0)),
        out_shape=jax.ShapeDtypeStruct((groups, q, comps * slots), jnp.float32),
    )(parent_local, m, cos, sin)


def parent_translate(padded, coef_real, coef_imag, mask, reach):
    comps = padded.shape[0]
    half = comps // 2
    count = padded.shape[1] - 2 * reach
    offsets = list(range(-reach, 0)) + list(range(1, reach + 1))
    re_sum = jnp.zeros((half, count, padded.shape[2]), jnp.float32)
    im_sum = jnp.zeros((half, count, padded.shape[2]), jnp.float32)
    for position, offset in enumerate(offsets):
        source = padded[:, reach + offset : reach + offset + count]
        re = source[:half]
        im = source[half:]
        cr = coef_real[position][None, None, :]
        ci = coef_imag[position][None, None, :]
        weight = mask[position].astype(jnp.float32)[None, :, None]
        re_sum = re_sum + weight * (cr * re - ci * im)
        im_sum = im_sum + weight * (cr * im + ci * re)
    return jnp.concatenate([re_sum, im_sum], axis=0)


def body(
    pattern,
    child_coef,
    child_mask,
    interp_index,
    interp_weight,
    phase_angle,
    parent_coef,
    parent_mask,
):
    child_dev, comps, box_dev = pattern.shape
    dir_size = lax.axis_size("dir")
    parent_dirs = interp_index.shape[1]
    parent_dev = parent_dirs // dir_size
    groups = phase_angle.shape[0]
    slots = box_dev // groups
    dir_rank = lax.axis_index("dir")
    box_rank = lax.axis_index("box")
    child_first = dir_rank * child_dev
    parent_first = dir_rank * parent_dev
    cosine = jnp.cos(phase_angle)
    sine = jnp.sin(phase_angle)
    rows = interp_matrix(interp_index, interp_weight, child_first, child_dev)

    child_reach = child_coef.shape[1] // 2
    child_padded = with_halo(pattern, (("box", 2),), child_reach)
    child_local = translate_padded(
        child_padded, child_coef[0], child_coef[1], child_mask, child_reach
    )

    parent_reach = parent_coef.shape[1] // 2
    own_real = lax.dynamic_slice_in_dim(parent_coef[0], parent_first, parent_dev, 1)
    own_imag = lax.dynamic_slice_in_dim(parent_coef[1], parent_first, parent_dev, 1)
    own_mask = lax.dynamic_slice_in_dim(parent_mask, box_rank * slots, slots, 1)
    rhs = comps // 2
    step = rhs // CHUNKS
    fars = []
    for chunk in range(CHUNKS):
        part = pattern.reshape(child_dev, 2, rhs, box_dev)[:, :, chunk * step : (chunk + 1) * step]
        xt = part.reshape(child_dev, 2 * step, slots, groups).transpose(3, 1, 2, 0)
        xt = xt.reshape(groups, 2 * step * slots, child_dev)
        field = upward(xt, rows, cosine, sine, dir_size, 2 * step)
        field = dir_reduce_scatter(field)
        padded = with_halo(field, (("box", 1),), parent_reach)
        local = parent_translate(padded, own_real, own_imag, own_mask, parent_reach)
        local_all = dir_all_gather(local)
        far = downward(local_all, rows, cosine, sine)
        fars.append(far.reshape(groups, child_dev, 2, step, slots))
    far = jnp.concatenate(fars, axis=3).transpose(1, 2, 3, 4, 0)
    far = far.reshape(child_dev, comps, box_dev)
    return child_local + far


def solution(mesh):
    placed = (P("dir", None, "box"), P(None, None, "dir"), P(None, "box"), P(), P(), P(), P(), P())
    return jax.shard_map(
        body, mesh=mesh, in_specs=placed, out_specs=P("dir", None, "box"), check_vma=False
    )
```

```python
import jax
import jax.numpy as jnp
from jax import lax
from jax.experimental import pallas as pl
from jax.experimental.pallas import tpu as pltpu
from jax.sharding import PartitionSpec as P

HIGHEST = lax.Precision.HIGH


def with_halo(block, sides, width):
    for axis, dim in sides:
        count = lax.axis_size(axis)
        forward = [(i, i + 1) for i in range(count - 1)]
        backward = [(target, source) for source, target in forward]
        low = lax.ppermute(
            lax.slice_in_dim(block, block.shape[dim] - width, None, axis=dim), axis, forward
        )
        high = lax.ppermute(lax.slice_in_dim(block, 0, width, axis=dim), axis, backward)
        block = jnp.concatenate([low, block, high], axis=dim)
    return block


CORE_SWAP = [(0, 1), (1, 0), (2, 3), (3, 2)]
ROW_SWAP = [(0, 2), (2, 0), (1, 3), (3, 1)]


def reduce_cores(field):
    core = lax.axis_index("dir") % 2
    pairs = field.reshape((2, 2) + field.shape[1:])
    keep = lax.dynamic_index_in_dim(pairs, core, 1, keepdims=False)
    send = lax.dynamic_index_in_dim(pairs, 1 - core, 1, keepdims=False)
    return keep + lax.ppermute(send, "dir", CORE_SWAP)


def split_rows(acc):
    row = lax.axis_index("dir") // 2
    keep = lax.dynamic_index_in_dim(acc, row, 0, keepdims=False)
    send = lax.dynamic_index_in_dim(acc, 1 - row, 0, keepdims=False)
    return keep, send


def gather_cores(local, other):
    rank = lax.axis_index("dir")
    first = rank // 2 == 0
    pair = jnp.stack([jnp.where(first, local, other), jnp.where(first, other, local)], axis=0)
    mate = lax.ppermute(pair, "dir", CORE_SWAP)
    low = rank % 2 == 0
    quad = jnp.stack([jnp.where(low, pair, mate), jnp.where(low, mate, pair)], axis=1)
    return quad.reshape((4,) + local.shape)


def interp_matrix(index, weight, first_row, row_count):
    rows = first_row + lax.iota(jnp.int32, row_count)
    matrix = jnp.zeros((row_count, index.shape[1]), jnp.float32)
    for point in range(index.shape[0]):
        matrix = matrix + jnp.where(
            rows[:, None] == index[point][None, :], weight[point][None, :], jnp.float32(0.0)
        )
    return matrix


def translate_padded(padded, coef_real, coef_imag, mask, reach):
    count = padded.shape[2] - 2 * reach
    half = padded.shape[1] // 2
    offsets = list(range(-reach, 0)) + list(range(1, reach + 1))
    summed = jnp.zeros((padded.shape[0], padded.shape[1], count), jnp.float32)
    for position, offset in enumerate(offsets):
        source = padded[:, :, reach + offset : reach + offset + count]
        real_part = source[:, :half]
        imag_part = source[:, half:]
        scale_real = coef_real[position][:, None, None]
        scale_imag = coef_imag[position][:, None, None]
        weight = mask[position].astype(jnp.float32)[None, None, :]
        turned = jnp.concatenate(
            [
                scale_real * real_part - scale_imag * imag_part,
                scale_real * imag_part + scale_imag * real_part,
            ],
            axis=1,
        )
        summed = summed + weight * turned
    return summed


def upward_kernel(xt_ref, m_ref, cos_ref, sin_ref, out_ref):
    groups = xt_ref.shape[0]
    comps, slots, width = out_ref.shape[1:]
    half = comps // 2
    m = m_ref[...]
    acc_re = jnp.zeros((half, slots, width), jnp.float32)
    acc_im = jnp.zeros((half, slots, width), jnp.float32)
    for g in range(groups):
        r = jnp.dot(xt_ref[g], m, precision=HIGHEST, preferred_element_type=jnp.float32)
        r = r.reshape(comps, slots, width)
        c = cos_ref[pl.ds(g, 1), :].reshape(1, 1, width)
        s = sin_ref[pl.ds(g, 1), :].reshape(1, 1, width)
        re = r[:half]
        im = r[half:]
        acc_re = acc_re + (c * re - s * im)
        acc_im = acc_im + (c * im + s * re)
    out_ref[0, :half] = acc_re
    out_ref[0, half:] = acc_im


def upward(xt, m, cos, sin, parts, comps):
    groups, rows, q = xt.shape
    total = m.shape[1]
    width = total // parts
    slots = rows // comps
    return pl.pallas_call(
        upward_kernel,
        grid=(parts,),
        in_specs=[
            pl.BlockSpec((groups, rows, q), lambda j: (0, 0, 0)),
            pl.BlockSpec((q, width), lambda j: (0, j)),
            pl.BlockSpec((groups, width), lambda j: (0, j)),
            pl.BlockSpec((groups, width), lambda j: (0, j)),
        ],
        out_specs=pl.BlockSpec((1, comps, slots, width), lambda j: (j, 0, 0, 0)),
        out_shape=jax.ShapeDtypeStruct((parts, comps, slots, width), jnp.float32),
    )(xt, m, cos, sin)


def downward_kernel(pl_ref, m_ref, cos_ref, sin_ref, out_ref):
    g = pl.program_id(0)
    parts, comps, slots, width = pl_ref.shape
    half = comps // 2
    q = m_ref.shape[0]
    acc = jnp.zeros((q, comps * slots), jnp.float32)
    for d in range(parts):
        x = pl_ref[d]
        c = cos_ref[pl.ds(g, 1), pl.ds(d * width, width)].reshape(1, 1, width)
        s = sin_ref[pl.ds(g, 1), pl.ds(d * width, width)].reshape(1, 1, width)
        re = x[:half]
        im = x[half:]
        spread = jnp.concatenate([c * re + s * im, c * im - s * re], axis=0)
        spread = spread.reshape(comps * slots, width)
        acc = acc + lax.dot_general(
            m_ref[:, pl.ds(d * width, width)],
            spread,
            (((1,), (1,)), ((), ())),
            precision=HIGHEST,
            preferred_element_type=jnp.float32,
        )
    out_ref[0] = acc


def downward(parent_local, m, cos, sin):
    parts, comps, slots, width = parent_local.shape
    groups = cos.shape[0]
    q = m.shape[0]
    return pl.pallas_call(
        downward_kernel,
        grid=(groups,),
        in_specs=[
            pl.BlockSpec((parts, comps, slots, width), lambda g: (0, 0, 0, 0)),
            pl.BlockSpec((q, parts * width), lambda g: (0, 0)),
            pl.BlockSpec((groups, parts * width), lambda g: (0, 0)),
            pl.BlockSpec((groups, parts * width), lambda g: (0, 0)),
        ],
        out_specs=pl.BlockSpec((1, q, comps * slots), lambda g: (g, 0, 0)),
        out_shape=jax.ShapeDtypeStruct((groups, q, comps * slots), jnp.float32),
    )(parent_local, m, cos, sin)


def parent_translate(padded, coef_real, coef_imag, mask, reach):
    comps = padded.shape[0]
    half = comps // 2
    count = padded.shape[1] - 2 * reach
    offsets = list(range(-reach, 0)) + list(range(1, reach + 1))
    re_sum = jnp.zeros((half, count, padded.shape[2]), jnp.float32)
    im_sum = jnp.zeros((half, count, padded.shape[2]), jnp.float32)
    for position, offset in enumerate(offsets):
        source = padded[:, reach + offset : reach + offset + count]
        re = source[:half]
        im = source[half:]
        cr = coef_real[position][None, None, :]
        ci = coef_imag[position][None, None, :]
        weight = mask[position].astype(jnp.float32)[None, :, None]
        re_sum = re_sum + weight * (cr * re - ci * im)
        im_sum = im_sum + weight * (cr * im + ci * re)
    return jnp.concatenate([re_sum, im_sum], axis=0)


def body(
    pattern,
    child_coef,
    child_mask,
    interp_index,
    interp_weight,
    phase_angle,
    parent_coef,
    parent_mask,
):
    child_dev, comps, box_dev = pattern.shape
    dir_size = lax.axis_size("dir")
    parent_dirs = interp_index.shape[1]
    parent_dev = parent_dirs // dir_size
    groups = phase_angle.shape[0]
    slots = box_dev // groups
    dir_rank = lax.axis_index("dir")
    box_rank = lax.axis_index("box")
    child_first = dir_rank * child_dev
    parent_first = dir_rank * parent_dev
    cosine = jnp.cos(phase_angle)
    sine = jnp.sin(phase_angle)
    rows = interp_matrix(interp_index, interp_weight, child_first, child_dev)

    child_reach = child_coef.shape[1] // 2
    child_padded = with_halo(pattern, (("box", 2),), child_reach)
    child_local = translate_padded(
        child_padded, child_coef[0], child_coef[1], child_mask, child_reach
    )

    parent_reach = parent_coef.shape[1] // 2
    own_real = lax.dynamic_slice_in_dim(parent_coef[0], parent_first, parent_dev, 1)
    own_imag = lax.dynamic_slice_in_dim(parent_coef[1], parent_first, parent_dev, 1)
    own_mask = lax.dynamic_slice_in_dim(parent_mask, box_rank * slots, slots, 1)
    rhs = comps // 2
    step = rhs // 2

    def chunk_xt(chunk):
        part = pattern.reshape(child_dev, 2, rhs, box_dev)[:, :, chunk * step : (chunk + 1) * step]
        xt = part.reshape(child_dev, 2 * step, slots, groups).transpose(3, 1, 2, 0)
        return xt.reshape(groups, 2 * step * slots, child_dev)

    def translate(field):
        padded = with_halo(field, (("box", 1),), parent_reach)
        return parent_translate(padded, own_real, own_imag, own_mask, parent_reach)

    acc_a = reduce_cores(upward(chunk_xt(0), rows, cosine, sine, dir_size, 2 * step))
    acc_a, xt_b = lax.optimization_barrier((acc_a, chunk_xt(1)))
    keep_a, send_a = split_rows(acc_a)
    recv_a = lax.ppermute(send_a, "dir", ROW_SWAP)
    field_b = upward(xt_b, rows, cosine, sine, dir_size, 2 * step)
    field_b, recv_a = lax.optimization_barrier((field_b, recv_a))
    sum_a = keep_a + recv_a
    acc_b = reduce_cores(field_b)
    sum_a, acc_b = lax.optimization_barrier((sum_a, acc_b))
    keep_b, send_b = split_rows(acc_b)
    recv_b = lax.ppermute(send_b, "dir", ROW_SWAP)
    local_a = translate(sum_a)
    local_a, recv_b = lax.optimization_barrier((local_a, recv_b))
    sum_b = keep_b + recv_b
    other_a = lax.ppermute(local_a, "dir", ROW_SWAP)
    local_b = translate(sum_b)
    other_a, local_b = lax.optimization_barrier((other_a, local_b))
    all_a = gather_cores(local_a, other_a)
    all_a, local_b = lax.optimization_barrier((all_a, local_b))
    other_b = lax.ppermute(local_b, "dir", ROW_SWAP)
    far_a = downward(all_a, rows, cosine, sine)
    far_a, other_b = lax.optimization_barrier((far_a, other_b))
    far_b = downward(gather_cores(local_b, other_b), rows, cosine, sine)
    fars = [far.reshape(groups, child_dev, 2, step, slots) for far in (far_a, far_b)]
    far = jnp.concatenate(fars, axis=3).transpose(1, 2, 3, 4, 0)
    far = far.reshape(child_dev, comps, box_dev)
    return child_local + far


def solution(mesh):
    placed = (P("dir", None, "box"), P(None, None, "dir"), P(None, "box"), P(), P(), P(), P(), P())
    return jax.shard_map(
        body, mesh=mesh, in_specs=placed, out_specs=P("dir", None, "box"), check_vma=False
    )
```

```python
import jax
import jax.numpy as jnp
from jax import lax
from jax.experimental import pallas as pl
from jax.experimental.pallas import tpu as pltpu
from jax.sharding import PartitionSpec as P

HIGHEST = lax.Precision.HIGH


def with_halo(block, sides, width):
    for axis, dim in sides:
        count = lax.axis_size(axis)
        forward = [(i, i + 1) for i in range(count - 1)]
        backward = [(target, source) for source, target in forward]
        low = lax.ppermute(
            lax.slice_in_dim(block, block.shape[dim] - width, None, axis=dim), axis, forward
        )
        high = lax.ppermute(lax.slice_in_dim(block, 0, width, axis=dim), axis, backward)
        block = jnp.concatenate([low, block, high], axis=dim)
    return block


CORE_SWAP = [(0, 1), (1, 0), (2, 3), (3, 2)]
ROW_SWAP = [(0, 2), (2, 0), (1, 3), (3, 1)]


def reduce_cores(field):
    core = lax.axis_index("dir") % 2
    pairs = field.reshape((2, 2) + field.shape[1:])
    keep = lax.dynamic_index_in_dim(pairs, core, 1, keepdims=False)
    send = lax.dynamic_index_in_dim(pairs, 1 - core, 1, keepdims=False)
    return keep + lax.ppermute(send, "dir", CORE_SWAP)


def split_rows(acc):
    row = lax.axis_index("dir") // 2
    keep = lax.dynamic_index_in_dim(acc, row, 0, keepdims=False)
    send = lax.dynamic_index_in_dim(acc, 1 - row, 0, keepdims=False)
    return keep, send


def gather_cores(local, other):
    rank = lax.axis_index("dir")
    first = rank // 2 == 0
    pair = jnp.stack([jnp.where(first, local, other), jnp.where(first, other, local)], axis=0)
    mate = lax.ppermute(pair, "dir", CORE_SWAP)
    low = rank % 2 == 0
    quad = jnp.stack([jnp.where(low, pair, mate), jnp.where(low, mate, pair)], axis=1)
    return quad.reshape((4,) + local.shape)


def pack(pieces):
    return jnp.concatenate([piece.reshape(-1) for piece in pieces])


def unpack(flat, like):
    out, first = [], 0
    for piece in like:
        out.append(flat[first : first + piece.size].reshape(piece.shape))
        first += piece.size
    return out


def interp_matrix(index, weight, first_row, row_count):
    rows = first_row + lax.iota(jnp.int32, row_count)
    matrix = jnp.zeros((row_count, index.shape[1]), jnp.float32)
    for point in range(index.shape[0]):
        matrix = matrix + jnp.where(
            rows[:, None] == index[point][None, :], weight[point][None, :], jnp.float32(0.0)
        )
    return matrix


def translate_padded(padded, coef_real, coef_imag, mask, reach):
    count = padded.shape[2] - 2 * reach
    half = padded.shape[1] // 2
    offsets = list(range(-reach, 0)) + list(range(1, reach + 1))
    summed = jnp.zeros((padded.shape[0], padded.shape[1], count), jnp.float32)
    for position, offset in enumerate(offsets):
        source = padded[:, :, reach + offset : reach + offset + count]
        real_part = source[:, :half]
        imag_part = source[:, half:]
        scale_real = coef_real[position][:, None, None]
        scale_imag = coef_imag[position][:, None, None]
        weight = mask[position].astype(jnp.float32)[None, None, :]
        turned = jnp.concatenate(
            [
                scale_real * real_part - scale_imag * imag_part,
                scale_real * imag_part + scale_imag * real_part,
            ],
            axis=1,
        )
        summed = summed + weight * turned
    return summed


def upward_kernel(xt_ref, m_ref, cos_ref, sin_ref, out_ref):
    groups = xt_ref.shape[0]
    comps, slots, width = out_ref.shape[1:]
    half = comps // 2
    m = m_ref[...]
    acc_re = jnp.zeros((half, slots, width), jnp.float32)
    acc_im = jnp.zeros((half, slots, width), jnp.float32)
    for g in range(groups):
        r = jnp.dot(xt_ref[g], m, precision=HIGHEST, preferred_element_type=jnp.float32)
        r = r.reshape(comps, slots, width)
        c = cos_ref[pl.ds(g, 1), :].reshape(1, 1, width)
        s = sin_ref[pl.ds(g, 1), :].reshape(1, 1, width)
        re = r[:half]
        im = r[half:]
        acc_re = acc_re + (c * re - s * im)
        acc_im = acc_im + (c * im + s * re)
    out_ref[0, :half] = acc_re
    out_ref[0, half:] = acc_im


def upward(xt, m, cos, sin, parts, comps):
    groups, rows, q = xt.shape
    total = m.shape[1]
    width = total // parts
    slots = rows // comps
    return pl.pallas_call(
        upward_kernel,
        grid=(parts,),
        in_specs=[
            pl.BlockSpec((groups, rows, q), lambda j: (0, 0, 0)),
            pl.BlockSpec((q, width), lambda j: (0, j)),
            pl.BlockSpec((groups, width), lambda j: (0, j)),
            pl.BlockSpec((groups, width), lambda j: (0, j)),
        ],
        out_specs=pl.BlockSpec((1, comps, slots, width), lambda j: (j, 0, 0, 0)),
        out_shape=jax.ShapeDtypeStruct((parts, comps, slots, width), jnp.float32),
    )(xt, m, cos, sin)


def downward_kernel(pl_ref, m_ref, cos_ref, sin_ref, out_ref):
    g = pl.program_id(0)
    parts, comps, slots, width = pl_ref.shape
    half = comps // 2
    q = m_ref.shape[0]
    acc = jnp.zeros((q, comps * slots), jnp.float32)
    for d in range(parts):
        x = pl_ref[d]
        c = cos_ref[pl.ds(g, 1), pl.ds(d * width, width)].reshape(1, 1, width)
        s = sin_ref[pl.ds(g, 1), pl.ds(d * width, width)].reshape(1, 1, width)
        re = x[:half]
        im = x[half:]
        spread = jnp.concatenate([c * re + s * im, c * im - s * re], axis=0)
        spread = spread.reshape(comps * slots, width)
        acc = acc + lax.dot_general(
            m_ref[:, pl.ds(d * width, width)],
            spread,
            (((1,), (1,)), ((), ())),
            precision=HIGHEST,
            preferred_element_type=jnp.float32,
        )
    out_ref[0] = acc


def downward(parent_local, m, cos, sin):
    parts, comps, slots, width = parent_local.shape
    groups = cos.shape[0]
    q = m.shape[0]
    return pl.pallas_call(
        downward_kernel,
        grid=(groups,),
        in_specs=[
            pl.BlockSpec((parts, comps, slots, width), lambda g: (0, 0, 0, 0)),
            pl.BlockSpec((q, parts * width), lambda g: (0, 0)),
            pl.BlockSpec((groups, parts * width), lambda g: (0, 0)),
            pl.BlockSpec((groups, parts * width), lambda g: (0, 0)),
        ],
        out_specs=pl.BlockSpec((1, q, comps * slots), lambda g: (g, 0, 0)),
        out_shape=jax.ShapeDtypeStruct((groups, q, comps * slots), jnp.float32),
    )(parent_local, m, cos, sin)


def parent_translate(padded, coef_real, coef_imag, mask, reach):
    comps = padded.shape[0]
    half = comps // 2
    count = padded.shape[1] - 2 * reach
    offsets = list(range(-reach, 0)) + list(range(1, reach + 1))
    re_sum = jnp.zeros((half, count, padded.shape[2]), jnp.float32)
    im_sum = jnp.zeros((half, count, padded.shape[2]), jnp.float32)
    for position, offset in enumerate(offsets):
        source = padded[:, reach + offset : reach + offset + count]
        re = source[:half]
        im = source[half:]
        cr = coef_real[position][None, None, :]
        ci = coef_imag[position][None, None, :]
        weight = mask[position].astype(jnp.float32)[None, :, None]
        re_sum = re_sum + weight * (cr * re - ci * im)
        im_sum = im_sum + weight * (cr * im + ci * re)
    return jnp.concatenate([re_sum, im_sum], axis=0)


def body(
    pattern,
    child_coef,
    child_mask,
    interp_index,
    interp_weight,
    phase_angle,
    parent_coef,
    parent_mask,
):
    child_dev, comps, box_dev = pattern.shape
    dir_size = lax.axis_size("dir")
    parent_dirs = interp_index.shape[1]
    parent_dev = parent_dirs // dir_size
    groups = phase_angle.shape[0]
    slots = box_dev // groups
    dir_rank = lax.axis_index("dir")
    box_rank = lax.axis_index("box")
    child_first = dir_rank * child_dev
    parent_first = dir_rank * parent_dev
    cosine = jnp.cos(phase_angle)
    sine = jnp.sin(phase_angle)
    rows = interp_matrix(interp_index, interp_weight, child_first, child_dev)

    child_reach = child_coef.shape[1] // 2

    parent_reach = parent_coef.shape[1] // 2
    own_real = lax.dynamic_slice_in_dim(parent_coef[0], parent_first, parent_dev, 1)
    own_imag = lax.dynamic_slice_in_dim(parent_coef[1], parent_first, parent_dev, 1)
    own_mask = lax.dynamic_slice_in_dim(parent_mask, box_rank * slots, slots, 1)
    rhs = comps // 2
    step = rhs // 2

    def chunk_xt(chunk):
        part = pattern.reshape(child_dev, 2, rhs, box_dev)[:, :, chunk * step : (chunk + 1) * step]
        xt = part.reshape(child_dev, 2 * step, slots, groups).transpose(3, 1, 2, 0)
        return xt.reshape(groups, 2 * step * slots, child_dev)

    def translate(field):
        padded = with_halo(field, (("box", 1),), parent_reach)
        return parent_translate(padded, own_real, own_imag, own_mask, parent_reach)

    acc_a = reduce_cores(upward(chunk_xt(0), rows, cosine, sine, dir_size, 2 * step))
    acc_a, xt_b = lax.optimization_barrier((acc_a, chunk_xt(1)))
    keep_a, send_a = split_rows(acc_a)
    recv_a = lax.ppermute(send_a, "dir", ROW_SWAP)
    field_b = upward(xt_b, rows, cosine, sine, dir_size, 2 * step)
    field_b, recv_a = lax.optimization_barrier((field_b, recv_a))
    sum_a = keep_a + recv_a
    acc_b = reduce_cores(field_b)
    sum_a, acc_b = lax.optimization_barrier((sum_a, acc_b))
    keep_b, send_b = split_rows(acc_b)
    recv_b = lax.ppermute(send_b, "dir", ROW_SWAP)
    box_size = lax.axis_size("box")
    forward = [(i, i + 1) for i in range(box_size - 1)]
    backward = [(i + 1, i) for i in range(box_size - 1)]
    pieces_up = (pattern[:, :, box_dev - child_reach :], sum_a[:, slots - parent_reach :])
    pieces_down = (pattern[:, :, :child_reach], sum_a[:, :parent_reach])
    got_up = unpack(lax.ppermute(pack(pieces_up), "box", forward), pieces_up)
    got_down = unpack(lax.ppermute(pack(pieces_down), "box", backward), pieces_down)
    child_padded = jnp.concatenate([got_up[0], pattern, got_down[0]], axis=2)
    child_local = translate_padded(
        child_padded, child_coef[0], child_coef[1], child_mask, child_reach
    )
    padded_a = jnp.concatenate([got_up[1], sum_a, got_down[1]], axis=1)
    local_a = parent_translate(padded_a, own_real, own_imag, own_mask, parent_reach)
    local_a, recv_b = lax.optimization_barrier((local_a, recv_b))
    sum_b = keep_b + recv_b
    other_a = lax.ppermute(local_a, "dir", ROW_SWAP)
    local_b = translate(sum_b)
    other_a, local_b = lax.optimization_barrier((other_a, local_b))
    all_a = gather_cores(local_a, other_a)
    all_a, local_b = lax.optimization_barrier((all_a, local_b))
    other_b = lax.ppermute(local_b, "dir", ROW_SWAP)
    far_a = downward(all_a, rows, cosine, sine)
    far_a, other_b = lax.optimization_barrier((far_a, other_b))
    far_b = downward(gather_cores(local_b, other_b), rows, cosine, sine)
    fars = [far.reshape(groups, child_dev, 2, step, slots) for far in (far_a, far_b)]
    far = jnp.concatenate(fars, axis=3).transpose(1, 2, 3, 4, 0)
    far = far.reshape(child_dev, comps, box_dev)
    return child_local + far


def solution(mesh):
    placed = (P("dir", None, "box"), P(None, None, "dir"), P(None, "box"), P(), P(), P(), P(), P())
    return jax.shard_map(
        body, mesh=mesh, in_specs=placed, out_specs=P("dir", None, "box"), check_vma=False
    )
```

```python
import jax
import jax.numpy as jnp
from jax import lax
from jax.experimental import pallas as pl
from jax.experimental.pallas import tpu as pltpu
from jax.sharding import PartitionSpec as P

HIGHEST = lax.Precision.HIGH


def with_halo(block, sides, width):
    for axis, dim in sides:
        count = lax.axis_size(axis)
        forward = [(i, i + 1) for i in range(count - 1)]
        backward = [(target, source) for source, target in forward]
        low = lax.ppermute(
            lax.slice_in_dim(block, block.shape[dim] - width, None, axis=dim), axis, forward
        )
        high = lax.ppermute(lax.slice_in_dim(block, 0, width, axis=dim), axis, backward)
        block = jnp.concatenate([low, block, high], axis=dim)
    return block


CORE_SWAP = [(0, 1), (1, 0), (2, 3), (3, 2)]
ROW_SWAP = [(0, 2), (2, 0), (1, 3), (3, 1)]


def reduce_cores(field):
    core = lax.axis_index("dir") % 2
    pairs = field.reshape((2, 2) + field.shape[1:])
    keep = lax.dynamic_index_in_dim(pairs, core, 1, keepdims=False)
    send = lax.dynamic_index_in_dim(pairs, 1 - core, 1, keepdims=False)
    return keep + lax.ppermute(send, "dir", CORE_SWAP)


def split_rows(acc):
    row = lax.axis_index("dir") // 2
    keep = lax.dynamic_index_in_dim(acc, row, 0, keepdims=False)
    send = lax.dynamic_index_in_dim(acc, 1 - row, 0, keepdims=False)
    return keep, send


def gather_cores(local, other):
    rank = lax.axis_index("dir")
    first = rank // 2 == 0
    pair = jnp.stack([jnp.where(first, local, other), jnp.where(first, other, local)], axis=0)
    mate = lax.ppermute(pair, "dir", CORE_SWAP)
    low = rank % 2 == 0
    quad = jnp.stack([jnp.where(low, pair, mate), jnp.where(low, mate, pair)], axis=1)
    return quad.reshape((4,) + local.shape)


def interp_matrix(index, weight, first_row, row_count):
    rows = first_row + lax.iota(jnp.int32, row_count)
    matrix = jnp.zeros((row_count, index.shape[1]), jnp.float32)
    for point in range(index.shape[0]):
        matrix = matrix + jnp.where(
            rows[:, None] == index[point][None, :], weight[point][None, :], jnp.float32(0.0)
        )
    return matrix


def translate_padded(padded, coef_real, coef_imag, mask, reach):
    count = padded.shape[2] - 2 * reach
    half = padded.shape[1] // 2
    offsets = list(range(-reach, 0)) + list(range(1, reach + 1))
    summed = jnp.zeros((padded.shape[0], padded.shape[1], count), jnp.float32)
    for position, offset in enumerate(offsets):
        source = padded[:, :, reach + offset : reach + offset + count]
        real_part = source[:, :half]
        imag_part = source[:, half:]
        scale_real = coef_real[position][:, None, None]
        scale_imag = coef_imag[position][:, None, None]
        weight = mask[position].astype(jnp.float32)[None, None, :]
        turned = jnp.concatenate(
            [
                scale_real * real_part - scale_imag * imag_part,
                scale_real * imag_part + scale_imag * real_part,
            ],
            axis=1,
        )
        summed = summed + weight * turned
    return summed


def upward_kernel(xt_ref, m_ref, cos_ref, sin_ref, out_ref):
    groups = xt_ref.shape[0]
    comps, slots, width = out_ref.shape[1:]
    half = comps // 2
    m = m_ref[...]
    acc_re = jnp.zeros((half, slots, width), jnp.float32)
    acc_im = jnp.zeros((half, slots, width), jnp.float32)
    for g in range(groups):
        r = jnp.dot(xt_ref[g], m, precision=HIGHEST, preferred_element_type=jnp.float32)
        r = r.reshape(comps, slots, width)
        c = cos_ref[pl.ds(g, 1), :].reshape(1, 1, width)
        s = sin_ref[pl.ds(g, 1), :].reshape(1, 1, width)
        re = r[:half]
        im = r[half:]
        acc_re = acc_re + (c * re - s * im)
        acc_im = acc_im + (c * im + s * re)
    out_ref[0, :half] = acc_re
    out_ref[0, half:] = acc_im


def upward(xt, m, cos, sin, parts, comps):
    groups, rows, q = xt.shape
    total = m.shape[1]
    width = total // parts
    slots = rows // comps
    return pl.pallas_call(
        upward_kernel,
        grid=(parts,),
        in_specs=[
            pl.BlockSpec((groups, rows, q), lambda j: (0, 0, 0)),
            pl.BlockSpec((q, width), lambda j: (0, j)),
            pl.BlockSpec((groups, width), lambda j: (0, j)),
            pl.BlockSpec((groups, width), lambda j: (0, j)),
        ],
        out_specs=pl.BlockSpec((1, comps, slots, width), lambda j: (j, 0, 0, 0)),
        out_shape=jax.ShapeDtypeStruct((parts, comps, slots, width), jnp.float32),
    )(xt, m, cos, sin)


def downward_kernel(pl_ref, m_ref, cos_ref, sin_ref, out_ref):
    g = pl.program_id(0)
    parts, comps, slots, width = pl_ref.shape
    half = comps // 2
    q = m_ref.shape[0]
    acc = jnp.zeros((q, comps * slots), jnp.float32)
    for d in range(parts):
        x = pl_ref[d]
        c = cos_ref[pl.ds(g, 1), pl.ds(d * width, width)].reshape(1, 1, width)
        s = sin_ref[pl.ds(g, 1), pl.ds(d * width, width)].reshape(1, 1, width)
        re = x[:half]
        im = x[half:]
        spread = jnp.concatenate([c * re + s * im, c * im - s * re], axis=0)
        spread = spread.reshape(comps * slots, width)
        acc = acc + lax.dot_general(
            m_ref[:, pl.ds(d * width, width)],
            spread,
            (((1,), (1,)), ((), ())),
            precision=HIGHEST,
            preferred_element_type=jnp.float32,
        )
    out_ref[0] = acc


def downward(parent_local, m, cos, sin):
    parts, comps, slots, width = parent_local.shape
    groups = cos.shape[0]
    q = m.shape[0]
    return pl.pallas_call(
        downward_kernel,
        grid=(groups,),
        in_specs=[
            pl.BlockSpec((parts, comps, slots, width), lambda g: (0, 0, 0, 0)),
            pl.BlockSpec((q, parts * width), lambda g: (0, 0)),
            pl.BlockSpec((groups, parts * width), lambda g: (0, 0)),
            pl.BlockSpec((groups, parts * width), lambda g: (0, 0)),
        ],
        out_specs=pl.BlockSpec((1, q, comps * slots), lambda g: (g, 0, 0)),
        out_shape=jax.ShapeDtypeStruct((groups, q, comps * slots), jnp.float32),
    )(parent_local, m, cos, sin)


def parent_translate(padded, coef_real, coef_imag, mask, reach):
    comps = padded.shape[0]
    half = comps // 2
    count = padded.shape[1] - 2 * reach
    offsets = list(range(-reach, 0)) + list(range(1, reach + 1))
    re_sum = jnp.zeros((half, count, padded.shape[2]), jnp.float32)
    im_sum = jnp.zeros((half, count, padded.shape[2]), jnp.float32)
    for position, offset in enumerate(offsets):
        source = padded[:, reach + offset : reach + offset + count]
        re = source[:half]
        im = source[half:]
        cr = coef_real[position][None, None, :]
        ci = coef_imag[position][None, None, :]
        weight = mask[position].astype(jnp.float32)[None, :, None]
        re_sum = re_sum + weight * (cr * re - ci * im)
        im_sum = im_sum + weight * (cr * im + ci * re)
    return jnp.concatenate([re_sum, im_sum], axis=0)


def translate_kernel(low_ref, keep_ref, recv_ref, high_ref, cr_ref, ci_ref, mask_ref, out_ref, pad_ref):
    comps, slots, width = keep_ref.shape
    reach = low_ref.shape[1]
    half = comps // 2
    pad_ref[:, :reach] = low_ref[...]
    pad_ref[:, reach : reach + slots] = keep_ref[...] + recv_ref[...]
    pad_ref[:, reach + slots :] = high_ref[...]
    offsets = list(range(-reach, 0)) + list(range(1, reach + 1))

    def lane_block(lb, carry):
        lanes = pl.ds(pl.multiple_of(lb * 128, 128), 128)
        for h in range(half):
            acc_re = jnp.zeros((slots, 128), jnp.float32)
            acc_im = jnp.zeros((slots, 128), jnp.float32)
            for k, t in enumerate(offsets):
                m = mask_ref[k]
                a = m * cr_ref[pl.ds(k, 1), lanes]
                b = m * ci_ref[pl.ds(k, 1), lanes]
                xr = pad_ref[h, pl.ds(reach + t, slots), lanes]
                xi = pad_ref[h + half, pl.ds(reach + t, slots), lanes]
                acc_re = acc_re + (a * xr - b * xi)
                acc_im = acc_im + (a * xi + b * xr)
            out_ref[h, :, lanes] = acc_re
            out_ref[h + half, :, lanes] = acc_im
        return carry

    lax.fori_loop(0, width // 128, lane_block, 0)


def translate_call(low, keep, recv, high, cr, ci, mask_b):
    comps, slots, width = keep.shape
    reach = low.shape[1]
    return pl.pallas_call(
        translate_kernel,
        out_shape=jax.ShapeDtypeStruct(keep.shape, jnp.float32),
        scratch_shapes=[pltpu.VMEM((comps, slots + 2 * reach, width), jnp.float32)],
    )(low, keep, recv, high, cr, ci, mask_b)


def body(
    pattern,
    child_coef,
    child_mask,
    interp_index,
    interp_weight,
    phase_angle,
    parent_coef,
    parent_mask,
):
    child_dev, comps, box_dev = pattern.shape
    dir_size = lax.axis_size("dir")
    parent_dirs = interp_index.shape[1]
    parent_dev = parent_dirs // dir_size
    groups = phase_angle.shape[0]
    slots = box_dev // groups
    dir_rank = lax.axis_index("dir")
    box_rank = lax.axis_index("box")
    child_first = dir_rank * child_dev
    parent_first = dir_rank * parent_dev
    cosine = jnp.cos(phase_angle)
    sine = jnp.sin(phase_angle)
    rows = interp_matrix(interp_index, interp_weight, child_first, child_dev)

    child_reach = child_coef.shape[1] // 2
    child_padded = with_halo(pattern, (("box", 2),), child_reach)
    child_local = translate_padded(
        child_padded, child_coef[0], child_coef[1], child_mask, child_reach
    )

    parent_reach = parent_coef.shape[1] // 2
    own_real = lax.dynamic_slice_in_dim(parent_coef[0], parent_first, parent_dev, 1)
    own_imag = lax.dynamic_slice_in_dim(parent_coef[1], parent_first, parent_dev, 1)
    own_mask = lax.dynamic_slice_in_dim(parent_mask, box_rank * slots, slots, 1)
    rhs = comps // 2
    step = rhs // 2

    def chunk_xt(chunk):
        part = pattern.reshape(child_dev, 2, rhs, box_dev)[:, :, chunk * step : (chunk + 1) * step]
        xt = part.reshape(child_dev, 2 * step, slots, groups).transpose(3, 1, 2, 0)
        return xt.reshape(groups, 2 * step * slots, child_dev)

    box_size = lax.axis_size("box")
    forward = [(i, i + 1) for i in range(box_size - 1)]
    backward = [(i + 1, i) for i in range(box_size - 1)]
    mask_lanes = jnp.broadcast_to(
        own_mask.astype(jnp.float32)[:, :, None], own_mask.shape + (128,)
    )

    def translate(keep, recv):
        low = keep[:, slots - parent_reach :] + recv[:, slots - parent_reach :]
        high = keep[:, :parent_reach] + recv[:, :parent_reach]
        low = lax.ppermute(low, "box", forward)
        high = lax.ppermute(high, "box", backward)
        return translate_call(low, keep, recv, high, own_real, own_imag, mask_lanes)

    acc_a = reduce_cores(upward(chunk_xt(0), rows, cosine, sine, dir_size, 2 * step))
    acc_a, xt_b = lax.optimization_barrier((acc_a, chunk_xt(1)))
    keep_a, send_a = split_rows(acc_a)
    recv_a = lax.ppermute(send_a, "dir", ROW_SWAP)
    field_b = upward(xt_b, rows, cosine, sine, dir_size, 2 * step)
    field_b, recv_a = lax.optimization_barrier((field_b, recv_a))
    acc_b = reduce_cores(field_b)
    keep_a, recv_a, acc_b = lax.optimization_barrier((keep_a, recv_a, acc_b))
    keep_b, send_b = split_rows(acc_b)
    recv_b = lax.ppermute(send_b, "dir", ROW_SWAP)
    local_a = translate(keep_a, recv_a)
    local_a, recv_b = lax.optimization_barrier((local_a, recv_b))
    other_a = lax.ppermute(local_a, "dir", ROW_SWAP)
    local_b = translate(keep_b, recv_b)
    other_a, local_b = lax.optimization_barrier((other_a, local_b))
    all_a = gather_cores(local_a, other_a)
    all_a, local_b = lax.optimization_barrier((all_a, local_b))
    other_b = lax.ppermute(local_b, "dir", ROW_SWAP)
    far_a = downward(all_a, rows, cosine, sine)
    far_a, other_b = lax.optimization_barrier((far_a, other_b))
    far_b = downward(gather_cores(local_b, other_b), rows, cosine, sine)
    fars = [far.reshape(groups, child_dev, 2, step, slots) for far in (far_a, far_b)]
    far = jnp.concatenate(fars, axis=3).transpose(1, 2, 3, 4, 0)
    far = far.reshape(child_dev, comps, box_dev)
    return child_local + far


def solution(mesh):
    placed = (P("dir", None, "box"), P(None, None, "dir"), P(None, "box"), P(), P(), P(), P(), P())
    return jax.shard_map(
        body, mesh=mesh, in_specs=placed, out_specs=P("dir", None, "box"), check_vma=False
    )
```

```python
import jax
import jax.numpy as jnp
from jax import lax
from jax.experimental import pallas as pl
from jax.experimental.pallas import tpu as pltpu
from jax.sharding import PartitionSpec as P

HIGHEST = lax.Precision.HIGH


def with_halo(block, sides, width):
    for axis, dim in sides:
        count = lax.axis_size(axis)
        forward = [(i, i + 1) for i in range(count - 1)]
        backward = [(target, source) for source, target in forward]
        low = lax.ppermute(
            lax.slice_in_dim(block, block.shape[dim] - width, None, axis=dim), axis, forward
        )
        high = lax.ppermute(lax.slice_in_dim(block, 0, width, axis=dim), axis, backward)
        block = jnp.concatenate([low, block, high], axis=dim)
    return block


CORE_SWAP = [(0, 1), (1, 0), (2, 3), (3, 2)]
ROW_SWAP = [(0, 2), (2, 0), (1, 3), (3, 1)]


def reduce_cores(field):
    core = lax.axis_index("dir") % 2
    pairs = field.reshape((2, 2) + field.shape[1:])
    keep = lax.dynamic_index_in_dim(pairs, core, 1, keepdims=False)
    send = lax.dynamic_index_in_dim(pairs, 1 - core, 1, keepdims=False)
    return keep + lax.ppermute(send, "dir", CORE_SWAP)


def split_rows(acc):
    row = lax.axis_index("dir") // 2
    keep = lax.dynamic_index_in_dim(acc, row, 0, keepdims=False)
    send = lax.dynamic_index_in_dim(acc, 1 - row, 0, keepdims=False)
    return keep, send


def gather_cores(local, other):
    rank = lax.axis_index("dir")
    first = rank // 2 == 0
    pair = jnp.stack([jnp.where(first, local, other), jnp.where(first, other, local)], axis=0)
    mate = lax.ppermute(pair, "dir", CORE_SWAP)
    low = rank % 2 == 0
    quad = jnp.stack([jnp.where(low, pair, mate), jnp.where(low, mate, pair)], axis=1)
    return quad.reshape((4,) + local.shape)


def interp_matrix(index, weight, first_row, row_count):
    rows = first_row + lax.iota(jnp.int32, row_count)
    matrix = jnp.zeros((row_count, index.shape[1]), jnp.float32)
    for point in range(index.shape[0]):
        matrix = matrix + jnp.where(
            rows[:, None] == index[point][None, :], weight[point][None, :], jnp.float32(0.0)
        )
    return matrix


def translate_padded(padded, coef_real, coef_imag, mask, reach):
    count = padded.shape[2] - 2 * reach
    half = padded.shape[1] // 2
    offsets = list(range(-reach, 0)) + list(range(1, reach + 1))
    summed = jnp.zeros((padded.shape[0], padded.shape[1], count), jnp.float32)
    for position, offset in enumerate(offsets):
        source = padded[:, :, reach + offset : reach + offset + count]
        real_part = source[:, :half]
        imag_part = source[:, half:]
        scale_real = coef_real[position][:, None, None]
        scale_imag = coef_imag[position][:, None, None]
        weight = mask[position].astype(jnp.float32)[None, None, :]
        turned = jnp.concatenate(
            [
                scale_real * real_part - scale_imag * imag_part,
                scale_real * imag_part + scale_imag * real_part,
            ],
            axis=1,
        )
        summed = summed + weight * turned
    return summed


def upward_kernel(xt_ref, m_ref, cos_ref, sin_ref, out_ref):
    groups = xt_ref.shape[0]
    comps, slots, width = out_ref.shape[1:]
    half = comps // 2
    m = m_ref[...]
    acc_re = jnp.zeros((half, slots, width), jnp.float32)
    acc_im = jnp.zeros((half, slots, width), jnp.float32)
    for g in range(groups):
        r = jnp.dot(xt_ref[g], m, precision=HIGHEST, preferred_element_type=jnp.float32)
        r = r.reshape(comps, slots, width)
        c = cos_ref[pl.ds(g, 1), :].reshape(1, 1, width)
        s = sin_ref[pl.ds(g, 1), :].reshape(1, 1, width)
        re = r[:half]
        im = r[half:]
        acc_re = acc_re + (c * re - s * im)
        acc_im = acc_im + (c * im + s * re)
    out_ref[0, :half] = acc_re
    out_ref[0, half:] = acc_im


def upward(xt, m, cos, sin, parts, comps):
    groups, rows, q = xt.shape
    total = m.shape[1]
    width = total // parts
    slots = rows // comps
    return pl.pallas_call(
        upward_kernel,
        grid=(parts,),
        in_specs=[
            pl.BlockSpec((groups, rows, q), lambda j: (0, 0, 0)),
            pl.BlockSpec((q, width), lambda j: (0, j)),
            pl.BlockSpec((groups, width), lambda j: (0, j)),
            pl.BlockSpec((groups, width), lambda j: (0, j)),
        ],
        out_specs=pl.BlockSpec((1, comps, slots, width), lambda j: (j, 0, 0, 0)),
        out_shape=jax.ShapeDtypeStruct((parts, comps, slots, width), jnp.float32),
    )(xt, m, cos, sin)


def downward_kernel(pl_ref, m_ref, cos_ref, sin_ref, out_ref):
    g = pl.program_id(0)
    parts, comps, slots, width = pl_ref.shape
    half = comps // 2
    q = m_ref.shape[0]
    acc = jnp.zeros((q, comps * slots), jnp.float32)
    for d in range(parts):
        x = pl_ref[d]
        c = cos_ref[pl.ds(g, 1), pl.ds(d * width, width)].reshape(1, 1, width)
        s = sin_ref[pl.ds(g, 1), pl.ds(d * width, width)].reshape(1, 1, width)
        re = x[:half]
        im = x[half:]
        spread = jnp.concatenate([c * re + s * im, c * im - s * re], axis=0)
        spread = spread.reshape(comps * slots, width)
        acc = acc + lax.dot_general(
            m_ref[:, pl.ds(d * width, width)],
            spread,
            (((1,), (1,)), ((), ())),
            precision=HIGHEST,
            preferred_element_type=jnp.float32,
        )
    out_ref[0] = acc


def downward(parent_local, m, cos, sin):
    parts, comps, slots, width = parent_local.shape
    groups = cos.shape[0]
    q = m.shape[0]
    return pl.pallas_call(
        downward_kernel,
        grid=(groups,),
        in_specs=[
            pl.BlockSpec((parts, comps, slots, width), lambda g: (0, 0, 0, 0)),
            pl.BlockSpec((q, parts * width), lambda g: (0, 0)),
            pl.BlockSpec((groups, parts * width), lambda g: (0, 0)),
            pl.BlockSpec((groups, parts * width), lambda g: (0, 0)),
        ],
        out_specs=pl.BlockSpec((1, q, comps * slots), lambda g: (g, 0, 0)),
        out_shape=jax.ShapeDtypeStruct((groups, q, comps * slots), jnp.float32),
    )(parent_local, m, cos, sin)


def parent_translate(padded, coef_real, coef_imag, mask, reach):
    comps = padded.shape[0]
    half = comps // 2
    count = padded.shape[1] - 2 * reach
    offsets = list(range(-reach, 0)) + list(range(1, reach + 1))
    re_sum = jnp.zeros((half, count, padded.shape[2]), jnp.float32)
    im_sum = jnp.zeros((half, count, padded.shape[2]), jnp.float32)
    for position, offset in enumerate(offsets):
        source = padded[:, reach + offset : reach + offset + count]
        re = source[:half]
        im = source[half:]
        cr = coef_real[position][None, None, :]
        ci = coef_imag[position][None, None, :]
        weight = mask[position].astype(jnp.float32)[None, :, None]
        re_sum = re_sum + weight * (cr * re - ci * im)
        im_sum = im_sum + weight * (cr * im + ci * re)
    return jnp.concatenate([re_sum, im_sum], axis=0)


def translate_kernel(low_ref, keep_ref, recv_ref, high_ref, cr_ref, ci_ref, mask_ref, out_ref, pad_ref):
    comps, slots, width = keep_ref.shape
    reach = low_ref.shape[1]
    half = comps // 2
    pad_ref[:, :reach] = low_ref[...]
    pad_ref[:, reach : reach + slots] = keep_ref[...] + recv_ref[...]
    pad_ref[:, reach + slots :] = high_ref[...]
    offsets = list(range(-reach, 0)) + list(range(1, reach + 1))

    def lane_block(lb, carry):
        lanes = pl.ds(pl.multiple_of(lb * 128, 128), 128)
        for h in range(half):
            acc_re = jnp.zeros((slots, 128), jnp.float32)
            acc_im = jnp.zeros((slots, 128), jnp.float32)
            for k, t in enumerate(offsets):
                m = mask_ref[k]
                a = m * cr_ref[pl.ds(k, 1), lanes]
                b = m * ci_ref[pl.ds(k, 1), lanes]
                xr = pad_ref[h, pl.ds(reach + t, slots), lanes]
                xi = pad_ref[h + half, pl.ds(reach + t, slots), lanes]
                acc_re = acc_re + (a * xr - b * xi)
                acc_im = acc_im + (a * xi + b * xr)
            out_ref[h, :, lanes] = acc_re
            out_ref[h + half, :, lanes] = acc_im
        return carry

    lax.fori_loop(0, width // 128, lane_block, 0)


def translate_call(low, keep, recv, high, cr, ci, mask_b):
    comps, slots, width = keep.shape
    reach = low.shape[1]
    return pl.pallas_call(
        translate_kernel,
        out_shape=jax.ShapeDtypeStruct(keep.shape, jnp.float32),
        scratch_shapes=[pltpu.VMEM((comps, slots + 2 * reach, width), jnp.float32)],
    )(low, keep, recv, high, cr, ci, mask_b)


def body(
    pattern,
    child_coef,
    child_mask,
    interp_index,
    interp_weight,
    phase_angle,
    parent_coef,
    parent_mask,
):
    child_dev, comps, box_dev = pattern.shape
    dir_size = lax.axis_size("dir")
    parent_dirs = interp_index.shape[1]
    parent_dev = parent_dirs // dir_size
    groups = phase_angle.shape[0]
    slots = box_dev // groups
    dir_rank = lax.axis_index("dir")
    box_rank = lax.axis_index("box")
    child_first = dir_rank * child_dev
    parent_first = dir_rank * parent_dev
    cosine = jnp.cos(phase_angle)
    sine = jnp.sin(phase_angle)
    rows = interp_matrix(interp_index, interp_weight, child_first, child_dev)

    child_reach = child_coef.shape[1] // 2
    box_count = lax.axis_size("box")
    edge_up = [(i, i + 1) for i in range(box_count - 1)]
    edge_down = [(i + 1, i) for i in range(box_count - 1)]

    def edge_send(piece, pairs):
        flat = piece.transpose(2, 0, 1).reshape(piece.shape[2], -1)
        got = lax.ppermute(flat, "box", pairs)
        return got.reshape(piece.shape[2], child_dev, comps).transpose(1, 2, 0)

    child_padded = jnp.concatenate(
        [
            edge_send(pattern[:, :, box_dev - child_reach :], edge_up),
            pattern,
            edge_send(pattern[:, :, :child_reach], edge_down),
        ],
        axis=2,
    )
    child_local = translate_padded(
        child_padded, child_coef[0], child_coef[1], child_mask, child_reach
    )

    parent_reach = parent_coef.shape[1] // 2
    own_real = lax.dynamic_slice_in_dim(parent_coef[0], parent_first, parent_dev, 1)
    own_imag = lax.dynamic_slice_in_dim(parent_coef[1], parent_first, parent_dev, 1)
    own_mask = lax.dynamic_slice_in_dim(parent_mask, box_rank * slots, slots, 1)
    rhs = comps // 2
    step = rhs // 2

    def chunk_xt(chunk):
        part = pattern.reshape(child_dev, 2, rhs, box_dev)[:, :, chunk * step : (chunk + 1) * step]
        xt = part.reshape(child_dev, 2 * step, slots, groups).transpose(3, 1, 2, 0)
        return xt.reshape(groups, 2 * step * slots, child_dev)

    box_size = lax.axis_size("box")
    forward = [(i, i + 1) for i in range(box_size - 1)]
    backward = [(i + 1, i) for i in range(box_size - 1)]
    mask_lanes = jnp.broadcast_to(
        own_mask.astype(jnp.float32)[:, :, None], own_mask.shape + (128,)
    )

    def translate(keep, recv):
        low = keep[:, slots - parent_reach :] + recv[:, slots - parent_reach :]
        high = keep[:, :parent_reach] + recv[:, :parent_reach]
        low = lax.ppermute(low, "box", forward)
        high = lax.ppermute(high, "box", backward)
        return translate_call(low, keep, recv, high, own_real, own_imag, mask_lanes)

    acc_a = reduce_cores(upward(chunk_xt(0), rows, cosine, sine, dir_size, 2 * step))
    acc_a, xt_b = lax.optimization_barrier((acc_a, chunk_xt(1)))
    keep_a, send_a = split_rows(acc_a)
    recv_a = lax.ppermute(send_a, "dir", ROW_SWAP)
    field_b = upward(xt_b, rows, cosine, sine, dir_size, 2 * step)
    field_b, recv_a = lax.optimization_barrier((field_b, recv_a))
    acc_b = reduce_cores(field_b)
    keep_a, recv_a, acc_b = lax.optimization_barrier((keep_a, recv_a, acc_b))
    keep_b, send_b = split_rows(acc_b)
    recv_b = lax.ppermute(send_b, "dir", ROW_SWAP)
    local_a = translate(keep_a, recv_a)
    local_a, recv_b = lax.optimization_barrier((local_a, recv_b))
    other_a = lax.ppermute(local_a, "dir", ROW_SWAP)
    local_b = translate(keep_b, recv_b)
    other_a, local_b = lax.optimization_barrier((other_a, local_b))
    all_a = gather_cores(local_a, other_a)
    all_a, local_b = lax.optimization_barrier((all_a, local_b))
    other_b = lax.ppermute(local_b, "dir", ROW_SWAP)
    far_a = downward(all_a, rows, cosine, sine)
    far_a, other_b = lax.optimization_barrier((far_a, other_b))
    far_b = downward(gather_cores(local_b, other_b), rows, cosine, sine)
    fars = [far.reshape(groups, child_dev, 2, step, slots) for far in (far_a, far_b)]
    far = jnp.concatenate(fars, axis=3).transpose(1, 2, 3, 4, 0)
    far = far.reshape(child_dev, comps, box_dev)
    return child_local + far


def solution(mesh):
    placed = (P("dir", None, "box"), P(None, None, "dir"), P(None, "box"), P(), P(), P(), P(), P())
    return jax.shard_map(
        body, mesh=mesh, in_specs=placed, out_specs=P("dir", None, "box"), check_vma=False
    )
```

```python
import jax
import jax.numpy as jnp
from jax import lax
from jax.experimental import pallas as pl
from jax.experimental.pallas import tpu as pltpu
from jax.sharding import PartitionSpec as P

HIGHEST = lax.Precision.HIGH


def with_halo(block, sides, width):
    for axis, dim in sides:
        count = lax.axis_size(axis)
        forward = [(i, i + 1) for i in range(count - 1)]
        backward = [(target, source) for source, target in forward]
        low = lax.ppermute(
            lax.slice_in_dim(block, block.shape[dim] - width, None, axis=dim), axis, forward
        )
        high = lax.ppermute(lax.slice_in_dim(block, 0, width, axis=dim), axis, backward)
        block = jnp.concatenate([low, block, high], axis=dim)
    return block


CORE_SWAP = [(0, 1), (1, 0), (2, 3), (3, 2)]
ROW_SWAP = [(0, 2), (2, 0), (1, 3), (3, 1)]


def reduce_cores(field):
    core = lax.axis_index("dir") % 2
    pairs = field.reshape((2, 2) + field.shape[1:])
    keep = lax.dynamic_index_in_dim(pairs, core, 1, keepdims=False)
    send = lax.dynamic_index_in_dim(pairs, 1 - core, 1, keepdims=False)
    return keep + lax.ppermute(send, "dir", CORE_SWAP)


def split_rows(acc):
    row = lax.axis_index("dir") // 2
    keep = lax.dynamic_index_in_dim(acc, row, 0, keepdims=False)
    send = lax.dynamic_index_in_dim(acc, 1 - row, 0, keepdims=False)
    return keep, send


def gather_cores(local, other):
    rank = lax.axis_index("dir")
    first = rank // 2 == 0
    pair = jnp.stack([jnp.where(first, local, other), jnp.where(first, other, local)], axis=0)
    mate = lax.ppermute(pair, "dir", CORE_SWAP)
    low = rank % 2 == 0
    quad = jnp.stack([jnp.where(low, pair, mate), jnp.where(low, mate, pair)], axis=1)
    return quad.reshape((4,) + local.shape)


def interp_matrix(index, weight, first_row, row_count):
    rows = first_row + lax.iota(jnp.int32, row_count)
    matrix = jnp.zeros((row_count, index.shape[1]), jnp.float32)
    for point in range(index.shape[0]):
        matrix = matrix + jnp.where(
            rows[:, None] == index[point][None, :], weight[point][None, :], jnp.float32(0.0)
        )
    return matrix


def translate_padded(padded, coef_real, coef_imag, mask, reach):
    count = padded.shape[2] - 2 * reach
    half = padded.shape[1] // 2
    offsets = list(range(-reach, 0)) + list(range(1, reach + 1))
    summed = jnp.zeros((padded.shape[0], padded.shape[1], count), jnp.float32)
    for position, offset in enumerate(offsets):
        source = padded[:, :, reach + offset : reach + offset + count]
        real_part = source[:, :half]
        imag_part = source[:, half:]
        scale_real = coef_real[position][:, None, None]
        scale_imag = coef_imag[position][:, None, None]
        weight = mask[position].astype(jnp.float32)[None, None, :]
        turned = jnp.concatenate(
            [
                scale_real * real_part - scale_imag * imag_part,
                scale_real * imag_part + scale_imag * real_part,
            ],
            axis=1,
        )
        summed = summed + weight * turned
    return summed


def upward_kernel(xt_ref, m_ref, cos_ref, sin_ref, out_ref):
    groups = xt_ref.shape[0]
    comps, slots, width = out_ref.shape[1:]
    half = comps // 2
    m = m_ref[...]
    acc_re = jnp.zeros((half, slots, width), jnp.float32)
    acc_im = jnp.zeros((half, slots, width), jnp.float32)
    for g in range(groups):
        r = jnp.dot(xt_ref[g], m, precision=HIGHEST, preferred_element_type=jnp.float32)
        r = r.reshape(comps, slots, width)
        c = cos_ref[pl.ds(g, 1), :].reshape(1, 1, width)
        s = sin_ref[pl.ds(g, 1), :].reshape(1, 1, width)
        re = r[:half]
        im = r[half:]
        acc_re = acc_re + (c * re - s * im)
        acc_im = acc_im + (c * im + s * re)
    out_ref[0, :half] = acc_re
    out_ref[0, half:] = acc_im


def upward(xt, m, cos, sin, parts, comps):
    groups, rows, q = xt.shape
    total = m.shape[1]
    width = total // parts
    slots = rows // comps
    return pl.pallas_call(
        upward_kernel,
        grid=(parts,),
        in_specs=[
            pl.BlockSpec((groups, rows, q), lambda j: (0, 0, 0)),
            pl.BlockSpec((q, width), lambda j: (0, j)),
            pl.BlockSpec((groups, width), lambda j: (0, j)),
            pl.BlockSpec((groups, width), lambda j: (0, j)),
        ],
        out_specs=pl.BlockSpec((1, comps, slots, width), lambda j: (j, 0, 0, 0)),
        out_shape=jax.ShapeDtypeStruct((parts, comps, slots, width), jnp.float32),
    )(xt, m, cos, sin)


def downward_kernel(pl_ref, m_ref, cos_ref, sin_ref, out_ref):
    g = pl.program_id(0)
    parts, comps, slots, width = pl_ref.shape
    half = comps // 2
    q = m_ref.shape[0]
    acc = jnp.zeros((q, comps * slots), jnp.float32)
    for d in range(parts):
        x = pl_ref[d]
        c = cos_ref[pl.ds(g, 1), pl.ds(d * width, width)].reshape(1, 1, width)
        s = sin_ref[pl.ds(g, 1), pl.ds(d * width, width)].reshape(1, 1, width)
        re = x[:half]
        im = x[half:]
        spread = jnp.concatenate([c * re + s * im, c * im - s * re], axis=0)
        spread = spread.reshape(comps * slots, width)
        acc = acc + lax.dot_general(
            m_ref[:, pl.ds(d * width, width)],
            spread,
            (((1,), (1,)), ((), ())),
            precision=HIGHEST,
            preferred_element_type=jnp.float32,
        )
    out_ref[0] = acc


def downward(parent_local, m, cos, sin):
    parts, comps, slots, width = parent_local.shape
    groups = cos.shape[0]
    q = m.shape[0]
    return pl.pallas_call(
        downward_kernel,
        grid=(groups,),
        in_specs=[
            pl.BlockSpec((parts, comps, slots, width), lambda g: (0, 0, 0, 0)),
            pl.BlockSpec((q, parts * width), lambda g: (0, 0)),
            pl.BlockSpec((groups, parts * width), lambda g: (0, 0)),
            pl.BlockSpec((groups, parts * width), lambda g: (0, 0)),
        ],
        out_specs=pl.BlockSpec((1, q, comps * slots), lambda g: (g, 0, 0)),
        out_shape=jax.ShapeDtypeStruct((groups, q, comps * slots), jnp.float32),
    )(parent_local, m, cos, sin)


def parent_translate(padded, coef_real, coef_imag, mask, reach):
    comps = padded.shape[0]
    half = comps // 2
    count = padded.shape[1] - 2 * reach
    offsets = list(range(-reach, 0)) + list(range(1, reach + 1))
    re_sum = jnp.zeros((half, count, padded.shape[2]), jnp.float32)
    im_sum = jnp.zeros((half, count, padded.shape[2]), jnp.float32)
    for position, offset in enumerate(offsets):
        source = padded[:, reach + offset : reach + offset + count]
        re = source[:half]
        im = source[half:]
        cr = coef_real[position][None, None, :]
        ci = coef_imag[position][None, None, :]
        weight = mask[position].astype(jnp.float32)[None, :, None]
        re_sum = re_sum + weight * (cr * re - ci * im)
        im_sum = im_sum + weight * (cr * im + ci * re)
    return jnp.concatenate([re_sum, im_sum], axis=0)


def translate_kernel(low_ref, keep_ref, recv_ref, high_ref, cr_ref, ci_ref, mask_ref, out_ref, pad_ref):
    comps, slots, width = keep_ref.shape
    reach = low_ref.shape[1]
    half = comps // 2
    pad_ref[:, :reach] = low_ref[...]
    pad_ref[:, reach : reach + slots] = keep_ref[...] + recv_ref[...]
    pad_ref[:, reach + slots :] = high_ref[...]
    offsets = list(range(-reach, 0)) + list(range(1, reach + 1))

    def lane_block(lb, carry):
        lanes = pl.ds(pl.multiple_of(lb * 128, 128), 128)
        for h in range(half):
            acc_re = jnp.zeros((slots, 128), jnp.float32)
            acc_im = jnp.zeros((slots, 128), jnp.float32)
            for k, t in enumerate(offsets):
                m = mask_ref[k]
                a = m * cr_ref[pl.ds(k, 1), lanes]
                b = m * ci_ref[pl.ds(k, 1), lanes]
                xr = pad_ref[h, pl.ds(reach + t, slots), lanes]
                xi = pad_ref[h + half, pl.ds(reach + t, slots), lanes]
                acc_re = acc_re + (a * xr - b * xi)
                acc_im = acc_im + (a * xi + b * xr)
            out_ref[h, :, lanes] = acc_re
            out_ref[h + half, :, lanes] = acc_im
        return carry

    lax.fori_loop(0, width // 128, lane_block, 0)


def translate_call(low, keep, recv, high, cr, ci, mask_b):
    comps, slots, width = keep.shape
    reach = low.shape[1]
    return pl.pallas_call(
        translate_kernel,
        out_shape=jax.ShapeDtypeStruct(keep.shape, jnp.float32),
        scratch_shapes=[pltpu.VMEM((comps, slots + 2 * reach, width), jnp.float32)],
    )(low, keep, recv, high, cr, ci, mask_b)


def body(
    pattern,
    child_coef,
    child_mask,
    interp_index,
    interp_weight,
    phase_angle,
    parent_coef,
    parent_mask,
):
    child_dev, comps, box_dev = pattern.shape
    dir_size = lax.axis_size("dir")
    parent_dirs = interp_index.shape[1]
    parent_dev = parent_dirs // dir_size
    groups = phase_angle.shape[0]
    slots = box_dev // groups
    dir_rank = lax.axis_index("dir")
    box_rank = lax.axis_index("box")
    child_first = dir_rank * child_dev
    parent_first = dir_rank * parent_dev
    cosine = jnp.cos(phase_angle)
    sine = jnp.sin(phase_angle)
    rows = interp_matrix(interp_index, interp_weight, child_first, child_dev)

    child_reach = child_coef.shape[1] // 2
    child_padded = with_halo(pattern, (("box", 2),), child_reach)

    parent_reach = parent_coef.shape[1] // 2
    own_real = lax.dynamic_slice_in_dim(parent_coef[0], parent_first, parent_dev, 1)
    own_imag = lax.dynamic_slice_in_dim(parent_coef[1], parent_first, parent_dev, 1)
    own_mask = lax.dynamic_slice_in_dim(parent_mask, box_rank * slots, slots, 1)
    rhs = comps // 2
    step = rhs // 2

    def chunk_xt(chunk):
        part = pattern.reshape(child_dev, 2, rhs, box_dev)[:, :, chunk * step : (chunk + 1) * step]
        xt = part.reshape(child_dev, 2 * step, slots, groups).transpose(3, 1, 2, 0)
        return xt.reshape(groups, 2 * step * slots, child_dev)

    box_size = lax.axis_size("box")
    forward = [(i, i + 1) for i in range(box_size - 1)]
    backward = [(i + 1, i) for i in range(box_size - 1)]
    mask_lanes = jnp.broadcast_to(
        own_mask.astype(jnp.float32)[:, :, None], own_mask.shape + (128,)
    )

    def translate(keep, recv):
        low = keep[:, slots - parent_reach :] + recv[:, slots - parent_reach :]
        high = keep[:, :parent_reach] + recv[:, :parent_reach]
        low = lax.ppermute(low, "box", forward)
        high = lax.ppermute(high, "box", backward)
        return translate_call(low, keep, recv, high, own_real, own_imag, mask_lanes)

    field_a, child_padded = lax.optimization_barrier(
        (upward(chunk_xt(0), rows, cosine, sine, dir_size, 2 * step), child_padded)
    )
    acc_a = reduce_cores(field_a)
    child_local = translate_padded(
        child_padded, child_coef[0], child_coef[1], child_mask, child_reach
    )
    acc_a, xt_b = lax.optimization_barrier((acc_a, chunk_xt(1)))
    keep_a, send_a = split_rows(acc_a)
    recv_a = lax.ppermute(send_a, "dir", ROW_SWAP)
    field_b = upward(xt_b, rows, cosine, sine, dir_size, 2 * step)
    field_b, recv_a = lax.optimization_barrier((field_b, recv_a))
    acc_b = reduce_cores(field_b)
    keep_a, recv_a, acc_b = lax.optimization_barrier((keep_a, recv_a, acc_b))
    keep_b, send_b = split_rows(acc_b)
    recv_b = lax.ppermute(send_b, "dir", ROW_SWAP)
    local_a = translate(keep_a, recv_a)
    local_a, recv_b = lax.optimization_barrier((local_a, recv_b))
    other_a = lax.ppermute(local_a, "dir", ROW_SWAP)
    local_b = translate(keep_b, recv_b)
    other_a, local_b = lax.optimization_barrier((other_a, local_b))
    all_a = gather_cores(local_a, other_a)
    all_a, local_b = lax.optimization_barrier((all_a, local_b))
    other_b = lax.ppermute(local_b, "dir", ROW_SWAP)
    far_a = downward(all_a, rows, cosine, sine)
    far_a, other_b = lax.optimization_barrier((far_a, other_b))
    far_b = downward(gather_cores(local_b, other_b), rows, cosine, sine)
    fars = [far.reshape(groups, child_dev, 2, step, slots) for far in (far_a, far_b)]
    far = jnp.concatenate(fars, axis=3).transpose(1, 2, 3, 4, 0)
    far = far.reshape(child_dev, comps, box_dev)
    return child_local + far


def solution(mesh):
    placed = (P("dir", None, "box"), P(None, None, "dir"), P(None, "box"), P(), P(), P(), P(), P())
    return jax.shard_map(
        body, mesh=mesh, in_specs=placed, out_specs=P("dir", None, "box"), check_vma=False
    )
```

```python
import jax
import jax.numpy as jnp
from jax import lax
from jax.experimental import pallas as pl
from jax.experimental.pallas import tpu as pltpu
from jax.sharding import PartitionSpec as P

HIGHEST = lax.Precision.HIGH


def with_halo(block, sides, width):
    for axis, dim in sides:
        count = lax.axis_size(axis)
        forward = [(i, i + 1) for i in range(count - 1)]
        backward = [(target, source) for source, target in forward]
        low = lax.ppermute(
            lax.slice_in_dim(block, block.shape[dim] - width, None, axis=dim), axis, forward
        )
        high = lax.ppermute(lax.slice_in_dim(block, 0, width, axis=dim), axis, backward)
        block = jnp.concatenate([low, block, high], axis=dim)
    return block


CORE_SWAP = [(0, 1), (1, 0), (2, 3), (3, 2)]
ROW_SWAP = [(0, 2), (2, 0), (1, 3), (3, 1)]


def reduce_cores(field):
    return field[:2] + lax.ppermute(field[2:], "dir", CORE_SWAP)


def gather_blocks(local, other):
    mate_local, mate_other = lax.ppermute((local, other), "dir", CORE_SWAP)
    return (local, other, mate_local, mate_other)


def interp_matrix(index, weight, first_row, row_count):
    rows = first_row + lax.iota(jnp.int32, row_count)
    matrix = jnp.zeros((row_count, index.shape[1]), jnp.float32)
    for point in range(index.shape[0]):
        matrix = matrix + jnp.where(
            rows[:, None] == index[point][None, :], weight[point][None, :], jnp.float32(0.0)
        )
    return matrix


def translate_padded(padded, coef_real, coef_imag, mask, reach):
    count = padded.shape[2] - 2 * reach
    half = padded.shape[1] // 2
    offsets = list(range(-reach, 0)) + list(range(1, reach + 1))
    summed = jnp.zeros((padded.shape[0], padded.shape[1], count), jnp.float32)
    for position, offset in enumerate(offsets):
        source = padded[:, :, reach + offset : reach + offset + count]
        real_part = source[:, :half]
        imag_part = source[:, half:]
        scale_real = coef_real[position][:, None, None]
        scale_imag = coef_imag[position][:, None, None]
        weight = mask[position].astype(jnp.float32)[None, None, :]
        turned = jnp.concatenate(
            [
                scale_real * real_part - scale_imag * imag_part,
                scale_real * imag_part + scale_imag * real_part,
            ],
            axis=1,
        )
        summed = summed + weight * turned
    return summed


def slot_part(slot):
    rank = lax.axis_index("dir")
    return ((rank // 2 + slot % 2) % 2) * 2 + (rank % 2 + slot // 2) % 2


def upward_kernel(xt_ref, m_ref, cos_ref, sin_ref, out_ref):
    groups = xt_ref.shape[0]
    comps, slots, width = out_ref.shape[1:]
    half = comps // 2
    first = pl.multiple_of(slot_part(pl.program_id(0)) * width, 128)
    m = m_ref[:, pl.ds(first, width)]
    acc_re = jnp.zeros((half, slots, width), jnp.float32)
    acc_im = jnp.zeros((half, slots, width), jnp.float32)
    for g in range(groups):
        r = jnp.dot(xt_ref[g], m, precision=HIGHEST, preferred_element_type=jnp.float32)
        r = r.reshape(comps, slots, width)
        c = cos_ref[pl.ds(g, 1), pl.ds(first, width)].reshape(1, 1, width)
        s = sin_ref[pl.ds(g, 1), pl.ds(first, width)].reshape(1, 1, width)
        re = r[:half]
        im = r[half:]
        acc_re = acc_re + (c * re - s * im)
        acc_im = acc_im + (c * im + s * re)
    out_ref[0, :half] = acc_re
    out_ref[0, half:] = acc_im


def upward(xt, m, cos, sin, parts, comps):
    groups, rows, q = xt.shape
    total = m.shape[1]
    width = total // parts
    slots = rows // comps
    return pl.pallas_call(
        upward_kernel,
        grid=(parts,),
        in_specs=[
            pl.BlockSpec((groups, rows, q), lambda j: (0, 0, 0)),
            pl.BlockSpec((q, total), lambda j: (0, 0)),
            pl.BlockSpec((groups, total), lambda j: (0, 0)),
            pl.BlockSpec((groups, total), lambda j: (0, 0)),
        ],
        out_specs=pl.BlockSpec((1, comps, slots, width), lambda j: (j, 0, 0, 0)),
        out_shape=jax.ShapeDtypeStruct((parts, comps, slots, width), jnp.float32),
    )(xt, m, cos, sin)


def downward_kernel(b0_ref, b1_ref, b2_ref, b3_ref, m_ref, cos_ref, sin_ref, out_ref):
    g = pl.program_id(0)
    comps, slots, width = b0_ref.shape
    half = comps // 2
    q = m_ref.shape[0]
    acc = jnp.zeros((q, comps * slots), jnp.float32)
    rank = lax.axis_index("dir")
    for code, ref in zip((0, 2, 1, 3), (b0_ref, b1_ref, b2_ref, b3_ref)):
        part = ((rank // 2 + code // 2) % 2) * 2 + (rank % 2 + code % 2) % 2
        first = pl.multiple_of(part * width, 128)
        x = ref[...]
        c = cos_ref[pl.ds(g, 1), pl.ds(first, width)].reshape(1, 1, width)
        s = sin_ref[pl.ds(g, 1), pl.ds(first, width)].reshape(1, 1, width)
        re = x[:half]
        im = x[half:]
        spread = jnp.concatenate([c * re + s * im, c * im - s * re], axis=0)
        spread = spread.reshape(comps * slots, width)
        acc = acc + lax.dot_general(
            m_ref[:, pl.ds(first, width)],
            spread,
            (((1,), (1,)), ((), ())),
            precision=HIGHEST,
            preferred_element_type=jnp.float32,
        )
    out_ref[0] = acc


def downward(blocks, m, cos, sin):
    comps, slots, width = blocks[0].shape
    groups = cos.shape[0]
    q, total = m.shape
    block = pl.BlockSpec((comps, slots, width), lambda g: (0, 0, 0))
    return pl.pallas_call(
        downward_kernel,
        grid=(groups,),
        in_specs=[block] * 4
        + [
            pl.BlockSpec((q, total), lambda g: (0, 0)),
            pl.BlockSpec((groups, total), lambda g: (0, 0)),
            pl.BlockSpec((groups, total), lambda g: (0, 0)),
        ],
        out_specs=pl.BlockSpec((1, q, comps * slots), lambda g: (g, 0, 0)),
        out_shape=jax.ShapeDtypeStruct((groups, q, comps * slots), jnp.float32),
    )(*blocks, m, cos, sin)


def parent_translate(padded, coef_real, coef_imag, mask, reach):
    comps = padded.shape[0]
    half = comps // 2
    count = padded.shape[1] - 2 * reach
    offsets = list(range(-reach, 0)) + list(range(1, reach + 1))
    re_sum = jnp.zeros((half, count, padded.shape[2]), jnp.float32)
    im_sum = jnp.zeros((half, count, padded.shape[2]), jnp.float32)
    for position, offset in enumerate(offsets):
        source = padded[:, reach + offset : reach + offset + count]
        re = source[:half]
        im = source[half:]
        cr = coef_real[position][None, None, :]
        ci = coef_imag[position][None, None, :]
        weight = mask[position].astype(jnp.float32)[None, :, None]
        re_sum = re_sum + weight * (cr * re - ci * im)
        im_sum = im_sum + weight * (cr * im + ci * re)
    return jnp.concatenate([re_sum, im_sum], axis=0)


def translate_kernel(low_ref, keep_ref, recv_ref, high_ref, cr_ref, ci_ref, mask_ref, out_ref, pad_ref):
    comps, slots, width = keep_ref.shape
    reach = low_ref.shape[1]
    half = comps // 2
    pad_ref[:, :reach] = low_ref[...]
    pad_ref[:, reach : reach + slots] = keep_ref[...] + recv_ref[...]
    pad_ref[:, reach + slots :] = high_ref[...]
    offsets = list(range(-reach, 0)) + list(range(1, reach + 1))

    def lane_block(lb, carry):
        lanes = pl.ds(pl.multiple_of(lb * 128, 128), 128)
        for h in range(half):
            acc_re = jnp.zeros((slots, 128), jnp.float32)
            acc_im = jnp.zeros((slots, 128), jnp.float32)
            for k, t in enumerate(offsets):
                m = mask_ref[k]
                a = m * cr_ref[pl.ds(k, 1), lanes]
                b = m * ci_ref[pl.ds(k, 1), lanes]
                xr = pad_ref[h, pl.ds(reach + t, slots), lanes]
                xi = pad_ref[h + half, pl.ds(reach + t, slots), lanes]
                acc_re = acc_re + (a * xr - b * xi)
                acc_im = acc_im + (a * xi + b * xr)
            out_ref[h, :, lanes] = acc_re
            out_ref[h + half, :, lanes] = acc_im
        return carry

    lax.fori_loop(0, width // 128, lane_block, 0)


def translate_call(low, keep, recv, high, cr, ci, mask_b):
    comps, slots, width = keep.shape
    reach = low.shape[1]
    return pl.pallas_call(
        translate_kernel,
        out_shape=jax.ShapeDtypeStruct(keep.shape, jnp.float32),
        scratch_shapes=[pltpu.VMEM((comps, slots + 2 * reach, width), jnp.float32)],
    )(low, keep, recv, high, cr, ci, mask_b)


def body(
    pattern,
    child_coef,
    child_mask,
    interp_index,
    interp_weight,
    phase_angle,
    parent_coef,
    parent_mask,
):
    child_dev, comps, box_dev = pattern.shape
    dir_size = lax.axis_size("dir")
    parent_dirs = interp_index.shape[1]
    parent_dev = parent_dirs // dir_size
    groups = phase_angle.shape[0]
    slots = box_dev // groups
    dir_rank = lax.axis_index("dir")
    box_rank = lax.axis_index("box")
    child_first = dir_rank * child_dev
    parent_first = dir_rank * parent_dev
    cosine = jnp.cos(phase_angle)
    sine = jnp.sin(phase_angle)
    rows = interp_matrix(interp_index, interp_weight, child_first, child_dev)

    child_reach = child_coef.shape[1] // 2
    child_padded = with_halo(pattern, (("box", 2),), child_reach)
    child_local = translate_padded(
        child_padded, child_coef[0], child_coef[1], child_mask, child_reach
    )

    parent_reach = parent_coef.shape[1] // 2
    own_real = lax.dynamic_slice_in_dim(parent_coef[0], parent_first, parent_dev, 1)
    own_imag = lax.dynamic_slice_in_dim(parent_coef[1], parent_first, parent_dev, 1)
    own_mask = lax.dynamic_slice_in_dim(parent_mask, box_rank * slots, slots, 1)
    rhs = comps // 2
    step = rhs // 2

    def chunk_xt(chunk):
        part = pattern.reshape(child_dev, 2, rhs, box_dev)[:, :, chunk * step : (chunk + 1) * step]
        xt = part.reshape(child_dev, 2 * step, slots, groups).transpose(3, 1, 2, 0)
        return xt.reshape(groups, 2 * step * slots, child_dev)

    box_size = lax.axis_size("box")
    forward = [(i, i + 1) for i in range(box_size - 1)]
    backward = [(i + 1, i) for i in range(box_size - 1)]
    mask_lanes = jnp.broadcast_to(
        own_mask.astype(jnp.float32)[:, :, None], own_mask.shape + (128,)
    )

    def translate(keep, recv):
        low = keep[:, slots - parent_reach :] + recv[:, slots - parent_reach :]
        high = keep[:, :parent_reach] + recv[:, :parent_reach]
        low = lax.ppermute(low, "box", forward)
        high = lax.ppermute(high, "box", backward)
        return translate_call(low, keep, recv, high, own_real, own_imag, mask_lanes)

    acc_a = reduce_cores(upward(chunk_xt(0), rows, cosine, sine, dir_size, 2 * step))
    acc_a, xt_b = lax.optimization_barrier((acc_a, chunk_xt(1)))
    keep_a, send_a = acc_a[0], acc_a[1]
    recv_a = lax.ppermute(send_a, "dir", ROW_SWAP)
    field_b = upward(xt_b, rows, cosine, sine, dir_size, 2 * step)
    field_b, recv_a = lax.optimization_barrier((field_b, recv_a))
    acc_b = reduce_cores(field_b)
    keep_a, recv_a, acc_b = lax.optimization_barrier((keep_a, recv_a, acc_b))
    keep_b, send_b = acc_b[0], acc_b[1]
    recv_b = lax.ppermute(send_b, "dir", ROW_SWAP)
    local_a = translate(keep_a, recv_a)
    local_a, recv_b = lax.optimization_barrier((local_a, recv_b))
    other_a = lax.ppermute(local_a, "dir", ROW_SWAP)
    local_b = translate(keep_b, recv_b)
    other_a, local_b = lax.optimization_barrier((other_a, local_b))
    all_a = gather_blocks(local_a, other_a)
    all_a, local_b = lax.optimization_barrier((all_a, local_b))
    other_b = lax.ppermute(local_b, "dir", ROW_SWAP)
    far_a = downward(all_a, rows, cosine, sine)
    far_a, other_b = lax.optimization_barrier((far_a, other_b))
    far_b = downward(gather_blocks(local_b, other_b), rows, cosine, sine)
    fars = [far.reshape(groups, child_dev, 2, step, slots) for far in (far_a, far_b)]
    far = jnp.concatenate(fars, axis=3).transpose(1, 2, 3, 4, 0)
    far = far.reshape(child_dev, comps, box_dev)
    return child_local + far


def solution(mesh):
    placed = (P("dir", None, "box"), P(None, None, "dir"), P(None, "box"), P(), P(), P(), P(), P())
    return jax.shard_map(
        body, mesh=mesh, in_specs=placed, out_specs=P("dir", None, "box"), check_vma=False
    )
```

```python
import jax
import jax.numpy as jnp
from jax import lax
from jax.experimental import pallas as pl
from jax.experimental.pallas import tpu as pltpu
from jax.sharding import PartitionSpec as P

HIGHEST = lax.Precision.HIGH


def with_halo(block, sides, width):
    for axis, dim in sides:
        count = lax.axis_size(axis)
        forward = [(i, i + 1) for i in range(count - 1)]
        backward = [(target, source) for source, target in forward]
        low = lax.ppermute(
            lax.slice_in_dim(block, block.shape[dim] - width, None, axis=dim), axis, forward
        )
        high = lax.ppermute(lax.slice_in_dim(block, 0, width, axis=dim), axis, backward)
        block = jnp.concatenate([low, block, high], axis=dim)
    return block


CORE_SWAP = [(0, 1), (1, 0), (2, 3), (3, 2)]
ROW_SWAP = [(0, 2), (2, 0), (1, 3), (3, 1)]


def reduce_cores(field):
    keep, send = field
    return keep + lax.ppermute(send, "dir", CORE_SWAP)


def gather_blocks(local, other):
    mate_local, mate_other = lax.ppermute((local, other), "dir", CORE_SWAP)
    return (local, other, mate_local, mate_other)


def interp_matrix(index, weight, first_row, row_count):
    rows = first_row + lax.iota(jnp.int32, row_count)
    matrix = jnp.zeros((row_count, index.shape[1]), jnp.float32)
    for point in range(index.shape[0]):
        matrix = matrix + jnp.where(
            rows[:, None] == index[point][None, :], weight[point][None, :], jnp.float32(0.0)
        )
    return matrix


def translate_padded(padded, coef_real, coef_imag, mask, reach):
    count = padded.shape[2] - 2 * reach
    half = padded.shape[1] // 2
    offsets = list(range(-reach, 0)) + list(range(1, reach + 1))
    summed = jnp.zeros((padded.shape[0], padded.shape[1], count), jnp.float32)
    for position, offset in enumerate(offsets):
        source = padded[:, :, reach + offset : reach + offset + count]
        real_part = source[:, :half]
        imag_part = source[:, half:]
        scale_real = coef_real[position][:, None, None]
        scale_imag = coef_imag[position][:, None, None]
        weight = mask[position].astype(jnp.float32)[None, None, :]
        turned = jnp.concatenate(
            [
                scale_real * real_part - scale_imag * imag_part,
                scale_real * imag_part + scale_imag * real_part,
            ],
            axis=1,
        )
        summed = summed + weight * turned
    return summed


def slot_part(slot):
    rank = lax.axis_index("dir")
    return ((rank // 2 + slot % 2) % 2) * 2 + (rank % 2 + slot // 2) % 2


def upward_kernel(xt_ref, m_ref, cos_ref, sin_ref, keep_ref, send_ref):
    groups = xt_ref.shape[0]
    comps, slots, width = keep_ref.shape[1:]
    half = comps // 2
    for slot, out_ref in ((pl.program_id(0), keep_ref), (pl.program_id(0) + 2, send_ref)):
        first = pl.multiple_of(slot_part(slot) * width, 128)
        m = m_ref[:, pl.ds(first, width)]
        acc_re = jnp.zeros((half, slots, width), jnp.float32)
        acc_im = jnp.zeros((half, slots, width), jnp.float32)
        for g in range(groups):
            r = jnp.dot(xt_ref[g], m, precision=HIGHEST, preferred_element_type=jnp.float32)
            r = r.reshape(comps, slots, width)
            c = cos_ref[pl.ds(g, 1), pl.ds(first, width)].reshape(1, 1, width)
            s = sin_ref[pl.ds(g, 1), pl.ds(first, width)].reshape(1, 1, width)
            re = r[:half]
            im = r[half:]
            acc_re = acc_re + (c * re - s * im)
            acc_im = acc_im + (c * im + s * re)
        out_ref[0, :half] = acc_re
        out_ref[0, half:] = acc_im


def upward(xt, m, cos, sin, parts, comps):
    groups, rows, q = xt.shape
    total = m.shape[1]
    width = total // parts
    slots = rows // comps
    out = jax.ShapeDtypeStruct((parts // 2, comps, slots, width), jnp.float32)
    block = pl.BlockSpec((1, comps, slots, width), lambda j: (j, 0, 0, 0))
    return pl.pallas_call(
        upward_kernel,
        grid=(parts // 2,),
        in_specs=[
            pl.BlockSpec((groups, rows, q), lambda j: (0, 0, 0)),
            pl.BlockSpec((q, total), lambda j: (0, 0)),
            pl.BlockSpec((groups, total), lambda j: (0, 0)),
            pl.BlockSpec((groups, total), lambda j: (0, 0)),
        ],
        out_specs=[block, block],
        out_shape=[out, out],
    )(xt, m, cos, sin)


def downward_kernel(b0_ref, b1_ref, b2_ref, b3_ref, m_ref, cos_ref, sin_ref, out_ref):
    g = pl.program_id(0)
    comps, slots, width = b0_ref.shape
    half = comps // 2
    q = m_ref.shape[0]
    acc = jnp.zeros((q, comps * slots), jnp.float32)
    rank = lax.axis_index("dir")
    for code, ref in zip((0, 2, 1, 3), (b0_ref, b1_ref, b2_ref, b3_ref)):
        part = ((rank // 2 + code // 2) % 2) * 2 + (rank % 2 + code % 2) % 2
        first = pl.multiple_of(part * width, 128)
        x = ref[...]
        c = cos_ref[pl.ds(g, 1), pl.ds(first, width)].reshape(1, 1, width)
        s = sin_ref[pl.ds(g, 1), pl.ds(first, width)].reshape(1, 1, width)
        re = x[:half]
        im = x[half:]
        spread = jnp.concatenate([c * re + s * im, c * im - s * re], axis=0)
        spread = spread.reshape(comps * slots, width)
        acc = acc + lax.dot_general(
            m_ref[:, pl.ds(first, width)],
            spread,
            (((1,), (1,)), ((), ())),
            precision=HIGHEST,
            preferred_element_type=jnp.float32,
        )
    out_ref[0] = acc


def downward(blocks, m, cos, sin):
    comps, slots, width = blocks[0].shape
    groups = cos.shape[0]
    q, total = m.shape
    block = pl.BlockSpec((comps, slots, width), lambda g: (0, 0, 0))
    return pl.pallas_call(
        downward_kernel,
        grid=(groups,),
        in_specs=[block] * 4
        + [
            pl.BlockSpec((q, total), lambda g: (0, 0)),
            pl.BlockSpec((groups, total), lambda g: (0, 0)),
            pl.BlockSpec((groups, total), lambda g: (0, 0)),
        ],
        out_specs=pl.BlockSpec((1, q, comps * slots), lambda g: (g, 0, 0)),
        out_shape=jax.ShapeDtypeStruct((groups, q, comps * slots), jnp.float32),
    )(*blocks, m, cos, sin)


def parent_translate(padded, coef_real, coef_imag, mask, reach):
    comps = padded.shape[0]
    half = comps // 2
    count = padded.shape[1] - 2 * reach
    offsets = list(range(-reach, 0)) + list(range(1, reach + 1))
    re_sum = jnp.zeros((half, count, padded.shape[2]), jnp.float32)
    im_sum = jnp.zeros((half, count, padded.shape[2]), jnp.float32)
    for position, offset in enumerate(offsets):
        source = padded[:, reach + offset : reach + offset + count]
        re = source[:half]
        im = source[half:]
        cr = coef_real[position][None, None, :]
        ci = coef_imag[position][None, None, :]
        weight = mask[position].astype(jnp.float32)[None, :, None]
        re_sum = re_sum + weight * (cr * re - ci * im)
        im_sum = im_sum + weight * (cr * im + ci * re)
    return jnp.concatenate([re_sum, im_sum], axis=0)


def translate_kernel(low_ref, keep_ref, recv_ref, high_ref, cr_ref, ci_ref, mask_ref, out_ref, pad_ref):
    comps, slots, width = keep_ref.shape
    reach = low_ref.shape[1]
    half = comps // 2
    pad_ref[:, :reach] = low_ref[...]
    pad_ref[:, reach : reach + slots] = keep_ref[...] + recv_ref[...]
    pad_ref[:, reach + slots :] = high_ref[...]
    offsets = list(range(-reach, 0)) + list(range(1, reach + 1))

    def lane_block(lb, carry):
        lanes = pl.ds(pl.multiple_of(lb * 128, 128), 128)
        for h in range(half):
            acc_re = jnp.zeros((slots, 128), jnp.float32)
            acc_im = jnp.zeros((slots, 128), jnp.float32)
            for k, t in enumerate(offsets):
                m = mask_ref[k]
                a = m * cr_ref[pl.ds(k, 1), lanes]
                b = m * ci_ref[pl.ds(k, 1), lanes]
                xr = pad_ref[h, pl.ds(reach + t, slots), lanes]
                xi = pad_ref[h + half, pl.ds(reach + t, slots), lanes]
                acc_re = acc_re + (a * xr - b * xi)
                acc_im = acc_im + (a * xi + b * xr)
            out_ref[h, :, lanes] = acc_re
            out_ref[h + half, :, lanes] = acc_im
        return carry

    lax.fori_loop(0, width // 128, lane_block, 0)


def translate_call(low, keep, recv, high, cr, ci, mask_b):
    comps, slots, width = keep.shape
    reach = low.shape[1]
    return pl.pallas_call(
        translate_kernel,
        out_shape=jax.ShapeDtypeStruct(keep.shape, jnp.float32),
        scratch_shapes=[pltpu.VMEM((comps, slots + 2 * reach, width), jnp.float32)],
    )(low, keep, recv, high, cr, ci, mask_b)


def body(
    pattern,
    child_coef,
    child_mask,
    interp_index,
    interp_weight,
    phase_angle,
    parent_coef,
    parent_mask,
):
    child_dev, comps, box_dev = pattern.shape
    dir_size = lax.axis_size("dir")
    parent_dirs = interp_index.shape[1]
    parent_dev = parent_dirs // dir_size
    groups = phase_angle.shape[0]
    slots = box_dev // groups
    dir_rank = lax.axis_index("dir")
    box_rank = lax.axis_index("box")
    child_first = dir_rank * child_dev
    parent_first = dir_rank * parent_dev
    cosine = jnp.cos(phase_angle)
    sine = jnp.sin(phase_angle)
    rows = interp_matrix(interp_index, interp_weight, child_first, child_dev)

    child_reach = child_coef.shape[1] // 2
    child_padded = with_halo(pattern, (("box", 2),), child_reach)
    child_local = translate_padded(
        child_padded, child_coef[0], child_coef[1], child_mask, child_reach
    )

    parent_reach = parent_coef.shape[1] // 2
    own_real = lax.dynamic_slice_in_dim(parent_coef[0], parent_first, parent_dev, 1)
    own_imag = lax.dynamic_slice_in_dim(parent_coef[1], parent_first, parent_dev, 1)
    own_mask = lax.dynamic_slice_in_dim(parent_mask, box_rank * slots, slots, 1)
    rhs = comps // 2
    step = rhs // 2

    def chunk_xt(chunk):
        part = pattern.reshape(child_dev, 2, rhs, box_dev)[:, :, chunk * step : (chunk + 1) * step]
        xt = part.reshape(child_dev, 2 * step, slots, groups).transpose(3, 1, 2, 0)
        return xt.reshape(groups, 2 * step * slots, child_dev)

    box_size = lax.axis_size("box")
    forward = [(i, i + 1) for i in range(box_size - 1)]
    backward = [(i + 1, i) for i in range(box_size - 1)]
    mask_lanes = jnp.broadcast_to(
        own_mask.astype(jnp.float32)[:, :, None], own_mask.shape + (128,)
    )

    def translate(keep, recv):
        low = keep[:, slots - parent_reach :] + recv[:, slots - parent_reach :]
        high = keep[:, :parent_reach] + recv[:, :parent_reach]
        low = lax.ppermute(low, "box", forward)
        high = lax.ppermute(high, "box", backward)
        return translate_call(low, keep, recv, high, own_real, own_imag, mask_lanes)

    acc_a = reduce_cores(upward(chunk_xt(0), rows, cosine, sine, dir_size, 2 * step))
    acc_a, xt_b = lax.optimization_barrier((acc_a, chunk_xt(1)))
    keep_a, send_a = acc_a[0], acc_a[1]
    recv_a = lax.ppermute(send_a, "dir", ROW_SWAP)
    field_b = upward(xt_b, rows, cosine, sine, dir_size, 2 * step)
    field_b, recv_a = lax.optimization_barrier((field_b, recv_a))
    acc_b = reduce_cores(field_b)
    keep_a, recv_a, acc_b = lax.optimization_barrier((keep_a, recv_a, acc_b))
    keep_b, send_b = acc_b[0], acc_b[1]
    recv_b = lax.ppermute(send_b, "dir", ROW_SWAP)
    local_a = translate(keep_a, recv_a)
    local_a, recv_b = lax.optimization_barrier((local_a, recv_b))
    other_a = lax.ppermute(local_a, "dir", ROW_SWAP)
    local_b = translate(keep_b, recv_b)
    other_a, local_b = lax.optimization_barrier((other_a, local_b))
    all_a = gather_blocks(local_a, other_a)
    all_a, local_b = lax.optimization_barrier((all_a, local_b))
    other_b = lax.ppermute(local_b, "dir", ROW_SWAP)
    far_a = downward(all_a, rows, cosine, sine)
    far_a, other_b = lax.optimization_barrier((far_a, other_b))
    far_b = downward(gather_blocks(local_b, other_b), rows, cosine, sine)
    fars = [far.reshape(groups, child_dev, 2, step, slots) for far in (far_a, far_b)]
    far = jnp.concatenate(fars, axis=3).transpose(1, 2, 3, 4, 0)
    far = far.reshape(child_dev, comps, box_dev)
    return child_local + far


def solution(mesh):
    placed = (P("dir", None, "box"), P(None, None, "dir"), P(None, "box"), P(), P(), P(), P(), P())
    return jax.shard_map(
        body, mesh=mesh, in_specs=placed, out_specs=P("dir", None, "box"), check_vma=False
    )
```

```python
import jax
import jax.numpy as jnp
from jax import lax
from jax.experimental import pallas as pl
from jax.experimental.pallas import tpu as pltpu
from jax.sharding import PartitionSpec as P

HIGHEST = lax.Precision.HIGH


def with_halo(block, sides, width):
    for axis, dim in sides:
        count = lax.axis_size(axis)
        forward = [(i, i + 1) for i in range(count - 1)]
        backward = [(target, source) for source, target in forward]
        low = lax.ppermute(
            lax.slice_in_dim(block, block.shape[dim] - width, None, axis=dim), axis, forward
        )
        high = lax.ppermute(lax.slice_in_dim(block, 0, width, axis=dim), axis, backward)
        block = jnp.concatenate([low, block, high], axis=dim)
    return block


CORE_SWAP = [(0, 1), (1, 0), (2, 3), (3, 2)]
ROW_SWAP = [(0, 2), (2, 0), (1, 3), (3, 1)]


def reduce_cores(field):
    keep, send = field
    return keep + lax.ppermute(send, "dir", CORE_SWAP)


def gather_blocks(local, other):
    mate_local, mate_other = lax.ppermute((local, other), "dir", CORE_SWAP)
    return (local, other, mate_local, mate_other)


def interp_matrix(index, weight, first_row, row_count):
    rows = first_row + lax.iota(jnp.int32, row_count)
    matrix = jnp.zeros((row_count, index.shape[1]), jnp.float32)
    for point in range(index.shape[0]):
        matrix = matrix + jnp.where(
            rows[:, None] == index[point][None, :], weight[point][None, :], jnp.float32(0.0)
        )
    return matrix


def translate_padded(padded, coef_real, coef_imag, mask, reach):
    count = padded.shape[2] - 2 * reach
    half = padded.shape[1] // 2
    offsets = list(range(-reach, 0)) + list(range(1, reach + 1))
    summed = jnp.zeros((padded.shape[0], padded.shape[1], count), jnp.float32)
    for position, offset in enumerate(offsets):
        source = padded[:, :, reach + offset : reach + offset + count]
        real_part = source[:, :half]
        imag_part = source[:, half:]
        scale_real = coef_real[position][:, None, None]
        scale_imag = coef_imag[position][:, None, None]
        weight = mask[position].astype(jnp.float32)[None, None, :]
        turned = jnp.concatenate(
            [
                scale_real * real_part - scale_imag * imag_part,
                scale_real * imag_part + scale_imag * real_part,
            ],
            axis=1,
        )
        summed = summed + weight * turned
    return summed


def slot_part(slot):
    rank = lax.axis_index("dir")
    return ((rank // 2 + slot % 2) % 2) * 2 + (rank % 2 + slot // 2) % 2


def upward_kernel(xt_ref, m_ref, cos_ref, sin_ref, keep_ref, send_ref):
    groups = xt_ref.shape[0]
    comps, slots, width = keep_ref.shape[1:]
    half = comps // 2
    for slot, out_ref in ((pl.program_id(0), keep_ref), (pl.program_id(0) + 2, send_ref)):
        first = pl.multiple_of(slot_part(slot) * width, 128)
        m = m_ref[:, pl.ds(first, width)]
        acc_re = jnp.zeros((half, slots, width), jnp.float32)
        acc_im = jnp.zeros((half, slots, width), jnp.float32)
        for g in range(groups):
            r = jnp.dot(xt_ref[g], m, precision=HIGHEST, preferred_element_type=jnp.float32)
            r = r.reshape(comps, slots, width)
            c = cos_ref[pl.ds(g, 1), pl.ds(first, width)].reshape(1, 1, width)
            s = sin_ref[pl.ds(g, 1), pl.ds(first, width)].reshape(1, 1, width)
            re = r[:half]
            im = r[half:]
            acc_re = acc_re + (c * re - s * im)
            acc_im = acc_im + (c * im + s * re)
        out_ref[0, :half] = acc_re
        out_ref[0, half:] = acc_im


def upward(xt, m, cos, sin, parts, comps):
    groups, rows, q = xt.shape
    total = m.shape[1]
    width = total // parts
    slots = rows // comps
    out = jax.ShapeDtypeStruct((parts // 2, comps, slots, width), jnp.float32)
    block = pl.BlockSpec((1, comps, slots, width), lambda j: (j, 0, 0, 0))
    return pl.pallas_call(
        upward_kernel,
        grid=(parts // 2,),
        in_specs=[
            pl.BlockSpec((groups, rows, q), lambda j: (0, 0, 0)),
            pl.BlockSpec((q, total), lambda j: (0, 0)),
            pl.BlockSpec((groups, total), lambda j: (0, 0)),
            pl.BlockSpec((groups, total), lambda j: (0, 0)),
        ],
        out_specs=[block, block],
        out_shape=[out, out],
    )(xt, m, cos, sin)


def downward_kernel(b0_ref, b1_ref, b2_ref, b3_ref, m_ref, cos_ref, sin_ref, out_ref):
    g = pl.program_id(0)
    comps, slots, width = b0_ref.shape
    half = comps // 2
    q = m_ref.shape[0]
    acc = jnp.zeros((q, comps * slots), jnp.float32)
    rank = lax.axis_index("dir")
    for code, ref in zip((0, 2, 1, 3), (b0_ref, b1_ref, b2_ref, b3_ref)):
        part = ((rank // 2 + code // 2) % 2) * 2 + (rank % 2 + code % 2) % 2
        first = pl.multiple_of(part * width, 128)
        x = ref[...]
        c = cos_ref[pl.ds(g, 1), pl.ds(first, width)].reshape(1, 1, width)
        s = sin_ref[pl.ds(g, 1), pl.ds(first, width)].reshape(1, 1, width)
        re = x[:half]
        im = x[half:]
        spread = jnp.concatenate([c * re + s * im, c * im - s * re], axis=0)
        spread = spread.reshape(comps * slots, width)
        acc = acc + lax.dot_general(
            m_ref[:, pl.ds(first, width)],
            spread,
            (((1,), (1,)), ((), ())),
            precision=HIGHEST,
            preferred_element_type=jnp.float32,
        )
    out_ref[0] = acc


def downward(blocks, m, cos, sin):
    comps, slots, width = blocks[0].shape
    groups = cos.shape[0]
    q, total = m.shape
    block = pl.BlockSpec((comps, slots, width), lambda g: (0, 0, 0))
    return pl.pallas_call(
        downward_kernel,
        grid=(groups,),
        in_specs=[block] * 4
        + [
            pl.BlockSpec((q, total), lambda g: (0, 0)),
            pl.BlockSpec((groups, total), lambda g: (0, 0)),
            pl.BlockSpec((groups, total), lambda g: (0, 0)),
        ],
        out_specs=pl.BlockSpec((1, q, comps * slots), lambda g: (g, 0, 0)),
        out_shape=jax.ShapeDtypeStruct((groups, q, comps * slots), jnp.float32),
    )(*blocks, m, cos, sin)


def parent_translate(padded, coef_real, coef_imag, mask, reach):
    comps = padded.shape[0]
    half = comps // 2
    count = padded.shape[1] - 2 * reach
    offsets = list(range(-reach, 0)) + list(range(1, reach + 1))
    re_sum = jnp.zeros((half, count, padded.shape[2]), jnp.float32)
    im_sum = jnp.zeros((half, count, padded.shape[2]), jnp.float32)
    for position, offset in enumerate(offsets):
        source = padded[:, reach + offset : reach + offset + count]
        re = source[:half]
        im = source[half:]
        cr = coef_real[position][None, None, :]
        ci = coef_imag[position][None, None, :]
        weight = mask[position].astype(jnp.float32)[None, :, None]
        re_sum = re_sum + weight * (cr * re - ci * im)
        im_sum = im_sum + weight * (cr * im + ci * re)
    return jnp.concatenate([re_sum, im_sum], axis=0)


def translate_kernel(low_ref, keep_ref, recv_ref, high_ref, cr_ref, ci_ref, mask_ref, out_ref, pad_ref):
    comps, slots, width = keep_ref.shape
    reach = low_ref.shape[1]
    half = comps // 2
    pad_ref[:, :reach] = low_ref[...]
    pad_ref[:, reach : reach + slots] = keep_ref[...] + recv_ref[...]
    pad_ref[:, reach + slots :] = high_ref[...]
    offsets = list(range(-reach, 0)) + list(range(1, reach + 1))

    def lane_block(lb, carry):
        lanes = pl.ds(pl.multiple_of(lb * 128, 128), 128)
        for h in range(half):
            acc_re = jnp.zeros((slots, 128), jnp.float32)
            acc_im = jnp.zeros((slots, 128), jnp.float32)
            for k, t in enumerate(offsets):
                m = mask_ref[k]
                a = m * cr_ref[pl.ds(k, 1), lanes]
                b = m * ci_ref[pl.ds(k, 1), lanes]
                xr = pad_ref[h, pl.ds(reach + t, slots), lanes]
                xi = pad_ref[h + half, pl.ds(reach + t, slots), lanes]
                acc_re = acc_re + (a * xr - b * xi)
                acc_im = acc_im + (a * xi + b * xr)
            out_ref[h, :, lanes] = acc_re
            out_ref[h + half, :, lanes] = acc_im
        return carry

    lax.fori_loop(0, width // 128, lane_block, 0)


def translate_call(low, keep, recv, high, cr, ci, mask_b):
    comps, slots, width = keep.shape
    reach = low.shape[1]
    return pl.pallas_call(
        translate_kernel,
        out_shape=jax.ShapeDtypeStruct(keep.shape, jnp.float32),
        scratch_shapes=[pltpu.VMEM((comps, slots + 2 * reach, width), jnp.float32)],
    )(low, keep, recv, high, cr, ci, mask_b)


def body(
    pattern,
    child_coef,
    child_mask,
    interp_index,
    interp_weight,
    phase_angle,
    parent_coef,
    parent_mask,
):
    child_dev, comps, box_dev = pattern.shape
    dir_size = lax.axis_size("dir")
    parent_dirs = interp_index.shape[1]
    parent_dev = parent_dirs // dir_size
    groups = phase_angle.shape[0]
    slots = box_dev // groups
    dir_rank = lax.axis_index("dir")
    box_rank = lax.axis_index("box")
    child_first = dir_rank * child_dev
    parent_first = dir_rank * parent_dev
    cosine = jnp.cos(phase_angle)
    sine = jnp.sin(phase_angle)
    rows = interp_matrix(interp_index, interp_weight, child_first, child_dev)

    child_reach = child_coef.shape[1] // 2
    child_padded = with_halo(pattern, (("box", 2),), child_reach)

    parent_reach = parent_coef.shape[1] // 2
    own_real = lax.dynamic_slice_in_dim(parent_coef[0], parent_first, parent_dev, 1)
    own_imag = lax.dynamic_slice_in_dim(parent_coef[1], parent_first, parent_dev, 1)
    own_mask = lax.dynamic_slice_in_dim(parent_mask, box_rank * slots, slots, 1)
    rhs = comps // 2
    step = rhs // 2

    def chunk_xt(chunk):
        part = pattern.reshape(child_dev, 2, rhs, box_dev)[:, :, chunk * step : (chunk + 1) * step]
        xt = part.reshape(child_dev, 2 * step, slots, groups).transpose(3, 1, 2, 0)
        return xt.reshape(groups, 2 * step * slots, child_dev)

    box_size = lax.axis_size("box")
    forward = [(i, i + 1) for i in range(box_size - 1)]
    backward = [(i + 1, i) for i in range(box_size - 1)]
    mask_lanes = jnp.broadcast_to(
        own_mask.astype(jnp.float32)[:, :, None], own_mask.shape + (128,)
    )

    def translate(keep, recv):
        low = keep[:, slots - parent_reach :] + recv[:, slots - parent_reach :]
        high = keep[:, :parent_reach] + recv[:, :parent_reach]
        low = lax.ppermute(low, "box", forward)
        high = lax.ppermute(high, "box", backward)
        return translate_call(low, keep, recv, high, own_real, own_imag, mask_lanes)

    field_a, child_padded = lax.optimization_barrier(
        (upward(chunk_xt(0), rows, cosine, sine, dir_size, 2 * step), child_padded)
    )
    acc_a = reduce_cores(field_a)
    child_local = translate_padded(
        child_padded, child_coef[0], child_coef[1], child_mask, child_reach
    )
    acc_a, xt_b = lax.optimization_barrier((acc_a, chunk_xt(1)))
    keep_a, send_a = acc_a[0], acc_a[1]
    recv_a = lax.ppermute(send_a, "dir", ROW_SWAP)
    field_b = upward(xt_b, rows, cosine, sine, dir_size, 2 * step)
    field_b, recv_a = lax.optimization_barrier((field_b, recv_a))
    acc_b = reduce_cores(field_b)
    keep_a, recv_a, acc_b = lax.optimization_barrier((keep_a, recv_a, acc_b))
    keep_b, send_b = acc_b[0], acc_b[1]
    recv_b = lax.ppermute(send_b, "dir", ROW_SWAP)
    local_a = translate(keep_a, recv_a)
    local_a, recv_b = lax.optimization_barrier((local_a, recv_b))
    other_a = lax.ppermute(local_a, "dir", ROW_SWAP)
    local_b = translate(keep_b, recv_b)
    other_a, local_b = lax.optimization_barrier((other_a, local_b))
    all_a = gather_blocks(local_a, other_a)
    all_a, local_b = lax.optimization_barrier((all_a, local_b))
    other_b = lax.ppermute(local_b, "dir", ROW_SWAP)
    far_a = downward(all_a, rows, cosine, sine)
    far_a, other_b = lax.optimization_barrier((far_a, other_b))
    far_b = downward(gather_blocks(local_b, other_b), rows, cosine, sine)
    fars = [far.reshape(groups, child_dev, 2, step, slots) for far in (far_a, far_b)]
    far = jnp.concatenate(fars, axis=3).transpose(1, 2, 3, 4, 0)
    far = far.reshape(child_dev, comps, box_dev)
    return child_local + far


def solution(mesh):
    placed = (P("dir", None, "box"), P(None, None, "dir"), P(None, "box"), P(), P(), P(), P(), P())
    return jax.shard_map(
        body, mesh=mesh, in_specs=placed, out_specs=P("dir", None, "box"), check_vma=False
    )
```

```python
import jax
import jax.numpy as jnp
from jax import lax
from jax.experimental import pallas as pl
from jax.experimental.pallas import tpu as pltpu
from jax.sharding import PartitionSpec as P

HIGHEST = lax.Precision.HIGH


def with_halo(block, sides, width):
    for axis, dim in sides:
        count = lax.axis_size(axis)
        forward = [(i, i + 1) for i in range(count - 1)]
        backward = [(target, source) for source, target in forward]
        low = lax.ppermute(
            lax.slice_in_dim(block, block.shape[dim] - width, None, axis=dim), axis, forward
        )
        high = lax.ppermute(lax.slice_in_dim(block, 0, width, axis=dim), axis, backward)
        block = jnp.concatenate([low, block, high], axis=dim)
    return block


CORE_SWAP = [(0, 1), (1, 0), (2, 3), (3, 2)]
ROW_SWAP = [(0, 2), (2, 0), (1, 3), (3, 1)]


def reduce_cores(field):
    keep, send = field
    return keep + lax.ppermute(send, "dir", CORE_SWAP)


def gather_blocks(local, other):
    mate_local, mate_other = lax.ppermute((local, other), "dir", CORE_SWAP)
    return (local, other, mate_local, mate_other)


def interp_matrix(index, weight, first_row, row_count):
    rows = first_row + lax.iota(jnp.int32, row_count)
    matrix = jnp.zeros((row_count, index.shape[1]), jnp.float32)
    for point in range(index.shape[0]):
        matrix = matrix + jnp.where(
            rows[:, None] == index[point][None, :], weight[point][None, :], jnp.float32(0.0)
        )
    return matrix


def translate_padded(padded, coef_real, coef_imag, mask, reach):
    count = padded.shape[2] - 2 * reach
    half = padded.shape[1] // 2
    offsets = list(range(-reach, 0)) + list(range(1, reach + 1))
    summed = jnp.zeros((padded.shape[0], padded.shape[1], count), jnp.float32)
    for position, offset in enumerate(offsets):
        source = padded[:, :, reach + offset : reach + offset + count]
        real_part = source[:, :half]
        imag_part = source[:, half:]
        scale_real = coef_real[position][:, None, None]
        scale_imag = coef_imag[position][:, None, None]
        weight = mask[position].astype(jnp.float32)[None, None, :]
        turned = jnp.concatenate(
            [
                scale_real * real_part - scale_imag * imag_part,
                scale_real * imag_part + scale_imag * real_part,
            ],
            axis=1,
        )
        summed = summed + weight * turned
    return summed


def slot_part(slot):
    rank = lax.axis_index("dir")
    return ((rank // 2 + slot % 2) % 2) * 2 + (rank % 2 + slot // 2) % 2


def upward_kernel(xt_ref, m_ref, cos_ref, sin_ref, keep_ref, send_ref):
    groups = xt_ref.shape[0]
    comps, slots, width = keep_ref.shape[1:]
    half = comps // 2
    for slot, out_ref in ((pl.program_id(0), keep_ref), (pl.program_id(0) + 2, send_ref)):
        first = pl.multiple_of(slot_part(slot) * width, 128)
        m = m_ref[:, pl.ds(first, width)]
        acc_re = jnp.zeros((half, slots, width), jnp.float32)
        acc_im = jnp.zeros((half, slots, width), jnp.float32)
        for g in range(groups):
            r = jnp.dot(xt_ref[g], m, precision=HIGHEST, preferred_element_type=jnp.float32)
            r = r.reshape(comps, slots, width)
            c = cos_ref[pl.ds(g, 1), pl.ds(first, width)].reshape(1, 1, width)
            s = sin_ref[pl.ds(g, 1), pl.ds(first, width)].reshape(1, 1, width)
            re = r[:half]
            im = r[half:]
            acc_re = acc_re + (c * re - s * im)
            acc_im = acc_im + (c * im + s * re)
        out_ref[0, :half] = acc_re
        out_ref[0, half:] = acc_im


def upward(xt, m, cos, sin, parts, comps):
    groups, rows, q = xt.shape
    total = m.shape[1]
    width = total // parts
    slots = rows // comps
    out = jax.ShapeDtypeStruct((parts // 2, comps, slots, width), jnp.float32)
    block = pl.BlockSpec((1, comps, slots, width), lambda j: (j, 0, 0, 0))
    return pl.pallas_call(
        upward_kernel,
        grid=(parts // 2,),
        in_specs=[
            pl.BlockSpec((groups, rows, q), lambda j: (0, 0, 0)),
            pl.BlockSpec((q, total), lambda j: (0, 0)),
            pl.BlockSpec((groups, total), lambda j: (0, 0)),
            pl.BlockSpec((groups, total), lambda j: (0, 0)),
        ],
        out_specs=[block, block],
        out_shape=[out, out],
    )(xt, m, cos, sin)


def downward_kernel(b0_ref, b1_ref, b2_ref, b3_ref, m_ref, cos_ref, sin_ref, out_ref):
    g = pl.program_id(0)
    comps, slots, width = b0_ref.shape
    half = comps // 2
    q = m_ref.shape[0]
    acc = jnp.zeros((q, comps * slots), jnp.float32)
    rank = lax.axis_index("dir")
    for code, ref in zip((0, 2, 1, 3), (b0_ref, b1_ref, b2_ref, b3_ref)):
        part = ((rank // 2 + code // 2) % 2) * 2 + (rank % 2 + code % 2) % 2
        first = pl.multiple_of(part * width, 128)
        x = ref[...]
        c = cos_ref[pl.ds(g, 1), pl.ds(first, width)].reshape(1, 1, width)
        s = sin_ref[pl.ds(g, 1), pl.ds(first, width)].reshape(1, 1, width)
        re = x[:half]
        im = x[half:]
        spread = jnp.concatenate([c * re + s * im, c * im - s * re], axis=0)
        spread = spread.reshape(comps * slots, width)
        acc = acc + lax.dot_general(
            m_ref[:, pl.ds(first, width)],
            spread,
            (((1,), (1,)), ((), ())),
            precision=HIGHEST,
            preferred_element_type=jnp.float32,
        )
    out_ref[0] = acc


def downward(blocks, m, cos, sin):
    comps, slots, width = blocks[0].shape
    groups = cos.shape[0]
    q, total = m.shape
    block = pl.BlockSpec((comps, slots, width), lambda g: (0, 0, 0))
    return pl.pallas_call(
        downward_kernel,
        grid=(groups,),
        in_specs=[block] * 4
        + [
            pl.BlockSpec((q, total), lambda g: (0, 0)),
            pl.BlockSpec((groups, total), lambda g: (0, 0)),
            pl.BlockSpec((groups, total), lambda g: (0, 0)),
        ],
        out_specs=pl.BlockSpec((1, q, comps * slots), lambda g: (g, 0, 0)),
        out_shape=jax.ShapeDtypeStruct((groups, q, comps * slots), jnp.float32),
    )(*blocks, m, cos, sin)


def parent_translate(padded, coef_real, coef_imag, mask, reach):
    comps = padded.shape[0]
    half = comps // 2
    count = padded.shape[1] - 2 * reach
    offsets = list(range(-reach, 0)) + list(range(1, reach + 1))
    re_sum = jnp.zeros((half, count, padded.shape[2]), jnp.float32)
    im_sum = jnp.zeros((half, count, padded.shape[2]), jnp.float32)
    for position, offset in enumerate(offsets):
        source = padded[:, reach + offset : reach + offset + count]
        re = source[:half]
        im = source[half:]
        cr = coef_real[position][None, None, :]
        ci = coef_imag[position][None, None, :]
        weight = mask[position].astype(jnp.float32)[None, :, None]
        re_sum = re_sum + weight * (cr * re - ci * im)
        im_sum = im_sum + weight * (cr * im + ci * re)
    return jnp.concatenate([re_sum, im_sum], axis=0)


def translate_kernel(low_ref, keep_ref, recv_ref, high_ref, cr_ref, ci_ref, mask_ref, out_ref, pad_ref):
    comps, slots, width = keep_ref.shape
    reach = low_ref.shape[1]
    half = comps // 2
    pad_ref[:, :reach] = low_ref[...]
    pad_ref[:, reach : reach + slots] = keep_ref[...] + recv_ref[...]
    pad_ref[:, reach + slots :] = high_ref[...]
    offsets = list(range(-reach, 0)) + list(range(1, reach + 1))

    def lane_block(lb, carry):
        lanes = pl.ds(pl.multiple_of(lb * 128, 128), 128)
        for h in range(half):
            acc_re = jnp.zeros((slots, 128), jnp.float32)
            acc_im = jnp.zeros((slots, 128), jnp.float32)
            for k, t in enumerate(offsets):
                m = mask_ref[k]
                a = m * cr_ref[pl.ds(k, 1), lanes]
                b = m * ci_ref[pl.ds(k, 1), lanes]
                xr = pad_ref[h, pl.ds(reach + t, slots), lanes]
                xi = pad_ref[h + half, pl.ds(reach + t, slots), lanes]
                acc_re = acc_re + (a * xr - b * xi)
                acc_im = acc_im + (a * xi + b * xr)
            out_ref[h, :, lanes] = acc_re
            out_ref[h + half, :, lanes] = acc_im
        return carry

    lax.fori_loop(0, width // 128, lane_block, 0)


def translate_call(low, keep, recv, high, cr, ci, mask_b):
    comps, slots, width = keep.shape
    reach = low.shape[1]
    return pl.pallas_call(
        translate_kernel,
        out_shape=jax.ShapeDtypeStruct(keep.shape, jnp.float32),
        scratch_shapes=[pltpu.VMEM((comps, slots + 2 * reach, width), jnp.float32)],
    )(low, keep, recv, high, cr, ci, mask_b)


def body(
    pattern,
    child_coef,
    child_mask,
    interp_index,
    interp_weight,
    phase_angle,
    parent_coef,
    parent_mask,
):
    child_dev, comps, box_dev = pattern.shape
    dir_size = lax.axis_size("dir")
    parent_dirs = interp_index.shape[1]
    parent_dev = parent_dirs // dir_size
    groups = phase_angle.shape[0]
    slots = box_dev // groups
    dir_rank = lax.axis_index("dir")
    box_rank = lax.axis_index("box")
    child_first = dir_rank * child_dev
    parent_first = dir_rank * parent_dev
    cosine = jnp.cos(phase_angle)
    sine = jnp.sin(phase_angle)
    rows = interp_matrix(interp_index, interp_weight, child_first, child_dev)

    child_reach = child_coef.shape[1] // 2

    parent_reach = parent_coef.shape[1] // 2
    own_real = lax.dynamic_slice_in_dim(parent_coef[0], parent_first, parent_dev, 1)
    own_imag = lax.dynamic_slice_in_dim(parent_coef[1], parent_first, parent_dev, 1)
    own_mask = lax.dynamic_slice_in_dim(parent_mask, box_rank * slots, slots, 1)
    rhs = comps // 2
    step = rhs // 2

    def chunk_xt(chunk):
        part = pattern.reshape(child_dev, 2, rhs, box_dev)[:, :, chunk * step : (chunk + 1) * step]
        xt = part.reshape(child_dev, 2 * step, slots, groups).transpose(3, 1, 2, 0)
        return xt.reshape(groups, 2 * step * slots, child_dev)

    box_size = lax.axis_size("box")
    forward = [(i, i + 1) for i in range(box_size - 1)]
    backward = [(i + 1, i) for i in range(box_size - 1)]
    mask_lanes = jnp.broadcast_to(
        own_mask.astype(jnp.float32)[:, :, None], own_mask.shape + (128,)
    )

    def translate(keep, recv):
        low = keep[:, slots - parent_reach :] + recv[:, slots - parent_reach :]
        high = keep[:, :parent_reach] + recv[:, :parent_reach]
        low = lax.ppermute(low, "box", forward)
        high = lax.ppermute(high, "box", backward)
        return translate_call(low, keep, recv, high, own_real, own_imag, mask_lanes)

    acc_a = reduce_cores(upward(chunk_xt(0), rows, cosine, sine, dir_size, 2 * step))
    acc_a, xt_b = lax.optimization_barrier((acc_a, chunk_xt(1)))
    keep_a, send_a = acc_a[0], acc_a[1]
    recv_a = lax.ppermute(send_a, "dir", ROW_SWAP)
    field_b = upward(xt_b, rows, cosine, sine, dir_size, 2 * step)
    field_b, recv_a = lax.optimization_barrier((field_b, recv_a))
    acc_b = reduce_cores(field_b)
    keep_a, recv_a, acc_b = lax.optimization_barrier((keep_a, recv_a, acc_b))
    keep_b, send_b = acc_b[0], acc_b[1]
    recv_b = lax.ppermute(send_b, "dir", ROW_SWAP)
    local_a = translate(keep_a, recv_a)
    local_a, recv_b = lax.optimization_barrier((local_a, recv_b))
    other_a = lax.ppermute(local_a, "dir", ROW_SWAP)
    local_b = translate(keep_b, recv_b)
    other_a, local_b = lax.optimization_barrier((other_a, local_b))
    all_a = gather_blocks(local_a, other_a)
    all_a, local_b = lax.optimization_barrier((all_a, local_b))
    other_b = lax.ppermute(local_b, "dir", ROW_SWAP)
    far_a = downward(all_a, rows, cosine, sine)
    far_a, other_b, edges = lax.optimization_barrier((far_a, other_b, pattern))
    child_padded = with_halo(edges, (("box", 2),), child_reach)
    child_local = translate_padded(
        child_padded, child_coef[0], child_coef[1], child_mask, child_reach
    )
    far_b = downward(gather_blocks(local_b, other_b), rows, cosine, sine)
    fars = [far.reshape(groups, child_dev, 2, step, slots) for far in (far_a, far_b)]
    far = jnp.concatenate(fars, axis=3).transpose(1, 2, 3, 4, 0)
    far = far.reshape(child_dev, comps, box_dev)
    return child_local + far


def solution(mesh):
    placed = (P("dir", None, "box"), P(None, None, "dir"), P(None, "box"), P(), P(), P(), P(), P())
    return jax.shard_map(
        body, mesh=mesh, in_specs=placed, out_specs=P("dir", None, "box"), check_vma=False
    )
```

```python
import jax
import jax.numpy as jnp
from jax import lax
from jax.experimental import pallas as pl
from jax.experimental.pallas import tpu as pltpu
from jax.sharding import PartitionSpec as P

HIGHEST = lax.Precision.HIGH


def with_halo(block, sides, width):
    for axis, dim in sides:
        count = lax.axis_size(axis)
        rank = lax.axis_index(axis)
        forward = [(i, (i + 1) % count) for i in range(count)]
        backward = [((i + 1) % count, i) for i in range(count)]
        low = lax.ppermute(
            lax.slice_in_dim(block, block.shape[dim] - width, None, axis=dim), axis, forward
        )
        high = lax.ppermute(lax.slice_in_dim(block, 0, width, axis=dim), axis, backward)
        low = jnp.where(rank == 0, jnp.zeros_like(low), low)
        high = jnp.where(rank == count - 1, jnp.zeros_like(high), high)
        block = jnp.concatenate([low, block, high], axis=dim)
    return block


CORE_SWAP = [(0, 1), (1, 0), (2, 3), (3, 2)]
ROW_SWAP = [(0, 2), (2, 0), (1, 3), (3, 1)]


def reduce_cores(field):
    keep, send = field
    return keep + lax.ppermute(send, "dir", CORE_SWAP)


def gather_blocks(local, other):
    mate_local, mate_other = lax.ppermute((local, other), "dir", CORE_SWAP)
    return (local, other, mate_local, mate_other)


def interp_matrix(index, weight, first_row, row_count):
    rows = first_row + lax.iota(jnp.int32, row_count)
    matrix = jnp.zeros((row_count, index.shape[1]), jnp.float32)
    for point in range(index.shape[0]):
        matrix = matrix + jnp.where(
            rows[:, None] == index[point][None, :], weight[point][None, :], jnp.float32(0.0)
        )
    return matrix


def translate_padded(padded, coef_real, coef_imag, mask, reach):
    count = padded.shape[2] - 2 * reach
    half = padded.shape[1] // 2
    offsets = list(range(-reach, 0)) + list(range(1, reach + 1))
    summed = jnp.zeros((padded.shape[0], padded.shape[1], count), jnp.float32)
    for position, offset in enumerate(offsets):
        source = padded[:, :, reach + offset : reach + offset + count]
        real_part = source[:, :half]
        imag_part = source[:, half:]
        scale_real = coef_real[position][:, None, None]
        scale_imag = coef_imag[position][:, None, None]
        weight = mask[position].astype(jnp.float32)[None, None, :]
        turned = jnp.concatenate(
            [
                scale_real * real_part - scale_imag * imag_part,
                scale_real * imag_part + scale_imag * real_part,
            ],
            axis=1,
        )
        summed = summed + weight * turned
    return summed


def slot_part(slot):
    rank = lax.axis_index("dir")
    return ((rank // 2 + slot % 2) % 2) * 2 + (rank % 2 + slot // 2) % 2


def upward_kernel(xt_ref, m_ref, cos_ref, sin_ref, keep_ref, send_ref):
    groups = xt_ref.shape[0]
    comps, slots, width = keep_ref.shape[1:]
    half = comps // 2
    for slot, out_ref in ((pl.program_id(0), keep_ref), (pl.program_id(0) + 2, send_ref)):
        first = pl.multiple_of(slot_part(slot) * width, 128)
        m = m_ref[:, pl.ds(first, width)]
        acc_re = jnp.zeros((half, slots, width), jnp.float32)
        acc_im = jnp.zeros((half, slots, width), jnp.float32)
        for g in range(groups):
            r = jnp.dot(xt_ref[g], m, precision=HIGHEST, preferred_element_type=jnp.float32)
            r = r.reshape(comps, slots, width)
            c = cos_ref[pl.ds(g, 1), pl.ds(first, width)].reshape(1, 1, width)
            s = sin_ref[pl.ds(g, 1), pl.ds(first, width)].reshape(1, 1, width)
            re = r[:half]
            im = r[half:]
            acc_re = acc_re + (c * re - s * im)
            acc_im = acc_im + (c * im + s * re)
        out_ref[0, :half] = acc_re
        out_ref[0, half:] = acc_im


def upward(xt, m, cos, sin, parts, comps):
    groups, rows, q = xt.shape
    total = m.shape[1]
    width = total // parts
    slots = rows // comps
    out = jax.ShapeDtypeStruct((parts // 2, comps, slots, width), jnp.float32)
    block = pl.BlockSpec((1, comps, slots, width), lambda j: (j, 0, 0, 0))
    return pl.pallas_call(
        upward_kernel,
        grid=(parts // 2,),
        in_specs=[
            pl.BlockSpec((groups, rows, q), lambda j: (0, 0, 0)),
            pl.BlockSpec((q, total), lambda j: (0, 0)),
            pl.BlockSpec((groups, total), lambda j: (0, 0)),
            pl.BlockSpec((groups, total), lambda j: (0, 0)),
        ],
        out_specs=[block, block],
        out_shape=[out, out],
    )(xt, m, cos, sin)


def downward_kernel(b0_ref, b1_ref, b2_ref, b3_ref, m_ref, cos_ref, sin_ref, out_ref):
    g = pl.program_id(0)
    comps, slots, width = b0_ref.shape
    half = comps // 2
    q = m_ref.shape[0]
    acc = jnp.zeros((q, comps * slots), jnp.float32)
    rank = lax.axis_index("dir")
    for code, ref in zip((0, 2, 1, 3), (b0_ref, b1_ref, b2_ref, b3_ref)):
        part = ((rank // 2 + code // 2) % 2) * 2 + (rank % 2 + code % 2) % 2
        first = pl.multiple_of(part * width, 128)
        x = ref[...]
        c = cos_ref[pl.ds(g, 1), pl.ds(first, width)].reshape(1, 1, width)
        s = sin_ref[pl.ds(g, 1), pl.ds(first, width)].reshape(1, 1, width)
        re = x[:half]
        im = x[half:]
        spread = jnp.concatenate([c * re + s * im, c * im - s * re], axis=0)
        spread = spread.reshape(comps * slots, width)
        acc = acc + lax.dot_general(
            m_ref[:, pl.ds(first, width)],
            spread,
            (((1,), (1,)), ((), ())),
            precision=HIGHEST,
            preferred_element_type=jnp.float32,
        )
    out_ref[0] = acc


def downward(blocks, m, cos, sin):
    comps, slots, width = blocks[0].shape
    groups = cos.shape[0]
    q, total = m.shape
    block = pl.BlockSpec((comps, slots, width), lambda g: (0, 0, 0))
    return pl.pallas_call(
        downward_kernel,
        grid=(groups,),
        in_specs=[block] * 4
        + [
            pl.BlockSpec((q, total), lambda g: (0, 0)),
            pl.BlockSpec((groups, total), lambda g: (0, 0)),
            pl.BlockSpec((groups, total), lambda g: (0, 0)),
        ],
        out_specs=pl.BlockSpec((1, q, comps * slots), lambda g: (g, 0, 0)),
        out_shape=jax.ShapeDtypeStruct((groups, q, comps * slots), jnp.float32),
    )(*blocks, m, cos, sin)


def parent_translate(padded, coef_real, coef_imag, mask, reach):
    comps = padded.shape[0]
    half = comps // 2
    count = padded.shape[1] - 2 * reach
    offsets = list(range(-reach, 0)) + list(range(1, reach + 1))
    re_sum = jnp.zeros((half, count, padded.shape[2]), jnp.float32)
    im_sum = jnp.zeros((half, count, padded.shape[2]), jnp.float32)
    for position, offset in enumerate(offsets):
        source = padded[:, reach + offset : reach + offset + count]
        re = source[:half]
        im = source[half:]
        cr = coef_real[position][None, None, :]
        ci = coef_imag[position][None, None, :]
        weight = mask[position].astype(jnp.float32)[None, :, None]
        re_sum = re_sum + weight * (cr * re - ci * im)
        im_sum = im_sum + weight * (cr * im + ci * re)
    return jnp.concatenate([re_sum, im_sum], axis=0)


def translate_kernel(low_ref, keep_ref, recv_ref, high_ref, cr_ref, ci_ref, mask_ref, out_ref, pad_ref):
    comps, slots, width = keep_ref.shape
    reach = low_ref.shape[1]
    half = comps // 2
    pad_ref[:, :reach] = low_ref[...]
    pad_ref[:, reach : reach + slots] = keep_ref[...] + recv_ref[...]
    pad_ref[:, reach + slots :] = high_ref[...]
    offsets = list(range(-reach, 0)) + list(range(1, reach + 1))

    def lane_block(lb, carry):
        lanes = pl.ds(pl.multiple_of(lb * 128, 128), 128)
        for h in range(half):
            acc_re = jnp.zeros((slots, 128), jnp.float32)
            acc_im = jnp.zeros((slots, 128), jnp.float32)
            for k, t in enumerate(offsets):
                m = mask_ref[k]
                a = m * cr_ref[pl.ds(k, 1), lanes]
                b = m * ci_ref[pl.ds(k, 1), lanes]
                xr = pad_ref[h, pl.ds(reach + t, slots), lanes]
                xi = pad_ref[h + half, pl.ds(reach + t, slots), lanes]
                acc_re = acc_re + (a * xr - b * xi)
                acc_im = acc_im + (a * xi + b * xr)
            out_ref[h, :, lanes] = acc_re
            out_ref[h + half, :, lanes] = acc_im
        return carry

    lax.fori_loop(0, width // 128, lane_block, 0)


def translate_call(low, keep, recv, high, cr, ci, mask_b):
    comps, slots, width = keep.shape
    reach = low.shape[1]
    return pl.pallas_call(
        translate_kernel,
        out_shape=jax.ShapeDtypeStruct(keep.shape, jnp.float32),
        scratch_shapes=[pltpu.VMEM((comps, slots + 2 * reach, width), jnp.float32)],
    )(low, keep, recv, high, cr, ci, mask_b)


def body(
    pattern,
    child_coef,
    child_mask,
    interp_index,
    interp_weight,
    phase_angle,
    parent_coef,
    parent_mask,
):
    child_dev, comps, box_dev = pattern.shape
    dir_size = lax.axis_size("dir")
    parent_dirs = interp_index.shape[1]
    parent_dev = parent_dirs // dir_size
    groups = phase_angle.shape[0]
    slots = box_dev // groups
    dir_rank = lax.axis_index("dir")
    box_rank = lax.axis_index("box")
    child_first = dir_rank * child_dev
    parent_first = dir_rank * parent_dev
    cosine = jnp.cos(phase_angle)
    sine = jnp.sin(phase_angle)
    rows = interp_matrix(interp_index, interp_weight, child_first, child_dev)

    child_reach = child_coef.shape[1] // 2
    child_padded = with_halo(pattern, (("box", 2),), child_reach)
    child_local = translate_padded(
        child_padded, child_coef[0], child_coef[1], child_mask, child_reach
    )

    parent_reach = parent_coef.shape[1] // 2
    own_real = lax.dynamic_slice_in_dim(parent_coef[0], parent_first, parent_dev, 1)
    own_imag = lax.dynamic_slice_in_dim(parent_coef[1], parent_first, parent_dev, 1)
    own_mask = lax.dynamic_slice_in_dim(parent_mask, box_rank * slots, slots, 1)
    rhs = comps // 2
    step = rhs // 2

    def chunk_xt(chunk):
        part = pattern.reshape(child_dev, 2, rhs, box_dev)[:, :, chunk * step : (chunk + 1) * step]
        xt = part.reshape(child_dev, 2 * step, slots, groups).transpose(3, 1, 2, 0)
        return xt.reshape(groups, 2 * step * slots, child_dev)

    box_size = lax.axis_size("box")
    forward = [(i, (i + 1) % box_size) for i in range(box_size)]
    backward = [((i + 1) % box_size, i) for i in range(box_size)]
    mask_lanes = jnp.broadcast_to(
        own_mask.astype(jnp.float32)[:, :, None], own_mask.shape + (128,)
    )

    def translate(keep, recv):
        low = keep[:, slots - parent_reach :] + recv[:, slots - parent_reach :]
        high = keep[:, :parent_reach] + recv[:, :parent_reach]
        low = lax.ppermute(low, "box", forward)
        high = lax.ppermute(high, "box", backward)
        low = jnp.where(box_rank == 0, jnp.zeros_like(low), low)
        high = jnp.where(box_rank == box_size - 1, jnp.zeros_like(high), high)
        return translate_call(low, keep, recv, high, own_real, own_imag, mask_lanes)

    acc_a = reduce_cores(upward(chunk_xt(0), rows, cosine, sine, dir_size, 2 * step))
    acc_a, xt_b = lax.optimization_barrier((acc_a, chunk_xt(1)))
    keep_a, send_a = acc_a[0], acc_a[1]
    recv_a = lax.ppermute(send_a, "dir", ROW_SWAP)
    field_b = upward(xt_b, rows, cosine, sine, dir_size, 2 * step)
    field_b, recv_a = lax.optimization_barrier((field_b, recv_a))
    acc_b = reduce_cores(field_b)
    keep_a, recv_a, acc_b = lax.optimization_barrier((keep_a, recv_a, acc_b))
    keep_b, send_b = acc_b[0], acc_b[1]
    recv_b = lax.ppermute(send_b, "dir", ROW_SWAP)
    local_a = translate(keep_a, recv_a)
    local_a, recv_b = lax.optimization_barrier((local_a, recv_b))
    other_a = lax.ppermute(local_a, "dir", ROW_SWAP)
    local_b = translate(keep_b, recv_b)
    other_a, local_b = lax.optimization_barrier((other_a, local_b))
    all_a = gather_blocks(local_a, other_a)
    all_a, local_b = lax.optimization_barrier((all_a, local_b))
    other_b = lax.ppermute(local_b, "dir", ROW_SWAP)
    far_a = downward(all_a, rows, cosine, sine)
    far_a, other_b = lax.optimization_barrier((far_a, other_b))
    far_b = downward(gather_blocks(local_b, other_b), rows, cosine, sine)
    fars = [far.reshape(groups, child_dev, 2, step, slots) for far in (far_a, far_b)]
    far = jnp.concatenate(fars, axis=3).transpose(1, 2, 3, 4, 0)
    far = far.reshape(child_dev, comps, box_dev)
    return child_local + far


def solution(mesh):
    placed = (P("dir", None, "box"), P(None, None, "dir"), P(None, "box"), P(), P(), P(), P(), P())
    return jax.shard_map(
        body, mesh=mesh, in_specs=placed, out_specs=P("dir", None, "box"), check_vma=False
    )
```

```python
import jax
import jax.numpy as jnp
from jax import lax
from jax.experimental import pallas as pl
from jax.experimental.pallas import tpu as pltpu
from jax.sharding import PartitionSpec as P

HIGHEST = lax.Precision.HIGH


def with_halo(block, sides, width):
    for axis, dim in sides:
        count = lax.axis_size(axis)
        rank = lax.axis_index(axis)
        forward = [(i, (i + 1) % count) for i in range(count)]
        backward = [((i + 1) % count, i) for i in range(count)]
        low = lax.ppermute(
            lax.slice_in_dim(block, block.shape[dim] - width, None, axis=dim), axis, forward
        )
        high = lax.ppermute(lax.slice_in_dim(block, 0, width, axis=dim), axis, backward)
        low = jnp.where(rank == 0, jnp.zeros_like(low), low)
        high = jnp.where(rank == count - 1, jnp.zeros_like(high), high)
        block = jnp.concatenate([low, block, high], axis=dim)
    return block


CORE_SWAP = [(0, 1), (1, 0), (2, 3), (3, 2)]
ROW_SWAP = [(0, 2), (2, 0), (1, 3), (3, 1)]


def reduce_cores(field):
    keep, send = field
    return keep + lax.ppermute(send, "dir", CORE_SWAP)


def gather_blocks(local, other):
    mate_local, mate_other = lax.ppermute((local, other), "dir", CORE_SWAP)
    return (local, other, mate_local, mate_other)


def pack(pieces):
    return jnp.concatenate([piece.reshape(-1) for piece in pieces])


def unpack(flat, like):
    out, first = [], 0
    for piece in like:
        out.append(flat[first : first + piece.size].reshape(piece.shape))
        first += piece.size
    return out


def interp_matrix(index, weight, first_row, row_count):
    rows = first_row + lax.iota(jnp.int32, row_count)
    matrix = jnp.zeros((row_count, index.shape[1]), jnp.float32)
    for point in range(index.shape[0]):
        matrix = matrix + jnp.where(
            rows[:, None] == index[point][None, :], weight[point][None, :], jnp.float32(0.0)
        )
    return matrix


def translate_padded(padded, coef_real, coef_imag, mask, reach):
    count = padded.shape[2] - 2 * reach
    half = padded.shape[1] // 2
    offsets = list(range(-reach, 0)) + list(range(1, reach + 1))
    summed = jnp.zeros((padded.shape[0], padded.shape[1], count), jnp.float32)
    for position, offset in enumerate(offsets):
        source = padded[:, :, reach + offset : reach + offset + count]
        real_part = source[:, :half]
        imag_part = source[:, half:]
        scale_real = coef_real[position][:, None, None]
        scale_imag = coef_imag[position][:, None, None]
        weight = mask[position].astype(jnp.float32)[None, None, :]
        turned = jnp.concatenate(
            [
                scale_real * real_part - scale_imag * imag_part,
                scale_real * imag_part + scale_imag * real_part,
            ],
            axis=1,
        )
        summed = summed + weight * turned
    return summed


def slot_part(slot):
    rank = lax.axis_index("dir")
    return ((rank // 2 + slot % 2) % 2) * 2 + (rank % 2 + slot // 2) % 2


def upward_kernel(xt_ref, m_ref, cos_ref, sin_ref, keep_ref, send_ref):
    groups = xt_ref.shape[0]
    comps, slots, width = keep_ref.shape[1:]
    half = comps // 2
    for slot, out_ref in ((pl.program_id(0), keep_ref), (pl.program_id(0) + 2, send_ref)):
        first = pl.multiple_of(slot_part(slot) * width, 128)
        m = m_ref[:, pl.ds(first, width)]
        acc_re = jnp.zeros((half, slots, width), jnp.float32)
        acc_im = jnp.zeros((half, slots, width), jnp.float32)
        for g in range(groups):
            r = jnp.dot(xt_ref[g], m, precision=HIGHEST, preferred_element_type=jnp.float32)
            r = r.reshape(comps, slots, width)
            c = cos_ref[pl.ds(g, 1), pl.ds(first, width)].reshape(1, 1, width)
            s = sin_ref[pl.ds(g, 1), pl.ds(first, width)].reshape(1, 1, width)
            re = r[:half]
            im = r[half:]
            acc_re = acc_re + (c * re - s * im)
            acc_im = acc_im + (c * im + s * re)
        out_ref[0, :half] = acc_re
        out_ref[0, half:] = acc_im


def upward(xt, m, cos, sin, parts, comps):
    groups, rows, q = xt.shape
    total = m.shape[1]
    width = total // parts
    slots = rows // comps
    out = jax.ShapeDtypeStruct((parts // 2, comps, slots, width), jnp.float32)
    block = pl.BlockSpec((1, comps, slots, width), lambda j: (j, 0, 0, 0))
    return pl.pallas_call(
        upward_kernel,
        grid=(parts // 2,),
        in_specs=[
            pl.BlockSpec((groups, rows, q), lambda j: (0, 0, 0)),
            pl.BlockSpec((q, total), lambda j: (0, 0)),
            pl.BlockSpec((groups, total), lambda j: (0, 0)),
            pl.BlockSpec((groups, total), lambda j: (0, 0)),
        ],
        out_specs=[block, block],
        out_shape=[out, out],
    )(xt, m, cos, sin)


def downward_kernel(b0_ref, b1_ref, b2_ref, b3_ref, m_ref, cos_ref, sin_ref, out_ref):
    g = pl.program_id(0)
    comps, slots, width = b0_ref.shape
    half = comps // 2
    q = m_ref.shape[0]
    acc = jnp.zeros((q, comps * slots), jnp.float32)
    rank = lax.axis_index("dir")
    for code, ref in zip((0, 2, 1, 3), (b0_ref, b1_ref, b2_ref, b3_ref)):
        part = ((rank // 2 + code // 2) % 2) * 2 + (rank % 2 + code % 2) % 2
        first = pl.multiple_of(part * width, 128)
        x = ref[...]
        c = cos_ref[pl.ds(g, 1), pl.ds(first, width)].reshape(1, 1, width)
        s = sin_ref[pl.ds(g, 1), pl.ds(first, width)].reshape(1, 1, width)
        re = x[:half]
        im = x[half:]
        spread = jnp.concatenate([c * re + s * im, c * im - s * re], axis=0)
        spread = spread.reshape(comps * slots, width)
        acc = acc + lax.dot_general(
            m_ref[:, pl.ds(first, width)],
            spread,
            (((1,), (1,)), ((), ())),
            precision=HIGHEST,
            preferred_element_type=jnp.float32,
        )
    out_ref[0] = acc


def downward(blocks, m, cos, sin):
    comps, slots, width = blocks[0].shape
    groups = cos.shape[0]
    q, total = m.shape
    block = pl.BlockSpec((comps, slots, width), lambda g: (0, 0, 0))
    return pl.pallas_call(
        downward_kernel,
        grid=(groups,),
        in_specs=[block] * 4
        + [
            pl.BlockSpec((q, total), lambda g: (0, 0)),
            pl.BlockSpec((groups, total), lambda g: (0, 0)),
            pl.BlockSpec((groups, total), lambda g: (0, 0)),
        ],
        out_specs=pl.BlockSpec((1, q, comps * slots), lambda g: (g, 0, 0)),
        out_shape=jax.ShapeDtypeStruct((groups, q, comps * slots), jnp.float32),
    )(*blocks, m, cos, sin)


def parent_translate(padded, coef_real, coef_imag, mask, reach):
    comps = padded.shape[0]
    half = comps // 2
    count = padded.shape[1] - 2 * reach
    offsets = list(range(-reach, 0)) + list(range(1, reach + 1))
    re_sum = jnp.zeros((half, count, padded.shape[2]), jnp.float32)
    im_sum = jnp.zeros((half, count, padded.shape[2]), jnp.float32)
    for position, offset in enumerate(offsets):
        source = padded[:, reach + offset : reach + offset + count]
        re = source[:half]
        im = source[half:]
        cr = coef_real[position][None, None, :]
        ci = coef_imag[position][None, None, :]
        weight = mask[position].astype(jnp.float32)[None, :, None]
        re_sum = re_sum + weight * (cr * re - ci * im)
        im_sum = im_sum + weight * (cr * im + ci * re)
    return jnp.concatenate([re_sum, im_sum], axis=0)


def translate_kernel(low_ref, keep_ref, recv_ref, high_ref, cr_ref, ci_ref, mask_ref, out_ref, pad_ref):
    comps, slots, width = keep_ref.shape
    reach = low_ref.shape[1]
    half = comps // 2
    pad_ref[:, :reach] = low_ref[...]
    pad_ref[:, reach : reach + slots] = keep_ref[...] + recv_ref[...]
    pad_ref[:, reach + slots :] = high_ref[...]
    offsets = list(range(-reach, 0)) + list(range(1, reach + 1))

    def lane_block(lb, carry):
        lanes = pl.ds(pl.multiple_of(lb * 128, 128), 128)
        for h in range(half):
            acc_re = jnp.zeros((slots, 128), jnp.float32)
            acc_im = jnp.zeros((slots, 128), jnp.float32)
            for k, t in enumerate(offsets):
                m = mask_ref[k]
                a = m * cr_ref[pl.ds(k, 1), lanes]
                b = m * ci_ref[pl.ds(k, 1), lanes]
                xr = pad_ref[h, pl.ds(reach + t, slots), lanes]
                xi = pad_ref[h + half, pl.ds(reach + t, slots), lanes]
                acc_re = acc_re + (a * xr - b * xi)
                acc_im = acc_im + (a * xi + b * xr)
            out_ref[h, :, lanes] = acc_re
            out_ref[h + half, :, lanes] = acc_im
        return carry

    lax.fori_loop(0, width // 128, lane_block, 0)


def translate_call(low, keep, recv, high, cr, ci, mask_b):
    comps, slots, width = keep.shape
    reach = low.shape[1]
    return pl.pallas_call(
        translate_kernel,
        out_shape=jax.ShapeDtypeStruct(keep.shape, jnp.float32),
        scratch_shapes=[pltpu.VMEM((comps, slots + 2 * reach, width), jnp.float32)],
    )(low, keep, recv, high, cr, ci, mask_b)


def body(
    pattern,
    child_coef,
    child_mask,
    interp_index,
    interp_weight,
    phase_angle,
    parent_coef,
    parent_mask,
):
    child_dev, comps, box_dev = pattern.shape
    dir_size = lax.axis_size("dir")
    parent_dirs = interp_index.shape[1]
    parent_dev = parent_dirs // dir_size
    groups = phase_angle.shape[0]
    slots = box_dev // groups
    dir_rank = lax.axis_index("dir")
    box_rank = lax.axis_index("box")
    child_first = dir_rank * child_dev
    parent_first = dir_rank * parent_dev
    cosine = jnp.cos(phase_angle)
    sine = jnp.sin(phase_angle)
    rows = interp_matrix(interp_index, interp_weight, child_first, child_dev)

    child_reach = child_coef.shape[1] // 2

    parent_reach = parent_coef.shape[1] // 2
    own_real = lax.dynamic_slice_in_dim(parent_coef[0], parent_first, parent_dev, 1)
    own_imag = lax.dynamic_slice_in_dim(parent_coef[1], parent_first, parent_dev, 1)
    own_mask = lax.dynamic_slice_in_dim(parent_mask, box_rank * slots, slots, 1)
    rhs = comps // 2
    step = rhs // 2

    def chunk_xt(chunk):
        part = pattern.reshape(child_dev, 2, rhs, box_dev)[:, :, chunk * step : (chunk + 1) * step]
        xt = part.reshape(child_dev, 2 * step, slots, groups).transpose(3, 1, 2, 0)
        return xt.reshape(groups, 2 * step * slots, child_dev)

    box_size = lax.axis_size("box")
    forward = [(i, (i + 1) % box_size) for i in range(box_size)]
    backward = [((i + 1) % box_size, i) for i in range(box_size)]
    mask_lanes = jnp.broadcast_to(
        own_mask.astype(jnp.float32)[:, :, None], own_mask.shape + (128,)
    )

    def translate(keep, recv, extra=None):
        low = keep[:, slots - parent_reach :] + recv[:, slots - parent_reach :]
        high = keep[:, :parent_reach] + recv[:, :parent_reach]
        if extra is None:
            low = lax.ppermute(low, "box", forward)
            high = lax.ppermute(high, "box", backward)
        else:
            ups = (low, extra[0])
            downs = (high, extra[1])
            low, extra_low = unpack(lax.ppermute(pack(ups), "box", forward), ups)
            high, extra_high = unpack(lax.ppermute(pack(downs), "box", backward), downs)
        low = jnp.where(box_rank == 0, jnp.zeros_like(low), low)
        high = jnp.where(box_rank == box_size - 1, jnp.zeros_like(high), high)
        local = translate_call(low, keep, recv, high, own_real, own_imag, mask_lanes)
        if extra is None:
            return local
        extra_low = jnp.where(box_rank == 0, jnp.zeros_like(extra_low), extra_low)
        extra_high = jnp.where(box_rank == box_size - 1, jnp.zeros_like(extra_high), extra_high)
        return local, extra_low, extra_high

    acc_a = reduce_cores(upward(chunk_xt(0), rows, cosine, sine, dir_size, 2 * step))
    acc_a, xt_b = lax.optimization_barrier((acc_a, chunk_xt(1)))
    keep_a, send_a = acc_a[0], acc_a[1]
    recv_a = lax.ppermute(send_a, "dir", ROW_SWAP)
    field_b = upward(xt_b, rows, cosine, sine, dir_size, 2 * step)
    field_b, recv_a = lax.optimization_barrier((field_b, recv_a))
    acc_b = reduce_cores(field_b)
    keep_a, recv_a, acc_b = lax.optimization_barrier((keep_a, recv_a, acc_b))
    keep_b, send_b = acc_b[0], acc_b[1]
    recv_b = lax.ppermute(send_b, "dir", ROW_SWAP)
    local_a = translate(keep_a, recv_a)
    local_a, recv_b = lax.optimization_barrier((local_a, recv_b))
    other_a = lax.ppermute(local_a, "dir", ROW_SWAP)
    edges = (pattern[:, :, box_dev - child_reach :], pattern[:, :, :child_reach])
    local_b, child_low, child_high = translate(keep_b, recv_b, edges)
    child_padded = jnp.concatenate([child_low, pattern, child_high], axis=2)
    child_local = translate_padded(
        child_padded, child_coef[0], child_coef[1], child_mask, child_reach
    )
    other_a, local_b = lax.optimization_barrier((other_a, local_b))
    all_a = gather_blocks(local_a, other_a)
    all_a, local_b = lax.optimization_barrier((all_a, local_b))
    other_b = lax.ppermute(local_b, "dir", ROW_SWAP)
    far_a = downward(all_a, rows, cosine, sine)
    far_a, other_b = lax.optimization_barrier((far_a, other_b))
    far_b = downward(gather_blocks(local_b, other_b), rows, cosine, sine)
    fars = [far.reshape(groups, child_dev, 2, step, slots) for far in (far_a, far_b)]
    far = jnp.concatenate(fars, axis=3).transpose(1, 2, 3, 4, 0)
    far = far.reshape(child_dev, comps, box_dev)
    return child_local + far


def solution(mesh):
    placed = (P("dir", None, "box"), P(None, None, "dir"), P(None, "box"), P(), P(), P(), P(), P())
    return jax.shard_map(
        body, mesh=mesh, in_specs=placed, out_specs=P("dir", None, "box"), check_vma=False
    )
```
